32 devices in a mesh: groups: 2 (over y), section: 4 (over z), seq: 4 (over x, core).
Axes of the slice: x: 2, y: 2, z: 4, core: 2. Of those that a mesh axis runs over, the one named last changes fastest.
Arguments:
- incoming_states: bfloat16 [1536, 3072], P('groups', 'seq'), parts along dimension 0, may hold values from -6 to 6
- transit_states: bfloat16 [4, 512, 3072], P('section', 'groups', 'seq'), parts along dimension 1, may hold values from -6 to 6
- patch_sizes_list: int32 [8], P('groups'), parts along dimension 0, may hold values from 1 to 256, 768 in all
- outdated_lookups: bfloat16 [4, 16, 1536, 128], P('section', 'seq', 'groups'), parts along dimension 2, may hold values from -6 to 6
- outdated_contents: bfloat16 [4, 16, 1536, 128], P('section', 'seq', 'groups'), parts along dimension 2, may hold values from -6 to 6
- attention_projection: bfloat16 [4, 3072, 6144], P('section', None, 'seq'), may hold values from -0.109375 to 0.109375
- exit_projection: bfloat16 [4, 2048, 3072], P('section', None, 'seq'), may hold values from -0.125 to 0.125
- shift_and_scale: float32 [4, 2, 3072], P('section'), may hold values from -3 to 3
- branch_gates: float32 [4, 3072], P('section', 'seq'), may hold values from -4 to 4
Outputs:
- section_out: bfloat16 [4, 4, 512, 3072], P(None, 'section', 'groups', 'seq'), parts along dimension 2
The draws below stay inside these ranges and needn't reach their ends.
There are 2 independent parts, one for each index of `groups`. The reference program is written for one: setup_inputs(seed, part) draws one part's arguments, and reference() takes and returns one part's arrays. A program takes and returns all parts, laid end to end along the dimension named above; an argument that names none is the same for every part. Nothing has to cross between parts.
Inputs may be any that keep to these rules, and one draw needn't show every extreme that they name: `patch_sizes_list`: the 4 counts sum to 768; the largest equals 256.
All inputs are finite; a program needn't handle non-finite values.
Results may differ from the reference program's by a relative error of at most 0.005.
Values may be sent and summed in bfloat16 or wider, within the bound.
No kernel may reach another device: no remote copies, remote signals or barrier semaphores. Data moves between devices by JAX's collectives and lax.ppermute only.
A program may use at most 128 MiB of HBM per device.

```python
import math
import jax
import jax.numpy as jnp
import numpy as np
from jax import lax

HIDDEN_EXTENT = 3072
HEADS = 16
HEAD_DIM = 128
PATCHES = 4
LEN = 768
BIGGEST_PATCHSET = 256
LAYER_TOTAL = 4


def shard_levels(stream_key, shape, pieces, smallest, largest):
    factor_of = 1.0
    for axis_at, shards_of in pieces:
        draws = jax.random.uniform(jax.random.fold_in(jax.random.fold_in(stream_key, 6), axis_at), (shards_of,), jnp.float32, smallest / len(pieces), largest / len(pieces))
        factor_of = factor_of * jnp.repeat(jnp.exp(draws), shape[axis_at] // shards_of).reshape((-1,) + (1,) * (len(shape) - 1 - axis_at))
    return factor_of


def profile(amount, total, bound, lean):
    weights = [(1 << 20) // math.isqrt(rank ** lean) + 1 for rank in range(2, amount + 1)]
    spare, counts = total - bound - (amount - 1), [1] * (amount - 1)
    while spare > 0:
        movable = [i for i in range(amount - 1) if counts[i] < bound]
        pool, budget = sum([weights[i] for i in movable]), spare
        for i in movable:
            extra = min(bound - counts[i], max(1, budget * weights[i] // pool), spare)
            counts[i] = counts[i] + extra
            spare = spare - extra
    return np.array([bound] + counts)


def uneven(stream_key, number_of, total, reach, slope):
    if number_of == 2:
        one = jax.random.randint(stream_key, (), max(1, total - reach), min(reach, total - 1) + 1)
        return jnp.stack([one, total - one])
    sizes = jnp.asarray(profile(number_of, total, reach, slope), jnp.int32)
    pairs = (number_of - 1) // 2
    giver, receiver = sizes[1:1 + 2 * pairs:2], sizes[2:2 + 2 * pairs:2]
    slack = jnp.minimum(giver - 1, reach - receiver)
    moved = jax.random.randint(jax.random.fold_in(stream_key, 1), (pairs,), 0, 1 << 20) % (slack + 1)
    sizes = sizes.at[1:1 + 2 * pairs:2].set(giver - moved).at[2:2 + 2 * pairs:2].set(receiver + moved)
    return sizes[jax.random.permutation(jax.random.fold_in(stream_key, 2), number_of)]


def bell_draw(stream_key, dims, width, bound, pieces=(), held_as=jnp.bfloat16):
    entries = width * jax.random.normal(stream_key, dims, jnp.float32)
    if pieces:
        entries = entries * shard_levels(stream_key, dims, pieces, -0.22, 0.18)
    return jnp.clip(entries, -bound, bound).astype(held_as)


def setup_inputs(seed: int = 0, part: int = 0) -> dict:
    streams_of = jax.random.split(jax.random.key(seed), 10)
    own_keys = jax.random.split(jax.random.fold_in(streams_of[9], part), 10)
    return {
        "incoming_states": bell_draw(own_keys[0], (LEN, HIDDEN_EXTENT), 1.0, 6.0, ((1, 4),)),
        "transit_states": bell_draw(own_keys[1], (LAYER_TOTAL, BIGGEST_PATCHSET, HIDDEN_EXTENT), 1.0, 6.0, ((0, 4), (2, 4))),
        "patch_sizes_list": uneven(own_keys[2], PATCHES, LEN, BIGGEST_PATCHSET, 2).astype(jnp.int32),
        "outdated_lookups": bell_draw(own_keys[3], (LAYER_TOTAL, HEADS, LEN, HEAD_DIM), 1.0, 6.0, ((0, 4), (1, 4))),
        "outdated_contents": bell_draw(own_keys[4], (LAYER_TOTAL, HEADS, LEN, HEAD_DIM), 1.0, 6.0, ((0, 4), (1, 4))),
        "attention_projection": bell_draw(streams_of[5], (LAYER_TOTAL, HIDDEN_EXTENT, 3 * HEADS * HEAD_DIM), HIDDEN_EXTENT ** -0.5, 0.109375, ((0, 4), (2, 4))),
        "exit_projection": bell_draw(streams_of[6], (LAYER_TOTAL, HEADS * HEAD_DIM, HIDDEN_EXTENT), (HEADS * HEAD_DIM) ** -0.5, 0.125, ((0, 4), (2, 4))),
        "shift_and_scale": bell_draw(streams_of[7], (LAYER_TOTAL, 2, HIDDEN_EXTENT), 0.5, 3.0, ((0, 4),), jnp.float32),
        "branch_gates": bell_draw(streams_of[8], (LAYER_TOTAL, HIDDEN_EXTENT), 1.0, 4.0, ((0, 4), (1, 4)), jnp.float32),
    }


epsilon = 1e-06

def layer_norm(values):
    row_mean = lax.optimization_barrier(jnp.mean(values, axis=-1, keepdims=True))
    centred = values - row_mean
    spread = lax.optimization_barrier(jnp.mean(centred * centred, axis=-1, keepdims=True))
    return centred * lax.rsqrt(spread + epsilon)

def rms_norm(values):
    return values * lax.rsqrt(lax.optimization_barrier(jnp.mean(values * values, axis=-1, keepdims=True)) + epsilon)

def run_block(image_piece_lines, patch_count, patch_start, key_cache, value_cache, w_qkv_here, w_out_here, shift_scale, gating_here):
    live_rows = jnp.arange(BIGGEST_PATCHSET) < patch_count
    image_piece_lines = jnp.where(live_rows[:, None], image_piece_lines, jnp.zeros_like(image_piece_lines))
    inputs = image_piece_lines.astype(jnp.float32)
    shaped = (layer_norm(inputs) * (1.0 + shift_scale[1]) + shift_scale[0]).astype(jnp.bfloat16)
    mixed = jnp.dot(shaped, w_qkv_here, preferred_element_type=jnp.float32).reshape(BIGGEST_PATCHSET, HEADS, 3, HEAD_DIM)
    queries = rms_norm(mixed[:, :, 0]).astype(jnp.bfloat16)
    fresh_keys = jnp.transpose(rms_norm(mixed[:, :, 1]).astype(jnp.bfloat16), (1, 0, 2))
    fresh_values = jnp.transpose(mixed[:, :, 2].astype(jnp.bfloat16), (1, 0, 2))
    padding = jnp.zeros((HEADS, BIGGEST_PATCHSET, HEAD_DIM), jnp.bfloat16)
    start = patch_start.astype(jnp.int32)
    mask = live_rows[None, :, None]
    padded_keys = jnp.concatenate([key_cache, padding], axis=1)
    window = lax.dynamic_slice_in_dim(padded_keys, start, BIGGEST_PATCHSET, 1)
    padded_keys = lax.dynamic_update_slice_in_dim(padded_keys, jnp.where(mask, fresh_keys, window), start, 1)
    padded_values = jnp.concatenate([value_cache, padding], axis=1)
    window = lax.dynamic_slice_in_dim(padded_values, start, BIGGEST_PATCHSET, 1)
    padded_values = lax.dynamic_update_slice_in_dim(padded_values, jnp.where(mask, fresh_values, window), start, 1)
    key_cache = padded_keys[:, :LEN]
    value_cache = padded_values[:, :LEN]
    scores = jnp.einsum('qhd,hkd->hqk', queries.astype(jnp.float32), key_cache.astype(jnp.float32)) * HEAD_DIM ** (-0.5)
    expos = jnp.exp(scores)
    weights = (expos / lax.optimization_barrier(jnp.sum(expos, axis=-1, keepdims=True))).astype(jnp.bfloat16)
    attended = jnp.einsum('hqk,hkd->qhd', weights.astype(jnp.float32), value_cache.astype(jnp.float32)).astype(jnp.bfloat16)
    head_rows = attended.reshape(BIGGEST_PATCHSET, HEADS * HEAD_DIM)
    projected = jnp.dot(head_rows, w_out_here, preferred_element_type=jnp.float32)
    updated = inputs + gating_here * projected
    updated = jnp.where(live_rows[:, None], updated, jnp.zeros_like(updated)).astype(jnp.bfloat16)
    return (updated, key_cache, value_cache)

def reference(incoming_states, transit_states, patch_sizes_list, outdated_lookups, outdated_contents, attention_projection, exit_projection, shift_and_scale, branch_gates):
    starts = (jnp.cumsum(patch_sizes_list) - patch_sizes_list).astype(jnp.int32)
    entering_ext = jnp.concatenate([incoming_states, jnp.zeros((BIGGEST_PATCHSET, HIDDEN_EXTENT), jnp.bfloat16)], axis=0)
    key_caches = [outdated_lookups[active_layer] for active_layer in range(LAYER_TOTAL)]
    value_caches = [outdated_contents[active_layer] for active_layer in range(LAYER_TOTAL)]
    results = []
    for turn_number in range(PATCHES):
        turn_rows = []
        for active_layer in range(LAYER_TOTAL):
            patch_index = (turn_number - active_layer) % PATCHES
            if active_layer == 0:
                image_piece_lines = lax.dynamic_slice_in_dim(entering_ext, starts[turn_number].astype(jnp.int32), BIGGEST_PATCHSET, 0)
            elif turn_number == 0:
                image_piece_lines = transit_states[active_layer]
            else:
                image_piece_lines = results[turn_number - 1][active_layer - 1]
            updated, key_caches[active_layer], value_caches[active_layer] = run_block(image_piece_lines, patch_sizes_list[patch_index], starts[patch_index], key_caches[active_layer], value_caches[active_layer], attention_projection[active_layer], exit_projection[active_layer], shift_and_scale[active_layer], branch_gates[active_layer])
            turn_rows.append(updated)
        results.append(turn_rows)
    return jnp.stack([jnp.stack(turn_rows) for turn_rows in results])
```

```python
import jax
import jax.numpy as jnp
from jax import lax
from jax.sharding import PartitionSpec as P

epsilon = 1e-06


def passed_along(value, axis, steps):
    count = lax.axis_size(axis)
    leading, last = (max(0, -steps), min(count, count - steps))
    return lax.ppermute(value, axis, [(source, source + steps) for source in range(leading, last)])


def layer_norm(values):
    row_mean = jnp.mean(values, axis=-1, keepdims=True)
    centred = values - row_mean
    spread = jnp.mean(centred * centred, axis=-1, keepdims=True)
    return centred * lax.rsqrt(spread + epsilon)


def rms_norm(values):
    return values * lax.rsqrt(jnp.mean(values * values, axis=-1, keepdims=True) + epsilon)


def gather_features(rows):
    across_chips = lax.all_gather(rows, "seq_chip", axis=0)
    both_cores = lax.all_gather(across_chips, "seq_core", axis=1)
    count, width = rows.shape
    return jnp.transpose(both_cores, (2, 0, 1, 3)).reshape(count, -1)


def pick_entry(vector, position):
    return jnp.sum(jnp.where(jnp.arange(vector.shape[0]) == position, vector, 0))


def run_block(
    full_rows,
    own_rows,
    live_rows,
    patch_start,
    key_cache,
    value_cache,
    qkv_weights,
    shift_scale,
    gating_here,
    project,
):
    biggest_patch_span = full_rows.shape[0]
    heads_here = key_cache.shape[0]
    head_dim = key_cache.shape[2]
    seq_len = key_cache.shape[1] - biggest_patch_span
    shaped = (
        layer_norm(full_rows.astype(jnp.float32)) * (1.0 + shift_scale[1]) + shift_scale[0]
    ).astype(jnp.bfloat16)
    mixed = jnp.dot(shaped, qkv_weights, preferred_element_type=jnp.float32).reshape(
        biggest_patch_span, heads_here, 3, head_dim
    )
    queries = rms_norm(mixed[:, :, 0]).astype(jnp.bfloat16)
    fresh_keys = jnp.transpose(rms_norm(mixed[:, :, 1]).astype(jnp.bfloat16), (1, 0, 2))
    fresh_values = jnp.transpose(mixed[:, :, 2].astype(jnp.bfloat16), (1, 0, 2))
    mask = live_rows[None, :, None]
    window = lax.dynamic_slice_in_dim(key_cache, patch_start, biggest_patch_span, 1)
    key_cache = lax.dynamic_update_slice_in_dim(
        key_cache, jnp.where(mask, fresh_keys, window), patch_start, 1
    )
    window = lax.dynamic_slice_in_dim(value_cache, patch_start, biggest_patch_span, 1)
    value_cache = lax.dynamic_update_slice_in_dim(
        value_cache, jnp.where(mask, fresh_values, window), patch_start, 1
    )
    scores = jnp.einsum(
        "qhd,hkd->hqk", queries, key_cache[:, :seq_len], preferred_element_type=jnp.float32
    ) * head_dim ** (-0.5)
    expos = jnp.exp(scores)
    weights = (expos / jnp.sum(expos, axis=-1, keepdims=True)).astype(jnp.bfloat16)
    attended = jnp.einsum(
        "hqk,hkd->qhd", weights, value_cache[:, :seq_len], preferred_element_type=jnp.float32
    ).astype(jnp.bfloat16)
    head_rows = attended.reshape(biggest_patch_span, heads_here * head_dim)
    projected = project(head_rows)
    updated = own_rows.astype(jnp.float32) + gating_here * projected
    updated = jnp.where(live_rows[:, None], updated, 0.0).astype(jnp.bfloat16)
    return (updated, key_cache, value_cache)


def shards(
    incoming_states,
    transit_states,
    patch_sizes_list,
    outdated_lookups,
    outdated_contents,
    attention_projection,
    exit_projection,
    shift_and_scale,
    branch_gates,
):
    section_index = lax.axis_index("section")
    patches = patch_sizes_list.shape[0]
    biggest_patch_span = transit_states.shape[1]
    columns = incoming_states.shape[1]
    heads_here = outdated_lookups.shape[1]
    head_dim = outdated_lookups.shape[3]
    starts = jnp.cumsum(patch_sizes_list) - patch_sizes_list
    padding = jnp.zeros((heads_here, biggest_patch_span, head_dim), jnp.bfloat16)
    key_cache = jnp.concatenate([outdated_lookups[0], padding], axis=1)
    value_cache = jnp.concatenate([outdated_contents[0], padding], axis=1)
    qkv_weights = attention_projection[0]
    out_weights = exit_projection[0]
    shift_scale = shift_and_scale[0]
    gating_here = branch_gates[0]
    row_numbers = jnp.arange(biggest_patch_span)

    def gather_heads(head_rows):
        every_head = gather_features(head_rows)
        return jnp.dot(every_head, out_weights, preferred_element_type=jnp.float32)

    results = []
    entering_ext = jnp.concatenate(
        [incoming_states, jnp.zeros((biggest_patch_span, columns), jnp.bfloat16)], axis=0
    )
    earlier_result = transit_states[0]
    for turn_number in range(patches):
        patch_index = jnp.remainder(turn_number - section_index, patches)
        patch_count = pick_entry(patch_sizes_list, patch_index)
        patch_start = pick_entry(starts, patch_index)
        live_rows = row_numbers < patch_count
        entry_patch = lax.dynamic_slice_in_dim(
            entering_ext, starts[turn_number], biggest_patch_span, 0
        )
        own_rows = jnp.where(section_index == 0, entry_patch, earlier_result)
        own_rows = jnp.where(live_rows[:, None], own_rows, jnp.zeros_like(own_rows))
        full_rows = gather_features(own_rows)
        updated, key_cache, value_cache = run_block(
            full_rows,
            own_rows,
            live_rows,
            patch_start,
            key_cache,
            value_cache,
            qkv_weights,
            shift_scale,
            gating_here,
            gather_heads,
        )
        results.append(updated)
        if turn_number + 1 < patches:
            earlier_result = passed_along(updated, "section", 1)
    return jnp.stack(results)[:, None]


def chip_mesh(mesh):
    devices = mesh.devices
    groups, section, seq = devices.shape
    return jax.sharding.Mesh(
        devices.reshape(groups, section, seq // 2, 2), ("groups", "section", "seq_chip", "seq_core")
    )


def solution(mesh):
    mesh = chip_mesh(mesh)
    seq = ("seq_chip", "seq_core")
    return jax.shard_map(
        shards,
        mesh=mesh,
        in_specs=(
            P("groups", seq),
            P("section", "groups", seq),
            P("groups"),
            P("section", seq, "groups", None),
            P("section", seq, "groups", None),
            P("section", None, seq),
            P("section", None, seq),
            P("section", None, None),
            P("section", seq),
        ),
        out_specs=P(None, "section", "groups", seq),
        check_vma=False,
    )
```

```python
import functools

import jax
import jax.numpy as jnp
from jax import lax
from jax.experimental import pallas as pl
from jax.experimental.pallas import tpu as pltpu
from jax.sharding import PartitionSpec as P

epsilon = 1e-06


def passed_along(value, axis, steps):
    count = lax.axis_size(axis)
    leading, last = (max(0, -steps), min(count, count - steps))
    return lax.ppermute(value, axis, [(source, source + steps) for source in range(leading, last)])


def layer_norm(values):
    row_mean = jnp.mean(values, axis=-1, keepdims=True)
    centred = values - row_mean
    spread = jnp.mean(centred * centred, axis=-1, keepdims=True)
    return centred * lax.rsqrt(spread + epsilon)


def rms_norm(values):
    return values * lax.rsqrt(jnp.mean(values * values, axis=-1, keepdims=True) + epsilon)


def pick_entry(vector, position):
    return jnp.sum(jnp.where(jnp.arange(vector.shape[0]) == position, vector, 0))


def attention_kernel(where_ref, mixed_ref, keys_ref, values_ref, heads_ref, keys_out, values_out):
    head_dim = keys_ref.shape[2]
    seq_len = keys_ref.shape[1]
    span = mixed_ref.shape[0]
    start = where_ref[0]
    count = where_ref[1]
    block = mixed_ref[...]
    queries = rms_norm(block[:, :head_dim]).astype(jnp.bfloat16)
    fresh_keys = rms_norm(block[:, head_dim : 2 * head_dim]).astype(jnp.bfloat16)
    fresh_values = block[:, 2 * head_dim :].astype(jnp.bfloat16)
    rows = lax.broadcasted_iota(jnp.int32, (seq_len, span), 0)
    picks = lax.broadcasted_iota(jnp.int32, (seq_len, span), 1)
    placing = ((rows == picks + start) & (picks < count)).astype(jnp.bfloat16)
    row_ids = lax.broadcasted_iota(jnp.int32, (seq_len, 1), 0)
    inside = (row_ids >= start) & (row_ids < start + count)
    placed_keys = jnp.dot(placing, fresh_keys, preferred_element_type=jnp.float32)
    placed_values = jnp.dot(placing, fresh_values, preferred_element_type=jnp.float32)
    keys = jnp.where(inside, placed_keys.astype(jnp.bfloat16), keys_ref[0])
    values = jnp.where(inside, placed_values.astype(jnp.bfloat16), values_ref[0])
    keys_out[0] = keys
    values_out[0] = values
    scores = lax.dot_general(
        queries, keys, (((1,), (1,)), ((), ())), preferred_element_type=jnp.float32
    ) * head_dim ** (-0.5)
    expos = jnp.exp(scores)
    weights = (expos / jnp.sum(expos, axis=-1, keepdims=True)).astype(jnp.bfloat16)
    heads_ref[...] = jnp.dot(weights, values, preferred_element_type=jnp.float32).astype(
        jnp.bfloat16
    )


def attend(mixed, key_cache, value_cache, patch_start, patch_count):
    heads_here, seq_len, head_dim = key_cache.shape
    span = mixed.shape[0]
    where = jnp.stack([patch_start, patch_count]).astype(jnp.int32)
    cache_spec = pl.BlockSpec((1, seq_len, head_dim), lambda h, where: (h, 0, 0))
    grid_spec = pltpu.PrefetchScalarGridSpec(
        num_scalar_prefetch=1,
        grid=(heads_here,),
        in_specs=[
            pl.BlockSpec((span, 3 * head_dim), lambda h, where: (0, h)),
            cache_spec,
            cache_spec,
        ],
        out_specs=[
            pl.BlockSpec((span, head_dim), lambda h, where: (0, h)),
            cache_spec,
            cache_spec,
        ],
    )
    return pl.pallas_call(
        attention_kernel,
        grid_spec=grid_spec,
        out_shape=[
            jax.ShapeDtypeStruct((span, heads_here * head_dim), jnp.bfloat16),
            jax.ShapeDtypeStruct(key_cache.shape, key_cache.dtype),
            jax.ShapeDtypeStruct(value_cache.shape, value_cache.dtype),
        ],
        input_output_aliases={2: 1, 3: 2},
    )(where, mixed, key_cache, value_cache)


def run_block(
    full_rows,
    own_rows,
    live_rows,
    patch_start,
    patch_count,
    key_cache,
    value_cache,
    qkv_weights,
    shift_scale,
    gating_here,
    project,
):
    shaped = (
        layer_norm(full_rows.astype(jnp.float32)) * (1.0 + shift_scale[1]) + shift_scale[0]
    ).astype(jnp.bfloat16)
    mixed = jnp.dot(shaped, qkv_weights, preferred_element_type=jnp.float32)
    head_rows, key_cache, value_cache = attend(
        mixed, key_cache, value_cache, patch_start, patch_count
    )
    projected = project(head_rows)
    updated = own_rows.astype(jnp.float32) + gating_here * projected
    updated = jnp.where(live_rows[:, None], updated, 0.0).astype(jnp.bfloat16)
    return (updated, key_cache, value_cache)


def shards(
    incoming_states,
    transit_states,
    patch_sizes_list,
    outdated_lookups,
    outdated_contents,
    attention_projection,
    exit_projection,
    shift_and_scale,
    branch_gates,
):
    section_index = lax.axis_index("section")
    patches = patch_sizes_list.shape[0]
    biggest_patch_span = transit_states.shape[1]
    columns = incoming_states.shape[1]
    heads_here = outdated_lookups.shape[1]
    head_dim = outdated_lookups.shape[3]
    starts = jnp.cumsum(patch_sizes_list) - patch_sizes_list
    key_cache = outdated_lookups[0]
    value_cache = outdated_contents[0]
    qkv_weights = attention_projection[0]
    out_weights = exit_projection[0]
    shift_scale = shift_and_scale[0]
    gating_here = branch_gates[0]
    row_numbers = jnp.arange(biggest_patch_span)

    def gather_heads(head_rows):
        every_head = lax.all_gather(head_rows, "seq", axis=1, tiled=True)
        return jnp.dot(every_head, out_weights, preferred_element_type=jnp.float32)

    results = []
    entering_ext = jnp.concatenate(
        [incoming_states, jnp.zeros((biggest_patch_span, columns), jnp.bfloat16)], axis=0
    )
    earlier_result = transit_states[0]
    for turn_number in range(patches):
        patch_index = jnp.remainder(turn_number - section_index, patches)
        patch_count = pick_entry(patch_sizes_list, patch_index)
        patch_start = pick_entry(starts, patch_index)
        live_rows = row_numbers < patch_count
        entry_patch = lax.dynamic_slice_in_dim(
            entering_ext, starts[turn_number], biggest_patch_span, 0
        )
        own_rows = jnp.where(section_index == 0, entry_patch, earlier_result)
        own_rows = jnp.where(live_rows[:, None], own_rows, jnp.zeros_like(own_rows))
        full_rows = lax.all_gather(own_rows, "seq", axis=1, tiled=True)
        updated, key_cache, value_cache = run_block(
            full_rows,
            own_rows,
            live_rows,
            patch_start,
            patch_count,
            key_cache,
            value_cache,
            qkv_weights,
            shift_scale,
            gating_here,
            gather_heads,
        )
        results.append(updated)
        if turn_number + 1 < patches:
            earlier_result = passed_along(updated, "section", 1)
    return jnp.stack(results)[:, None]


def solution(mesh):
    return jax.shard_map(
        shards,
        mesh=mesh,
        in_specs=(
            P("groups", "seq"),
            P("section", "groups", "seq"),
            P("groups"),
            P("section", "seq", "groups", None),
            P("section", "seq", "groups", None),
            P("section", None, "seq"),
            P("section", None, "seq"),
            P("section", None, None),
            P("section", "seq"),
        ),
        out_specs=P(None, "section", "groups", "seq"),
        check_vma=False,
    )
```

```python
import functools

import jax
import jax.numpy as jnp
from jax import lax
from jax.experimental import pallas as pl
from jax.experimental.pallas import tpu as pltpu
from jax.sharding import PartitionSpec as P

epsilon = 1e-06


def passed_along(value, axis, steps):
    count = lax.axis_size(axis)
    leading, last = (max(0, -steps), min(count, count - steps))
    return lax.ppermute(value, axis, [(source, source + steps) for source in range(leading, last)])


def layer_norm(values):
    row_mean = jnp.mean(values, axis=-1, keepdims=True)
    centred = values - row_mean
    spread = jnp.mean(centred * centred, axis=-1, keepdims=True)
    return centred * lax.rsqrt(spread + epsilon)


def rms_norm(values):
    return values * lax.rsqrt(jnp.mean(values * values, axis=-1, keepdims=True) + epsilon)


def gather_columns(block):
    count = lax.axis_size("seq")
    here = lax.axis_index("seq")
    arrived = [block] + [
        lax.ppermute(block, "seq", [(source, (source + shift) % count) for source in range(count)])
        for shift in range(1, count)
    ]
    slots = jnp.remainder(here - jnp.arange(count), count)
    order = jnp.argsort(slots)
    stacked = jnp.take(jnp.stack(arrived), order, axis=0)
    return jnp.transpose(stacked, (1, 0, 2)).reshape(block.shape[0], count * block.shape[1])


def pick_entry(vector, position):
    return jnp.sum(jnp.where(jnp.arange(vector.shape[0]) == position, vector, 0))


def attention_kernel(where_ref, mixed_ref, keys_ref, values_ref, heads_ref, keys_out, values_out):
    head_dim = keys_ref.shape[2]
    seq_len = keys_ref.shape[1]
    span = mixed_ref.shape[0]
    start = where_ref[0]
    count = where_ref[1]
    block = mixed_ref[...]
    queries = rms_norm(block[:, :head_dim]).astype(jnp.bfloat16)
    fresh_keys = rms_norm(block[:, head_dim : 2 * head_dim]).astype(jnp.bfloat16)
    fresh_values = block[:, 2 * head_dim :].astype(jnp.bfloat16)
    rows = lax.broadcasted_iota(jnp.int32, (seq_len, span), 0)
    picks = lax.broadcasted_iota(jnp.int32, (seq_len, span), 1)
    placing = ((rows == picks + start) & (picks < count)).astype(jnp.bfloat16)
    row_ids = lax.broadcasted_iota(jnp.int32, (seq_len, 1), 0)
    inside = (row_ids >= start) & (row_ids < start + count)
    placed_keys = jnp.dot(placing, fresh_keys, preferred_element_type=jnp.float32)
    placed_values = jnp.dot(placing, fresh_values, preferred_element_type=jnp.float32)
    keys = jnp.where(inside, placed_keys.astype(jnp.bfloat16), keys_ref[0])
    values = jnp.where(inside, placed_values.astype(jnp.bfloat16), values_ref[0])
    keys_out[0] = keys
    values_out[0] = values
    scores = lax.dot_general(
        queries, keys, (((1,), (1,)), ((), ())), preferred_element_type=jnp.float32
    ) * head_dim ** (-0.5)
    expos = jnp.exp(scores)
    weights = (expos / jnp.sum(expos, axis=-1, keepdims=True)).astype(jnp.bfloat16)
    heads_ref[...] = jnp.dot(weights, values, preferred_element_type=jnp.float32).astype(
        jnp.bfloat16
    )


def attend(mixed, key_cache, value_cache, patch_start, patch_count):
    heads_here, seq_len, head_dim = key_cache.shape
    span = mixed.shape[0]
    where = jnp.stack([patch_start, patch_count]).astype(jnp.int32)
    cache_spec = pl.BlockSpec((1, seq_len, head_dim), lambda h, where: (h, 0, 0))
    grid_spec = pltpu.PrefetchScalarGridSpec(
        num_scalar_prefetch=1,
        grid=(heads_here,),
        in_specs=[
            pl.BlockSpec((span, 3 * head_dim), lambda h, where: (0, h)),
            cache_spec,
            cache_spec,
        ],
        out_specs=[
            pl.BlockSpec((span, head_dim), lambda h, where: (0, h)),
            cache_spec,
            cache_spec,
        ],
    )
    return pl.pallas_call(
        attention_kernel,
        grid_spec=grid_spec,
        out_shape=[
            jax.ShapeDtypeStruct((span, heads_here * head_dim), jnp.bfloat16),
            jax.ShapeDtypeStruct(key_cache.shape, key_cache.dtype),
            jax.ShapeDtypeStruct(value_cache.shape, value_cache.dtype),
        ],
        input_output_aliases={2: 1, 3: 2},
    )(where, mixed, key_cache, value_cache)


def run_block(
    full_rows,
    own_rows,
    live_rows,
    patch_start,
    patch_count,
    key_cache,
    value_cache,
    qkv_weights,
    shift_scale,
    gating_here,
    project,
):
    shaped = (
        layer_norm(full_rows.astype(jnp.float32)) * (1.0 + shift_scale[1]) + shift_scale[0]
    ).astype(jnp.bfloat16)
    mixed = jnp.dot(shaped, qkv_weights, preferred_element_type=jnp.float32)
    head_rows, key_cache, value_cache = attend(
        mixed, key_cache, value_cache, patch_start, patch_count
    )
    projected = project(head_rows)
    updated = own_rows.astype(jnp.float32) + gating_here * projected
    updated = jnp.where(live_rows[:, None], updated, 0.0).astype(jnp.bfloat16)
    return (updated, key_cache, value_cache)


def shards(
    incoming_states,
    transit_states,
    patch_sizes_list,
    outdated_lookups,
    outdated_contents,
    attention_projection,
    exit_projection,
    shift_and_scale,
    branch_gates,
):
    section_index = lax.axis_index("section")
    patches = patch_sizes_list.shape[0]
    biggest_patch_span = transit_states.shape[1]
    columns = incoming_states.shape[1]
    heads_here = outdated_lookups.shape[1]
    head_dim = outdated_lookups.shape[3]
    starts = jnp.cumsum(patch_sizes_list) - patch_sizes_list
    key_cache = outdated_lookups[0]
    value_cache = outdated_contents[0]
    qkv_weights = attention_projection[0]
    out_weights = exit_projection[0]
    shift_scale = shift_and_scale[0]
    gating_here = branch_gates[0]
    row_numbers = jnp.arange(biggest_patch_span)

    def gather_heads(head_rows):
        every_head = gather_columns(head_rows)
        return jnp.dot(every_head, out_weights, preferred_element_type=jnp.float32)

    results = []
    entering_ext = jnp.concatenate(
        [incoming_states, jnp.zeros((biggest_patch_span, columns), jnp.bfloat16)], axis=0
    )
    earlier_result = transit_states[0]
    for turn_number in range(patches):
        patch_index = jnp.remainder(turn_number - section_index, patches)
        patch_count = pick_entry(patch_sizes_list, patch_index)
        patch_start = pick_entry(starts, patch_index)
        live_rows = row_numbers < patch_count
        entry_patch = lax.dynamic_slice_in_dim(
            entering_ext, starts[turn_number], biggest_patch_span, 0
        )
        own_rows = jnp.where(section_index == 0, entry_patch, earlier_result)
        own_rows = jnp.where(live_rows[:, None], own_rows, jnp.zeros_like(own_rows))
        full_rows = gather_columns(own_rows)
        updated, key_cache, value_cache = run_block(
            full_rows,
            own_rows,
            live_rows,
            patch_start,
            patch_count,
            key_cache,
            value_cache,
            qkv_weights,
            shift_scale,
            gating_here,
            gather_heads,
        )
        results.append(updated)
        if turn_number + 1 < patches:
            earlier_result = passed_along(updated, "section", 1)
    return jnp.stack(results)[:, None]


def solution(mesh):
    return jax.shard_map(
        shards,
        mesh=mesh,
        in_specs=(
            P("groups", "seq"),
            P("section", "groups", "seq"),
            P("groups"),
            P("section", "seq", "groups", None),
            P("section", "seq", "groups", None),
            P("section", None, "seq"),
            P("section", None, "seq"),
            P("section", None, None),
            P("section", "seq"),
        ),
        out_specs=P(None, "section", "groups", "seq"),
        check_vma=False,
    )
```

```python
import jax
import jax.numpy as jnp
from jax import lax
from jax.experimental import pallas as pl
from jax.experimental.pallas import tpu as pltpu
from jax.sharding import PartitionSpec as P

epsilon = 1e-06


def passed_along(value, axis, steps):
    count = lax.axis_size(axis)
    leading, last = (max(0, -steps), min(count, count - steps))
    return lax.ppermute(value, axis, [(source, source + steps) for source in range(leading, last)])


def rms_norm(values):
    return values * lax.rsqrt(jnp.mean(values * values, axis=-1, keepdims=True) + epsilon)


def pick_entry(vector, position):
    return jnp.sum(jnp.where(jnp.arange(vector.shape[0]) == position, vector, 0))


def spread_over_seq(block):
    count = lax.axis_size("seq")
    return [block] + [
        lax.ppermute(block, "seq", [(source, (source + shift) % count) for source in range(count)])
        for shift in range(1, count)
    ]


def block_kernel(*refs):
    where_ref = refs[0]
    count = (len(refs) - 9) // 1
    part_refs = refs[1 : 1 + count]
    scale_ref, weights_ref, keys_ref, values_ref = refs[1 + count : 5 + count]
    heads_ref, keys_out, values_out = refs[5 + count : 8 + count]
    shaped_ref = refs[8 + count]
    start = where_ref[0]
    patch_count = where_ref[1]
    here = where_ref[2]
    head_dim = keys_ref.shape[2]
    seq_len = keys_ref.shape[1]
    span, width = part_refs[0].shape
    features = width * count

    @pl.when(pl.program_id(0) == 0)
    def _():
        parts = [part[...].astype(jnp.float32) for part in part_refs]
        row_mean = sum(jnp.sum(part, axis=-1, keepdims=True) for part in parts) / features
        centred = [part - row_mean for part in parts]
        spread = sum(jnp.sum(c * c, axis=-1, keepdims=True) for c in centred) / features
        inverse = lax.rsqrt(spread + epsilon)
        for shift in range(count):
            slot = lax.rem(here - shift + count, count)
            shift_scale = scale_ref[slot]
            shaped_ref[slot] = (
                (centred[shift] * inverse) * (1.0 + shift_scale[1:2]) + shift_scale[0:1]
            ).astype(jnp.bfloat16)

    mixed = sum(
        jnp.dot(
            shaped_ref[slot],
            weights_ref[slot * width : (slot + 1) * width, :],
            preferred_element_type=jnp.float32,
        )
        for slot in range(count)
    )
    queries = rms_norm(mixed[:, :head_dim]).astype(jnp.bfloat16)
    fresh_keys = rms_norm(mixed[:, head_dim : 2 * head_dim]).astype(jnp.bfloat16)
    fresh_values = mixed[:, 2 * head_dim :].astype(jnp.bfloat16)
    rows = lax.broadcasted_iota(jnp.int32, (seq_len, span), 0)
    picks = lax.broadcasted_iota(jnp.int32, (seq_len, span), 1)
    placing = ((rows == picks + start) & (picks < patch_count)).astype(jnp.bfloat16)
    row_ids = lax.broadcasted_iota(jnp.int32, (seq_len, 1), 0)
    inside = (row_ids >= start) & (row_ids < start + patch_count)
    placed_keys = jnp.dot(placing, fresh_keys, preferred_element_type=jnp.float32)
    placed_values = jnp.dot(placing, fresh_values, preferred_element_type=jnp.float32)
    keys = jnp.where(inside, placed_keys.astype(jnp.bfloat16), keys_ref[0])
    values = jnp.where(inside, placed_values.astype(jnp.bfloat16), values_ref[0])
    keys_out[0] = keys
    values_out[0] = values
    scores = lax.dot_general(
        queries, keys, (((1,), (1,)), ((), ())), preferred_element_type=jnp.float32
    ) * head_dim ** (-0.5)
    expos = jnp.exp(scores)
    weights = (expos / jnp.sum(expos, axis=-1, keepdims=True)).astype(jnp.bfloat16)
    heads_ref[...] = jnp.dot(weights, values, preferred_element_type=jnp.float32).astype(
        jnp.bfloat16
    )


def attend_block(parts, shift_scale, qkv_weights, key_cache, value_cache, where):
    count = len(parts)
    span, width = parts[0].shape
    heads_here, seq_len, head_dim = key_cache.shape
    features = qkv_weights.shape[0]
    scale_blocks = jnp.transpose(shift_scale.reshape(2, count, width), (1, 0, 2))
    whole = lambda shape: pl.BlockSpec(shape, lambda h, where: (0,) * len(shape))
    cache_spec = pl.BlockSpec((1, seq_len, head_dim), lambda h, where: (h, 0, 0))
    grid_spec = pltpu.PrefetchScalarGridSpec(
        num_scalar_prefetch=1,
        grid=(heads_here,),
        in_specs=[whole((span, width)) for _ in parts]
        + [
            whole((count, 2, width)),
            pl.BlockSpec((features, 3 * head_dim), lambda h, where: (0, h)),
            cache_spec,
            cache_spec,
        ],
        out_specs=[
            pl.BlockSpec((span, head_dim), lambda h, where: (0, h)),
            cache_spec,
            cache_spec,
        ],
        scratch_shapes=[pltpu.VMEM((count, span, width), jnp.bfloat16)],
    )
    return pl.pallas_call(
        block_kernel,
        grid_spec=grid_spec,
        out_shape=[
            jax.ShapeDtypeStruct((span, heads_here * head_dim), jnp.bfloat16),
            jax.ShapeDtypeStruct(key_cache.shape, key_cache.dtype),
            jax.ShapeDtypeStruct(value_cache.shape, value_cache.dtype),
        ],
        input_output_aliases={count + 3: 1, count + 4: 2},
        compiler_params=pltpu.CompilerParams(dimension_semantics=("arbitrary",)),
    )(where, *parts, scale_blocks, qkv_weights, key_cache, value_cache)


def exit_kernel(*refs):
    where_ref = refs[0]
    count = len(refs) - 5
    part_refs = refs[1 : 1 + count]
    weights_ref, own_ref, gate_ref = refs[1 + count : 4 + count]
    out_ref = refs[4 + count]
    patch_count = where_ref[1]
    here = where_ref[2]
    projected = sum(
        jnp.dot(
            part_refs[shift][...],
            weights_ref[lax.rem(here - shift + count, count)],
            preferred_element_type=jnp.float32,
        )
        for shift in range(count)
    )
    updated = own_ref[...].astype(jnp.float32) + gate_ref[...] * projected
    live = lax.broadcasted_iota(jnp.int32, updated.shape, 0) < patch_count
    out_ref[...] = jnp.where(live, updated, 0.0).astype(out_ref.dtype)


def leave_block(parts, out_weights, own_rows, gating_here, where):
    count = len(parts)
    span, head_width = parts[0].shape
    vmem = pl.BlockSpec(memory_space=pltpu.VMEM)
    smem = pl.BlockSpec(memory_space=pltpu.SMEM)
    return pl.pallas_call(
        exit_kernel,
        in_specs=[smem] + [vmem] * (count + 3),
        out_specs=vmem,
        out_shape=jax.ShapeDtypeStruct(own_rows.shape, own_rows.dtype),
    )(
        where,
        *parts,
        out_weights.reshape(count, head_width, out_weights.shape[1]),
        own_rows,
        gating_here.reshape(1, -1),
    )


def shards(
    incoming_states,
    transit_states,
    patch_sizes_list,
    outdated_lookups,
    outdated_contents,
    attention_projection,
    exit_projection,
    shift_and_scale,
    branch_gates,
):
    section_index = lax.axis_index("section")
    seq_index = lax.axis_index("seq")
    patches = patch_sizes_list.shape[0]
    biggest_patch_span = transit_states.shape[1]
    columns = incoming_states.shape[1]
    starts = jnp.cumsum(patch_sizes_list) - patch_sizes_list
    key_cache = outdated_lookups[0]
    value_cache = outdated_contents[0]
    qkv_weights = attention_projection[0]
    out_weights = exit_projection[0]
    shift_scale = shift_and_scale[0]
    gating_here = branch_gates[0]
    row_numbers = jnp.arange(biggest_patch_span)

    results = []
    entering_ext = jnp.concatenate(
        [incoming_states, jnp.zeros((biggest_patch_span, columns), jnp.bfloat16)], axis=0
    )
    earlier_result = transit_states[0]
    for turn_number in range(patches):
        patch_index = jnp.remainder(turn_number - section_index, patches)
        patch_count = pick_entry(patch_sizes_list, patch_index)
        patch_start = pick_entry(starts, patch_index)
        where = jnp.stack([patch_start, patch_count, seq_index]).astype(jnp.int32)
        live_rows = row_numbers < patch_count
        entry_patch = lax.dynamic_slice_in_dim(
            entering_ext, starts[turn_number], biggest_patch_span, 0
        )
        own_rows = jnp.where(section_index == 0, entry_patch, earlier_result)
        own_rows = jnp.where(live_rows[:, None], own_rows, jnp.zeros_like(own_rows))
        head_rows, key_cache, value_cache = attend_block(
            spread_over_seq(own_rows), shift_scale, qkv_weights, key_cache, value_cache, where
        )
        updated = leave_block(spread_over_seq(head_rows), out_weights, own_rows, gating_here, where)
        results.append(updated)
        if turn_number + 1 < patches:
            earlier_result = passed_along(updated, "section", 1)
    return jnp.stack(results)[:, None]


def solution(mesh):
    return jax.shard_map(
        shards,
        mesh=mesh,
        in_specs=(
            P("groups", "seq"),
            P("section", "groups", "seq"),
            P("groups"),
            P("section", "seq", "groups", None),
            P("section", "seq", "groups", None),
            P("section", None, "seq"),
            P("section", None, "seq"),
            P("section", None, None),
            P("section", "seq"),
        ),
        out_specs=P(None, "section", "groups", "seq"),
        check_vma=False,
    )
```

```python
import jax
import jax.numpy as jnp
from jax import lax
from jax.experimental import pallas as pl
from jax.experimental.pallas import tpu as pltpu
from jax.sharding import PartitionSpec as P

epsilon = 1e-06


def passed_along(value, axis, steps):
    count = lax.axis_size(axis)
    leading, last = (max(0, -steps), min(count, count - steps))
    return lax.ppermute(value, axis, [(source, source + steps) for source in range(leading, last)])


def rms_norm(values):
    return values * lax.rsqrt(jnp.mean(values * values, axis=-1, keepdims=True) + epsilon)


def pick_entry(vector, position):
    return jnp.sum(jnp.where(jnp.arange(vector.shape[0]) == position, vector, 0))


def spread_over_seq(block):
    count = lax.axis_size("seq")
    here = lax.axis_index("seq")
    partner = jnp.bitwise_xor(here, 1)
    to_partner = [(source, source ^ 1) for source in range(count)]
    across = [
        lax.ppermute(block, "seq", [(source, (source + step) % count) for source in range(count)])
        for step in range(2, count, 2)
    ]
    from_partner = lax.ppermute(block, "seq", to_partner)
    relayed = [lax.ppermute(part, "seq", to_partner) for part in across]
    sources = (
        [here]
        + [jnp.remainder(here - step, count) for step in range(2, count, 2)]
        + [partner]
        + [jnp.remainder(partner - step, count) for step in range(2, count, 2)]
    )
    return [block] + across + [from_partner] + relayed, sources


def block_kernel(*refs):
    where_ref = refs[0]
    count = len(refs) - 9
    part_refs = refs[1 : 1 + count]
    scale_ref, weights_ref, keys_ref, values_ref = refs[1 + count : 5 + count]
    heads_ref, keys_out, values_out = refs[5 + count : 8 + count]
    shaped_ref = refs[8 + count]
    start = where_ref[0]
    patch_count = where_ref[1]
    head_dim = keys_ref.shape[2]
    seq_len = keys_ref.shape[1]
    span, width = part_refs[0].shape
    features = width * count

    @pl.when(pl.program_id(0) == 0)
    def _():
        parts = [part[...].astype(jnp.float32) for part in part_refs]
        row_mean = sum(jnp.sum(part, axis=-1, keepdims=True) for part in parts) / features
        centred = [part - row_mean for part in parts]
        spread = sum(jnp.sum(c * c, axis=-1, keepdims=True) for c in centred) / features
        inverse = lax.rsqrt(spread + epsilon)
        for part in range(count):
            slot = where_ref[2 + part]
            shift_scale = scale_ref[slot]
            shaped_ref[slot] = (
                (centred[part] * inverse) * (1.0 + shift_scale[1:2]) + shift_scale[0:1]
            ).astype(jnp.bfloat16)

    mixed = sum(
        jnp.dot(
            shaped_ref[slot],
            weights_ref[slot * width : (slot + 1) * width, :],
            preferred_element_type=jnp.float32,
        )
        for slot in range(count)
    )
    queries = rms_norm(mixed[:, :head_dim]).astype(jnp.bfloat16)
    fresh_keys = rms_norm(mixed[:, head_dim : 2 * head_dim]).astype(jnp.bfloat16)
    fresh_values = mixed[:, 2 * head_dim :].astype(jnp.bfloat16)
    rows = lax.broadcasted_iota(jnp.int32, (seq_len, span), 0)
    picks = lax.broadcasted_iota(jnp.int32, (seq_len, span), 1)
    placing = ((rows == picks + start) & (picks < patch_count)).astype(jnp.bfloat16)
    row_ids = lax.broadcasted_iota(jnp.int32, (seq_len, 1), 0)
    inside = (row_ids >= start) & (row_ids < start + patch_count)
    placed_keys = jnp.dot(placing, fresh_keys, preferred_element_type=jnp.float32)
    placed_values = jnp.dot(placing, fresh_values, preferred_element_type=jnp.float32)
    keys = jnp.where(inside, placed_keys.astype(jnp.bfloat16), keys_ref[0])
    values = jnp.where(inside, placed_values.astype(jnp.bfloat16), values_ref[0])
    keys_out[0] = keys
    values_out[0] = values
    scores = lax.dot_general(
        queries, keys, (((1,), (1,)), ((), ())), preferred_element_type=jnp.float32
    ) * head_dim ** (-0.5)
    expos = jnp.exp(scores)
    weights = (expos / jnp.sum(expos, axis=-1, keepdims=True)).astype(jnp.bfloat16)
    heads_ref[...] = jnp.dot(weights, values, preferred_element_type=jnp.float32).astype(
        jnp.bfloat16
    )


def attend_block(parts, shift_scale, qkv_weights, key_cache, value_cache, where):
    count = len(parts)
    span, width = parts[0].shape
    heads_here, seq_len, head_dim = key_cache.shape
    features = qkv_weights.shape[0]
    scale_blocks = jnp.transpose(shift_scale.reshape(2, count, width), (1, 0, 2))
    whole = lambda shape: pl.BlockSpec(shape, lambda h, where: (0,) * len(shape))
    cache_spec = pl.BlockSpec((1, seq_len, head_dim), lambda h, where: (h, 0, 0))
    grid_spec = pltpu.PrefetchScalarGridSpec(
        num_scalar_prefetch=1,
        grid=(heads_here,),
        in_specs=[whole((span, width)) for _ in parts]
        + [
            whole((count, 2, width)),
            pl.BlockSpec((features, 3 * head_dim), lambda h, where: (0, h)),
            cache_spec,
            cache_spec,
        ],
        out_specs=[
            pl.BlockSpec((span, head_dim), lambda h, where: (0, h)),
            cache_spec,
            cache_spec,
        ],
        scratch_shapes=[pltpu.VMEM((count, span, width), jnp.bfloat16)],
    )
    return pl.pallas_call(
        block_kernel,
        grid_spec=grid_spec,
        out_shape=[
            jax.ShapeDtypeStruct((span, heads_here * head_dim), jnp.bfloat16),
            jax.ShapeDtypeStruct(key_cache.shape, key_cache.dtype),
            jax.ShapeDtypeStruct(value_cache.shape, value_cache.dtype),
        ],
        input_output_aliases={count + 3: 1, count + 4: 2},
        compiler_params=pltpu.CompilerParams(dimension_semantics=("arbitrary",)),
    )(where, *parts, scale_blocks, qkv_weights, key_cache, value_cache)


def exit_kernel(*refs):
    where_ref = refs[0]
    count = len(refs) - 5
    part_refs = refs[1 : 1 + count]
    weights_ref, own_ref, gate_ref = refs[1 + count : 4 + count]
    out_ref = refs[4 + count]
    patch_count = where_ref[1]
    projected = sum(
        jnp.dot(
            part_refs[part][...],
            weights_ref[where_ref[2 + part]],
            preferred_element_type=jnp.float32,
        )
        for part in range(count)
    )
    updated = own_ref[...].astype(jnp.float32) + gate_ref[...] * projected
    live = lax.broadcasted_iota(jnp.int32, updated.shape, 0) < patch_count
    out_ref[...] = jnp.where(live, updated, 0.0).astype(out_ref.dtype)


def leave_block(parts, out_weights, own_rows, gating_here, where):
    count = len(parts)
    span, head_width = parts[0].shape
    vmem = pl.BlockSpec(memory_space=pltpu.VMEM)
    smem = pl.BlockSpec(memory_space=pltpu.SMEM)
    return pl.pallas_call(
        exit_kernel,
        in_specs=[smem] + [vmem] * (count + 3),
        out_specs=vmem,
        out_shape=jax.ShapeDtypeStruct(own_rows.shape, own_rows.dtype),
    )(
        where,
        *parts,
        out_weights.reshape(count, head_width, out_weights.shape[1]),
        own_rows,
        gating_here.reshape(1, -1),
    )


def shards(
    incoming_states,
    transit_states,
    patch_sizes_list,
    outdated_lookups,
    outdated_contents,
    attention_projection,
    exit_projection,
    shift_and_scale,
    branch_gates,
):
    section_index = lax.axis_index("section")
    patches = patch_sizes_list.shape[0]
    biggest_patch_span = transit_states.shape[1]
    columns = incoming_states.shape[1]
    starts = jnp.cumsum(patch_sizes_list) - patch_sizes_list
    key_cache = outdated_lookups[0]
    value_cache = outdated_contents[0]
    qkv_weights = attention_projection[0]
    out_weights = exit_projection[0]
    shift_scale = shift_and_scale[0]
    gating_here = branch_gates[0]
    row_numbers = jnp.arange(biggest_patch_span)

    results = []
    entering_ext = jnp.concatenate(
        [incoming_states, jnp.zeros((biggest_patch_span, columns), jnp.bfloat16)], axis=0
    )
    earlier_result = transit_states[0]
    for turn_number in range(patches):
        patch_index = jnp.remainder(turn_number - section_index, patches)
        patch_count = pick_entry(patch_sizes_list, patch_index)
        patch_start = pick_entry(starts, patch_index)
        where = jnp.stack([patch_start, patch_count]).astype(jnp.int32)
        live_rows = row_numbers < patch_count
        entry_patch = lax.dynamic_slice_in_dim(
            entering_ext, starts[turn_number], biggest_patch_span, 0
        )
        own_rows = jnp.where(section_index == 0, entry_patch, earlier_result)
        own_rows = jnp.where(live_rows[:, None], own_rows, jnp.zeros_like(own_rows))
        row_parts, row_sources = spread_over_seq(own_rows)
        head_rows, key_cache, value_cache = attend_block(
            row_parts,
            shift_scale,
            qkv_weights,
            key_cache,
            value_cache,
            jnp.concatenate([where, jnp.stack(row_sources).astype(jnp.int32)]),
        )
        head_parts, head_sources = spread_over_seq(head_rows)
        updated = leave_block(
            head_parts,
            out_weights,
            own_rows,
            gating_here,
            jnp.concatenate([where, jnp.stack(head_sources).astype(jnp.int32)]),
        )
        results.append(updated)
        if turn_number + 1 < patches:
            earlier_result = passed_along(updated, "section", 1)
    return jnp.stack(results)[:, None]


def solution(mesh):
    return jax.shard_map(
        shards,
        mesh=mesh,
        in_specs=(
            P("groups", "seq"),
            P("section", "groups", "seq"),
            P("groups"),
            P("section", "seq", "groups", None),
            P("section", "seq", "groups", None),
            P("section", None, "seq"),
            P("section", None, "seq"),
            P("section", None, None),
            P("section", "seq"),
        ),
        out_specs=P(None, "section", "groups", "seq"),
        check_vma=False,
    )
```

```python
import jax
import jax.numpy as jnp
from jax import lax
from jax.experimental import pallas as pl
from jax.experimental.pallas import tpu as pltpu
from jax.sharding import PartitionSpec as P

epsilon = 1e-06


def passed_along(value, axis, steps):
    count = lax.axis_size(axis)
    leading, last = (max(0, -steps), min(count, count - steps))
    return lax.ppermute(value, axis, [(source, source + steps) for source in range(leading, last)])


def rms_norm(values):
    return values * lax.rsqrt(jnp.mean(values * values, axis=-1, keepdims=True) + epsilon)


def pick_entry(vector, position):
    return jnp.sum(jnp.where(jnp.arange(vector.shape[0]) == position, vector, 0))


def spread_over_seq(block):
    count = lax.axis_size("seq")
    to_partner = [(source, source ^ 1) for source in range(count)]
    across = [
        lax.ppermute(block, "seq", [(source, (source + step) % count) for source in range(count)])
        for step in range(2, count, 2)
    ]
    from_partner = lax.ppermute(block, "seq", to_partner)
    relayed = [lax.ppermute(part, "seq", to_partner) for part in across]
    return [block] + across + [from_partner] + relayed


def kernel_table(patch_start, patch_count):
    count = lax.axis_size("seq")
    here = lax.axis_index("seq")
    chips = count // 2
    entry = jnp.arange(count + 2) - 2
    base = jnp.where(entry < chips, here, jnp.bitwise_xor(here, 1))
    sources = jnp.remainder(base - 2 * jnp.remainder(entry, chips) + count, count)
    return jnp.where(entry == -2, patch_start, jnp.where(entry == -1, patch_count, sources)).astype(
        jnp.int32
    )


def block_kernel(*refs):
    where_ref = refs[0]
    count = len(refs) - 9
    part_refs = refs[1 : 1 + count]
    scale_ref, weights_ref, keys_ref, values_ref = refs[1 + count : 5 + count]
    heads_ref, keys_out, values_out = refs[5 + count : 8 + count]
    shaped_ref = refs[8 + count]
    start = where_ref[0]
    patch_count = where_ref[1]
    head_dim = keys_ref.shape[2]
    seq_len = keys_ref.shape[1]
    span, width = part_refs[0].shape
    features = width * count

    @pl.when(pl.program_id(0) == 0)
    def _():
        parts = [part[...].astype(jnp.float32) for part in part_refs]
        row_mean = sum(jnp.sum(part, axis=-1, keepdims=True) for part in parts) / features
        centred = [part - row_mean for part in parts]
        spread = sum(jnp.sum(c * c, axis=-1, keepdims=True) for c in centred) / features
        inverse = lax.rsqrt(spread + epsilon)
        for part in range(count):
            slot = where_ref[2 + part]
            shift_scale = scale_ref[slot]
            shaped_ref[slot] = (
                (centred[part] * inverse) * (1.0 + shift_scale[1:2]) + shift_scale[0:1]
            ).astype(jnp.bfloat16)

    mixed = sum(
        jnp.dot(
            shaped_ref[slot],
            weights_ref[slot * width : (slot + 1) * width, :],
            preferred_element_type=jnp.float32,
        )
        for slot in range(count)
    )
    queries = rms_norm(mixed[:, :head_dim]).astype(jnp.bfloat16)
    fresh_keys = rms_norm(mixed[:, head_dim : 2 * head_dim]).astype(jnp.bfloat16)
    fresh_values = mixed[:, 2 * head_dim :].astype(jnp.bfloat16)
    rows = lax.broadcasted_iota(jnp.int32, (seq_len, span), 0)
    picks = lax.broadcasted_iota(jnp.int32, (seq_len, span), 1)
    placing = ((rows == picks + start) & (picks < patch_count)).astype(jnp.bfloat16)
    row_ids = lax.broadcasted_iota(jnp.int32, (seq_len, 1), 0)
    inside = (row_ids >= start) & (row_ids < start + patch_count)
    placed_keys = jnp.dot(placing, fresh_keys, preferred_element_type=jnp.float32)
    placed_values = jnp.dot(placing, fresh_values, preferred_element_type=jnp.float32)
    keys = jnp.where(inside, placed_keys.astype(jnp.bfloat16), keys_ref[0])
    values = jnp.where(inside, placed_values.astype(jnp.bfloat16), values_ref[0])
    keys_out[0] = keys
    values_out[0] = values
    scores = lax.dot_general(
        queries, keys, (((1,), (1,)), ((), ())), preferred_element_type=jnp.float32
    ) * head_dim ** (-0.5)
    expos = jnp.exp(scores)
    weights = (expos / jnp.sum(expos, axis=-1, keepdims=True)).astype(jnp.bfloat16)
    heads_ref[...] = jnp.dot(weights, values, preferred_element_type=jnp.float32).astype(
        jnp.bfloat16
    )


def attend_block(parts, shift_scale, qkv_weights, key_cache, value_cache, where, in_place):
    count = len(parts)
    span, width = parts[0].shape
    heads_here, seq_len, head_dim = key_cache.shape
    features = qkv_weights.shape[0]
    scale_blocks = jnp.transpose(shift_scale.reshape(2, count, width), (1, 0, 2))
    whole = lambda shape: pl.BlockSpec(shape, lambda h, where: (0,) * len(shape))
    cache_spec = pl.BlockSpec((1, seq_len, head_dim), lambda h, where: (h, 0, 0))
    grid_spec = pltpu.PrefetchScalarGridSpec(
        num_scalar_prefetch=1,
        grid=(heads_here,),
        in_specs=[whole((span, width)) for _ in parts]
        + [
            whole((count, 2, width)),
            pl.BlockSpec((features, 3 * head_dim), lambda h, where: (0, h)),
            cache_spec,
            cache_spec,
        ],
        out_specs=[
            pl.BlockSpec((span, head_dim), lambda h, where: (0, h)),
            cache_spec,
            cache_spec,
        ],
        scratch_shapes=[pltpu.VMEM((count, span, width), jnp.bfloat16)],
    )
    return pl.pallas_call(
        block_kernel,
        grid_spec=grid_spec,
        out_shape=[
            jax.ShapeDtypeStruct((span, heads_here * head_dim), jnp.bfloat16),
            jax.ShapeDtypeStruct(key_cache.shape, key_cache.dtype),
            jax.ShapeDtypeStruct(value_cache.shape, value_cache.dtype),
        ],
        input_output_aliases={count + 3: 1, count + 4: 2} if in_place else {},
        compiler_params=pltpu.CompilerParams(dimension_semantics=("arbitrary",)),
    )(where, *parts, scale_blocks, qkv_weights, key_cache, value_cache)


def exit_kernel(*refs):
    where_ref = refs[0]
    count = len(refs) - 5
    part_refs = refs[1 : 1 + count]
    weights_ref, own_ref, gate_ref = refs[1 + count : 4 + count]
    out_ref = refs[4 + count]
    patch_count = where_ref[1]
    projected = sum(
        jnp.dot(
            part_refs[part][...],
            weights_ref[where_ref[2 + part]],
            preferred_element_type=jnp.float32,
        )
        for part in range(count)
    )
    updated = own_ref[...].astype(jnp.float32) + gate_ref[...] * projected
    live = lax.broadcasted_iota(jnp.int32, updated.shape, 0) < patch_count
    out_ref[...] = jnp.where(live, updated, 0.0).astype(out_ref.dtype)


def leave_block(parts, out_weights, own_rows, gating_here, where):
    count = len(parts)
    span, head_width = parts[0].shape
    vmem = pl.BlockSpec(memory_space=pltpu.VMEM)
    smem = pl.BlockSpec(memory_space=pltpu.SMEM)
    return pl.pallas_call(
        exit_kernel,
        in_specs=[smem] + [vmem] * (count + 3),
        out_specs=vmem,
        out_shape=jax.ShapeDtypeStruct(own_rows.shape, own_rows.dtype),
    )(
        where,
        *parts,
        out_weights.reshape(count, head_width, out_weights.shape[1]),
        own_rows,
        gating_here.reshape(1, -1),
    )


def shards(
    incoming_states,
    transit_states,
    patch_sizes_list,
    outdated_lookups,
    outdated_contents,
    attention_projection,
    exit_projection,
    shift_and_scale,
    branch_gates,
):
    section_index = lax.axis_index("section")
    patches = patch_sizes_list.shape[0]
    biggest_patch_span = transit_states.shape[1]
    columns = incoming_states.shape[1]
    starts = jnp.cumsum(patch_sizes_list) - patch_sizes_list
    key_cache = outdated_lookups[0]
    value_cache = outdated_contents[0]
    qkv_weights = attention_projection[0]
    out_weights = exit_projection[0]
    shift_scale = shift_and_scale[0]
    gating_here = branch_gates[0]
    row_numbers = jnp.arange(biggest_patch_span)

    results = []
    entering_ext = jnp.concatenate(
        [incoming_states, jnp.zeros((biggest_patch_span, columns), jnp.bfloat16)], axis=0
    )
    earlier_result = transit_states[0]
    for turn_number in range(patches):
        patch_index = jnp.remainder(turn_number - section_index, patches)
        patch_count = pick_entry(patch_sizes_list, patch_index)
        patch_start = pick_entry(starts, patch_index)
        where = kernel_table(patch_start, patch_count)
        live_rows = row_numbers < patch_count
        entry_patch = lax.dynamic_slice_in_dim(
            entering_ext, starts[turn_number], biggest_patch_span, 0
        )
        own_rows = jnp.where(section_index == 0, entry_patch, earlier_result)
        own_rows = jnp.where(live_rows[:, None], own_rows, jnp.zeros_like(own_rows))
        head_rows, key_cache, value_cache = attend_block(
            spread_over_seq(own_rows),
            shift_scale,
            qkv_weights,
            key_cache,
            value_cache,
            where,
            turn_number > 0,
        )
        updated = leave_block(
            spread_over_seq(head_rows), out_weights, own_rows, gating_here, where
        )
        results.append(updated)
        if turn_number + 1 < patches:
            earlier_result = passed_along(updated, "section", 1)
    return jnp.stack(results)[:, None]


def solution(mesh):
    return jax.shard_map(
        shards,
        mesh=mesh,
        in_specs=(
            P("groups", "seq"),
            P("section", "groups", "seq"),
            P("groups"),
            P("section", "seq", "groups", None),
            P("section", "seq", "groups", None),
            P("section", None, "seq"),
            P("section", None, "seq"),
            P("section", None, None),
            P("section", "seq"),
        ),
        out_specs=P(None, "section", "groups", "seq"),
        check_vma=False,
    )
```

```python
import jax
import jax.numpy as jnp
from jax import lax
from jax.experimental import pallas as pl
from jax.experimental.pallas import tpu as pltpu
from jax.sharding import PartitionSpec as P

epsilon = 1e-06


def rms_norm(values):
    return values * lax.rsqrt(jnp.mean(values * values, axis=-1, keepdims=True) + epsilon)


def pick_entry(vector, position):
    return jnp.sum(jnp.where(jnp.arange(vector.shape[0]) == position, vector, 0))


def across_chips(block):
    count = lax.axis_size("seq")
    return [
        lax.ppermute(block, "seq", [(source, (source + step) % count) for source in range(count)])
        for step in range(2, count, 2)
    ]


def across_chips_first_section(block):
    count = lax.axis_size("seq")
    return [
        lax.ppermute(
            block, ("section", "seq"), [(source, (source + step) % count) for source in range(count)]
        )
        for step in range(2, count, 2)
    ]


def with_partner(parts):
    count = lax.axis_size("seq")
    to_partner = [(source, source ^ 1) for source in range(count)]
    return parts + [lax.ppermute(part, "seq", to_partner) for part in parts]


def to_next_section(block):
    sections = lax.axis_size("section")
    count = lax.axis_size("seq")
    return [
        lax.ppermute(
            block,
            ("section", "seq"),
            [
                (section * count + source, (section + 1) * count + (source + step) % count)
                for section in range(sections - 1)
                for source in range(count)
            ],
        )
        for step in range(0, count, 2)
    ]


def kernel_table(patch_start, patch_count):
    count = lax.axis_size("seq")
    here = lax.axis_index("seq")
    chips = count // 2
    entry = jnp.arange(count + 2) - 2
    base = jnp.where(entry < chips, here, jnp.bitwise_xor(here, 1))
    sources = jnp.remainder(base - 2 * jnp.remainder(entry, chips) + count, count)
    return jnp.where(entry == -2, patch_start, jnp.where(entry == -1, patch_count, sources)).astype(
        jnp.int32
    )


def block_kernel(*refs):
    where_ref = refs[0]
    count = len(refs) - 9
    part_refs = refs[1 : 1 + count]
    scale_ref, weights_ref, keys_ref, values_ref = refs[1 + count : 5 + count]
    heads_ref, keys_out, values_out = refs[5 + count : 8 + count]
    shaped_ref = refs[8 + count]
    start = where_ref[0]
    patch_count = where_ref[1]
    head_dim = keys_ref.shape[2]
    seq_len = keys_ref.shape[1]
    span, width = part_refs[0].shape
    features = width * count

    @pl.when(pl.program_id(0) == 0)
    def _():
        parts = [part[...].astype(jnp.float32) for part in part_refs]
        row_mean = sum(jnp.sum(part, axis=-1, keepdims=True) for part in parts) / features
        centred = [part - row_mean for part in parts]
        spread = sum(jnp.sum(c * c, axis=-1, keepdims=True) for c in centred) / features
        inverse = lax.rsqrt(spread + epsilon)
        for part in range(count):
            slot = where_ref[2 + part]
            shift_scale = scale_ref[slot]
            shaped_ref[slot] = (
                (centred[part] * inverse) * (1.0 + shift_scale[1:2]) + shift_scale[0:1]
            ).astype(jnp.bfloat16)

    mixed = sum(
        jnp.dot(
            shaped_ref[slot],
            weights_ref[slot * width : (slot + 1) * width, :],
            preferred_element_type=jnp.float32,
        )
        for slot in range(count)
    )
    queries = rms_norm(mixed[:, :head_dim]).astype(jnp.bfloat16)
    fresh_keys = rms_norm(mixed[:, head_dim : 2 * head_dim]).astype(jnp.bfloat16)
    fresh_values = mixed[:, 2 * head_dim :].astype(jnp.bfloat16)
    rows = lax.broadcasted_iota(jnp.int32, (seq_len, span), 0)
    picks = lax.broadcasted_iota(jnp.int32, (seq_len, span), 1)
    placing = ((rows == picks + start) & (picks < patch_count)).astype(jnp.bfloat16)
    row_ids = lax.broadcasted_iota(jnp.int32, (seq_len, 1), 0)
    inside = (row_ids >= start) & (row_ids < start + patch_count)
    placed_keys = jnp.dot(placing, fresh_keys, preferred_element_type=jnp.float32)
    placed_values = jnp.dot(placing, fresh_values, preferred_element_type=jnp.float32)
    keys = jnp.where(inside, placed_keys.astype(jnp.bfloat16), keys_ref[0])
    values = jnp.where(inside, placed_values.astype(jnp.bfloat16), values_ref[0])
    keys_out[0] = keys
    values_out[0] = values
    scores = lax.dot_general(
        queries, keys, (((1,), (1,)), ((), ())), preferred_element_type=jnp.float32
    ) * head_dim ** (-0.5)
    expos = jnp.exp(scores)
    weights = (expos / jnp.sum(expos, axis=-1, keepdims=True)).astype(jnp.bfloat16)
    heads_ref[...] = jnp.dot(weights, values, preferred_element_type=jnp.float32).astype(
        jnp.bfloat16
    )


def attend_block(parts, shift_scale, qkv_weights, key_cache, value_cache, where, in_place):
    count = len(parts)
    span, width = parts[0].shape
    heads_here, seq_len, head_dim = key_cache.shape
    features = qkv_weights.shape[0]
    scale_blocks = jnp.transpose(shift_scale.reshape(2, count, width), (1, 0, 2))
    whole = lambda shape: pl.BlockSpec(shape, lambda h, where: (0,) * len(shape))
    cache_spec = pl.BlockSpec((1, seq_len, head_dim), lambda h, where: (h, 0, 0))
    grid_spec = pltpu.PrefetchScalarGridSpec(
        num_scalar_prefetch=1,
        grid=(heads_here,),
        in_specs=[whole((span, width)) for _ in parts]
        + [
            whole((count, 2, width)),
            pl.BlockSpec((features, 3 * head_dim), lambda h, where: (0, h)),
            cache_spec,
            cache_spec,
        ],
        out_specs=[
            pl.BlockSpec((span, head_dim), lambda h, where: (0, h)),
            cache_spec,
            cache_spec,
        ],
        scratch_shapes=[pltpu.VMEM((count, span, width), jnp.bfloat16)],
    )
    return pl.pallas_call(
        block_kernel,
        grid_spec=grid_spec,
        out_shape=[
            jax.ShapeDtypeStruct((span, heads_here * head_dim), jnp.bfloat16),
            jax.ShapeDtypeStruct(key_cache.shape, key_cache.dtype),
            jax.ShapeDtypeStruct(value_cache.shape, value_cache.dtype),
        ],
        input_output_aliases={count + 3: 1, count + 4: 2} if in_place else {},
        compiler_params=pltpu.CompilerParams(dimension_semantics=("arbitrary",)),
    )(where, *parts, scale_blocks, qkv_weights, key_cache, value_cache)


def exit_kernel(*refs):
    where_ref = refs[0]
    count = len(refs) - 5
    part_refs = refs[1 : 1 + count]
    weights_ref, own_ref, gate_ref = refs[1 + count : 4 + count]
    out_ref = refs[4 + count]
    patch_count = where_ref[1]
    projected = sum(
        jnp.dot(
            part_refs[part][...],
            weights_ref[where_ref[2 + part]],
            preferred_element_type=jnp.float32,
        )
        for part in range(count)
    )
    updated = own_ref[...].astype(jnp.float32) + gate_ref[...] * projected
    live = lax.broadcasted_iota(jnp.int32, updated.shape, 0) < patch_count
    out_ref[...] = jnp.where(live, updated, 0.0).astype(out_ref.dtype)


def leave_block(parts, out_weights, own_rows, gating_here, where):
    count = len(parts)
    span, head_width = parts[0].shape
    vmem = pl.BlockSpec(memory_space=pltpu.VMEM)
    smem = pl.BlockSpec(memory_space=pltpu.SMEM)
    return pl.pallas_call(
        exit_kernel,
        in_specs=[smem] + [vmem] * (count + 3),
        out_specs=vmem,
        out_shape=jax.ShapeDtypeStruct(own_rows.shape, own_rows.dtype),
    )(
        where,
        *parts,
        out_weights.reshape(count, head_width, out_weights.shape[1]),
        own_rows,
        gating_here.reshape(1, -1),
    )


def shards(
    incoming_states,
    transit_states,
    patch_sizes_list,
    outdated_lookups,
    outdated_contents,
    attention_projection,
    exit_projection,
    shift_and_scale,
    branch_gates,
):
    section_index = lax.axis_index("section")
    patches = patch_sizes_list.shape[0]
    biggest_patch_span = transit_states.shape[1]
    columns = incoming_states.shape[1]
    starts = jnp.cumsum(patch_sizes_list) - patch_sizes_list
    key_cache = outdated_lookups[0]
    value_cache = outdated_contents[0]
    qkv_weights = attention_projection[0]
    out_weights = exit_projection[0]
    shift_scale = shift_and_scale[0]
    gating_here = branch_gates[0]
    row_numbers = jnp.arange(biggest_patch_span)

    results = []
    entering_ext = jnp.concatenate(
        [incoming_states, jnp.zeros((biggest_patch_span, columns), jnp.bfloat16)], axis=0
    )
    section_zero = section_index == 0
    own_rows = jnp.where(section_zero, entering_ext[:biggest_patch_span], transit_states[0])
    own_rows = jnp.where(
        (row_numbers < pick_entry(patch_sizes_list, jnp.remainder(-section_index, patches)))[:, None],
        own_rows,
        0,
    )
    row_parts = [own_rows] + across_chips(own_rows)
    for turn_number in range(patches):
        patch_index = jnp.remainder(turn_number - section_index, patches)
        patch_count = pick_entry(patch_sizes_list, patch_index)
        patch_start = pick_entry(starts, patch_index)
        where = kernel_table(patch_start, patch_count)
        head_rows, key_cache, value_cache = attend_block(
            with_partner(row_parts),
            shift_scale,
            qkv_weights,
            key_cache,
            value_cache,
            where,
            turn_number > 0,
        )
        updated = leave_block(
            with_partner([head_rows] + across_chips(head_rows)),
            out_weights,
            row_parts[0],
            gating_here,
            where,
        )
        results.append(updated)
        if turn_number + 1 < patches:
            entry_patch = lax.dynamic_slice_in_dim(
                entering_ext, starts[turn_number + 1], biggest_patch_span, 0
            )
            entry_patch = jnp.where(
                (row_numbers < patch_sizes_list[turn_number + 1])[:, None], entry_patch, 0
            )
            arrived = to_next_section(updated)
            entry_parts = [entry_patch] + across_chips_first_section(entry_patch)
            row_parts = [
                jnp.where(section_zero, entry, passed) for entry, passed in zip(entry_parts, arrived)
            ]
    return jnp.stack(results)[:, None]


def solution(mesh):
    return jax.shard_map(
        shards,
        mesh=mesh,
        in_specs=(
            P("groups", "seq"),
            P("section", "groups", "seq"),
            P("groups"),
            P("section", "seq", "groups", None),
            P("section", "seq", "groups", None),
            P("section", None, "seq"),
            P("section", None, "seq"),
            P("section", None, None),
            P("section", "seq"),
        ),
        out_specs=P(None, "section", "groups", "seq"),
        check_vma=False,
    )
```

```python
import jax
import jax.numpy as jnp
from jax import lax
from jax.experimental import pallas as pl
from jax.experimental.pallas import tpu as pltpu
from jax.sharding import PartitionSpec as P

epsilon = 1e-06


def rms_norm(values):
    return values * lax.rsqrt(jnp.mean(values * values, axis=-1, keepdims=True) + epsilon)


def pick_entry(vector, position):
    return jnp.sum(jnp.where(jnp.arange(vector.shape[0]) == position, vector, 0))


def across_chips(block):
    count = lax.axis_size("seq")
    return [
        lax.ppermute(block, "seq", [(source, (source + step) % count) for source in range(count)])
        for step in range(2, count, 2)
    ]


def across_chips_first_section(block):
    count = lax.axis_size("seq")
    return [
        lax.ppermute(
            block, ("section", "seq"), [(source, (source + step) % count) for source in range(count)]
        )
        for step in range(2, count, 2)
    ]


def with_partner(parts):
    count = lax.axis_size("seq")
    to_partner = [(source, source ^ 1) for source in range(count)]
    return parts + [lax.ppermute(part, "seq", to_partner) for part in parts]


def to_next_section(block):
    sections = lax.axis_size("section")
    count = lax.axis_size("seq")
    return [
        lax.ppermute(
            block,
            ("section", "seq"),
            [
                (section * count + source, (section + 1) * count + (source + step) % count)
                for section in range(sections - 1)
                for source in range(count)
            ],
        )
        for step in range(0, count, 2)
    ]


def kernel_table(patch_start, patch_count):
    count = lax.axis_size("seq")
    here = lax.axis_index("seq")
    chips = count // 2
    entry = jnp.arange(count + 2) - 2
    base = jnp.where(entry < chips, here, jnp.bitwise_xor(here, 1))
    sources = jnp.remainder(base - 2 * jnp.remainder(entry, chips) + count, count)
    return jnp.where(entry == -2, patch_start, jnp.where(entry == -1, patch_count, sources)).astype(
        jnp.int32
    )


def block_kernel(*refs):
    where_ref = refs[0]
    count = len(refs) - 10
    part_refs = refs[1 : 1 + count]
    scale_ref, weights_ref, keys_ref, values_ref = refs[1 + count : 5 + count]
    heads_ref, keys_out, values_out = refs[5 + count : 8 + count]
    shaped_ref, mixed_ref = refs[8 + count :]
    slot = pl.program_id(0)
    span, width = part_refs[0].shape
    heads_here, seq_len, head_dim = keys_ref.shape
    features = width * count

    @pl.when(slot == 0)
    def _():
        parts = [part[...].astype(jnp.float32) for part in part_refs]
        row_mean = sum(jnp.sum(part, axis=-1, keepdims=True) for part in parts) / features
        centred = [part - row_mean for part in parts]
        spread = sum(jnp.sum(c * c, axis=-1, keepdims=True) for c in centred) / features
        inverse = lax.rsqrt(spread + epsilon)
        for part in range(count):
            source = where_ref[2 + part]
            shift_scale = scale_ref[source]
            shaped_ref[source] = (
                (centred[part] * inverse) * (1.0 + shift_scale[1:2]) + shift_scale[0:1]
            ).astype(jnp.bfloat16)
        mixed_ref[...] = jnp.zeros_like(mixed_ref)

    mixed_ref[...] += jnp.dot(shaped_ref[slot], weights_ref[...], preferred_element_type=jnp.float32)

    @pl.when(slot == count - 1)
    def _():
        start = where_ref[0]
        patch_count = where_ref[1]
        rows = lax.broadcasted_iota(jnp.int32, (seq_len, span), 0)
        picks = lax.broadcasted_iota(jnp.int32, (seq_len, span), 1)
        placing = ((rows == picks + start) & (picks < patch_count)).astype(jnp.bfloat16)
        row_ids = lax.broadcasted_iota(jnp.int32, (seq_len, 1), 0)
        inside = (row_ids >= start) & (row_ids < start + patch_count)
        for head in range(heads_here):
            mixed = mixed_ref[:, 3 * head * head_dim : 3 * (head + 1) * head_dim]
            queries = rms_norm(mixed[:, :head_dim]).astype(jnp.bfloat16)
            fresh_keys = rms_norm(mixed[:, head_dim : 2 * head_dim]).astype(jnp.bfloat16)
            fresh_values = mixed[:, 2 * head_dim :].astype(jnp.bfloat16)
            placed_keys = jnp.dot(placing, fresh_keys, preferred_element_type=jnp.float32)
            placed_values = jnp.dot(placing, fresh_values, preferred_element_type=jnp.float32)
            keys = jnp.where(inside, placed_keys.astype(jnp.bfloat16), keys_ref[head])
            values = jnp.where(inside, placed_values.astype(jnp.bfloat16), values_ref[head])
            keys_out[head] = keys
            values_out[head] = values
            scores = lax.dot_general(
                queries, keys, (((1,), (1,)), ((), ())), preferred_element_type=jnp.float32
            ) * head_dim ** (-0.5)
            expos = jnp.exp(scores)
            weights = (expos / jnp.sum(expos, axis=-1, keepdims=True)).astype(jnp.bfloat16)
            heads_ref[:, head * head_dim : (head + 1) * head_dim] = jnp.dot(
                weights, values, preferred_element_type=jnp.float32
            ).astype(jnp.bfloat16)


def attend_block(parts, shift_scale, qkv_weights, key_cache, value_cache, where, in_place):
    count = len(parts)
    span, width = parts[0].shape
    heads_here, seq_len, head_dim = key_cache.shape
    columns = qkv_weights.shape[1]
    scale_blocks = jnp.transpose(shift_scale.reshape(2, count, width), (1, 0, 2))
    whole = lambda shape: pl.BlockSpec(shape, lambda j, where: (0,) * len(shape))
    grid_spec = pltpu.PrefetchScalarGridSpec(
        num_scalar_prefetch=1,
        grid=(count,),
        in_specs=[whole((span, width)) for _ in parts]
        + [
            whole((count, 2, width)),
            pl.BlockSpec((width, columns), lambda j, where: (j, 0)),
            whole(key_cache.shape),
            whole(value_cache.shape),
        ],
        out_specs=[
            whole((span, heads_here * head_dim)),
            whole(key_cache.shape),
            whole(value_cache.shape),
        ],
        scratch_shapes=[
            pltpu.VMEM((count, span, width), jnp.bfloat16),
            pltpu.VMEM((span, columns), jnp.float32),
        ],
    )
    return pl.pallas_call(
        block_kernel,
        grid_spec=grid_spec,
        out_shape=[
            jax.ShapeDtypeStruct((span, heads_here * head_dim), jnp.bfloat16),
            jax.ShapeDtypeStruct(key_cache.shape, key_cache.dtype),
            jax.ShapeDtypeStruct(value_cache.shape, value_cache.dtype),
        ],
        input_output_aliases={count + 3: 1, count + 4: 2} if in_place else {},
        compiler_params=pltpu.CompilerParams(dimension_semantics=("arbitrary",)),
    )(where, *parts, scale_blocks, qkv_weights, key_cache, value_cache)


def exit_kernel(*refs):
    where_ref = refs[0]
    count = len(refs) - 6
    part_refs = refs[1 : 1 + count]
    weights_ref, own_ref, gate_ref = refs[1 + count : 4 + count]
    out_ref, projected_ref = refs[4 + count :]
    step = pl.program_id(0)
    for part in range(count):

        @pl.when(step == part)
        def _():
            product = jnp.dot(part_refs[part][...], weights_ref[0], preferred_element_type=jnp.float32)
            if part == 0:
                projected_ref[...] = product
            else:
                projected_ref[...] += product

    @pl.when(step == count - 1)
    def _():
        updated = own_ref[...].astype(jnp.float32) + gate_ref[...] * projected_ref[...]
        live = lax.broadcasted_iota(jnp.int32, updated.shape, 0) < where_ref[1]
        out_ref[...] = jnp.where(live, updated, 0.0).astype(out_ref.dtype)


def leave_block(parts, out_weights, own_rows, gating_here, where):
    count = len(parts)
    span, head_width = parts[0].shape
    width = out_weights.shape[1]
    whole = lambda shape: pl.BlockSpec(shape, lambda p, where: (0,) * len(shape))
    grid_spec = pltpu.PrefetchScalarGridSpec(
        num_scalar_prefetch=1,
        grid=(count,),
        in_specs=[whole((span, head_width)) for _ in parts]
        + [
            pl.BlockSpec((1, head_width, width), lambda p, where: (where[2 + p], 0, 0)),
            whole(own_rows.shape),
            whole((1, width)),
        ],
        out_specs=whole(own_rows.shape),
        scratch_shapes=[pltpu.VMEM((span, width), jnp.float32)],
    )
    return pl.pallas_call(
        exit_kernel,
        grid_spec=grid_spec,
        out_shape=jax.ShapeDtypeStruct(own_rows.shape, own_rows.dtype),
        compiler_params=pltpu.CompilerParams(dimension_semantics=("arbitrary",)),
    )(
        where,
        *parts,
        out_weights.reshape(count, head_width, width),
        own_rows,
        gating_here.reshape(1, -1),
    )


def shards(
    incoming_states,
    transit_states,
    patch_sizes_list,
    outdated_lookups,
    outdated_contents,
    attention_projection,
    exit_projection,
    shift_and_scale,
    branch_gates,
):
    section_index = lax.axis_index("section")
    patches = patch_sizes_list.shape[0]
    biggest_patch_span = transit_states.shape[1]
    columns = incoming_states.shape[1]
    starts = jnp.cumsum(patch_sizes_list) - patch_sizes_list
    key_cache = outdated_lookups[0]
    value_cache = outdated_contents[0]
    qkv_weights = attention_projection[0]
    out_weights = exit_projection[0]
    shift_scale = shift_and_scale[0]
    gating_here = branch_gates[0]
    row_numbers = jnp.arange(biggest_patch_span)

    results = []
    entering_ext = jnp.concatenate(
        [incoming_states, jnp.zeros((biggest_patch_span, columns), jnp.bfloat16)], axis=0
    )
    section_zero = section_index == 0
    own_rows = jnp.where(section_zero, entering_ext[:biggest_patch_span], transit_states[0])
    own_rows = jnp.where(
        (row_numbers < pick_entry(patch_sizes_list, jnp.remainder(-section_index, patches)))[:, None],
        own_rows,
        0,
    )
    row_parts = [own_rows] + across_chips(own_rows)
    for turn_number in range(patches):
        patch_index = jnp.remainder(turn_number - section_index, patches)
        patch_count = pick_entry(patch_sizes_list, patch_index)
        patch_start = pick_entry(starts, patch_index)
        where = kernel_table(patch_start, patch_count)
        head_rows, key_cache, value_cache = attend_block(
            with_partner(row_parts),
            shift_scale,
            qkv_weights,
            key_cache,
            value_cache,
            where,
            turn_number > 0,
        )
        updated = leave_block(
            with_partner([head_rows] + across_chips(head_rows)),
            out_weights,
            row_parts[0],
            gating_here,
            where,
        )
        results.append(updated)
        if turn_number + 1 < patches:
            entry_patch = lax.dynamic_slice_in_dim(
                entering_ext, starts[turn_number + 1], biggest_patch_span, 0
            )
            entry_patch = jnp.where(
                (row_numbers < patch_sizes_list[turn_number + 1])[:, None], entry_patch, 0
            )
            arrived = to_next_section(updated)
            entry_parts = [entry_patch] + across_chips_first_section(entry_patch)
            row_parts = [
                jnp.where(section_zero, entry, passed) for entry, passed in zip(entry_parts, arrived)
            ]
    return jnp.stack(results)[:, None]


def solution(mesh):
    return jax.shard_map(
        shards,
        mesh=mesh,
        in_specs=(
            P("groups", "seq"),
            P("section", "groups", "seq"),
            P("groups"),
            P("section", "seq", "groups", None),
            P("section", "seq", "groups", None),
            P("section", None, "seq"),
            P("section", None, "seq"),
            P("section", None, None),
            P("section", "seq"),
        ),
        out_specs=P(None, "section", "groups", "seq"),
        check_vma=False,
    )
```

```python
import jax
import jax.numpy as jnp
from jax import lax
from jax.experimental import pallas as pl
from jax.experimental.pallas import tpu as pltpu
from jax.sharding import PartitionSpec as P

epsilon = 1e-06


def rms_norm(values):
    return values * lax.rsqrt(jnp.mean(values * values, axis=-1, keepdims=True) + epsilon)


def pick_entry(vector, position):
    return jnp.sum(jnp.where(jnp.arange(vector.shape[0]) == position, vector, 0))


def across_chips(block):
    count = lax.axis_size("seq")
    return [
        lax.ppermute(block, "seq", [(source, (source + step) % count) for source in range(count)])
        for step in range(2, count, 2)
    ]


def across_chips_first_section(block):
    count = lax.axis_size("seq")
    return [
        lax.ppermute(
            block, ("section", "seq"), [(source, (source + step) % count) for source in range(count)]
        )
        for step in range(2, count, 2)
    ]


def with_partner(parts):
    count = lax.axis_size("seq")
    to_partner = [(source, source ^ 1) for source in range(count)]
    return parts + [lax.ppermute(part, "seq", to_partner) for part in parts]


def to_next_section(block):
    sections = lax.axis_size("section")
    count = lax.axis_size("seq")
    return [
        lax.ppermute(
            block,
            ("section", "seq"),
            [
                (section * count + source, (section + 1) * count + (source + step) % count)
                for section in range(sections - 1)
                for source in range(count)
            ],
        )
        for step in range(0, count, 2)
    ]


def kernel_tables(patch_sizes_list, section_index):
    patches = patch_sizes_list.shape[0]
    count = lax.axis_size("seq")
    here = lax.axis_index("seq")
    chips = count // 2
    turn = lax.broadcasted_iota(jnp.int32, (patches, count + 2), 0)
    entry = lax.broadcasted_iota(jnp.int32, (patches, count + 2), 1) - 2
    patch_index = jnp.remainder(turn - section_index + patches, patches)
    patch_ids = jnp.arange(patches).reshape(1, 1, patches)
    sizes = patch_sizes_list.reshape(1, 1, patches)
    chosen = patch_ids == patch_index[:, :, None]
    patch_count = jnp.sum(jnp.where(chosen, sizes, 0), axis=-1)
    patch_start = jnp.sum(jnp.where(patch_ids < patch_index[:, :, None], sizes, 0), axis=-1)
    base = jnp.where(entry < chips, here, jnp.bitwise_xor(here, 1))
    sources = jnp.remainder(base - 2 * jnp.remainder(entry, chips) + count, count)
    return jnp.where(entry == -2, patch_start, jnp.where(entry == -1, patch_count, sources)).astype(
        jnp.int32
    )


def block_kernel(*refs):
    where_ref = refs[0]
    count = len(refs) - 9
    part_refs = refs[1 : 1 + count]
    scale_ref, weights_ref, keys_ref, values_ref = refs[1 + count : 5 + count]
    heads_ref, keys_out, values_out = refs[5 + count : 8 + count]
    shaped_ref = refs[8 + count]
    start = where_ref[0]
    patch_count = where_ref[1]
    head_dim = keys_ref.shape[2]
    seq_len = keys_ref.shape[1]
    span, width = part_refs[0].shape
    features = width * count

    @pl.when(pl.program_id(0) == 0)
    def _():
        parts = [part[...].astype(jnp.float32) for part in part_refs]
        row_mean = sum(jnp.sum(part, axis=-1, keepdims=True) for part in parts) / features
        centred = [part - row_mean for part in parts]
        spread = sum(jnp.sum(c * c, axis=-1, keepdims=True) for c in centred) / features
        inverse = lax.rsqrt(spread + epsilon)
        for part in range(count):
            slot = where_ref[2 + part]
            shift_scale = scale_ref[slot]
            shaped_ref[slot] = (
                (centred[part] * inverse) * (1.0 + shift_scale[1:2]) + shift_scale[0:1]
            ).astype(jnp.bfloat16)

    mixed = sum(
        jnp.dot(
            shaped_ref[slot],
            weights_ref[slot * width : (slot + 1) * width, :],
            preferred_element_type=jnp.float32,
        )
        for slot in range(count)
    )
    queries = rms_norm(mixed[:, :head_dim]).astype(jnp.bfloat16)
    fresh_keys = rms_norm(mixed[:, head_dim : 2 * head_dim]).astype(jnp.bfloat16)
    fresh_values = mixed[:, 2 * head_dim :].astype(jnp.bfloat16)
    rows = lax.broadcasted_iota(jnp.int32, (seq_len, span), 0)
    picks = lax.broadcasted_iota(jnp.int32, (seq_len, span), 1)
    placing = ((rows == picks + start) & (picks < patch_count)).astype(jnp.bfloat16)
    row_ids = lax.broadcasted_iota(jnp.int32, (seq_len, 1), 0)
    inside = (row_ids >= start) & (row_ids < start + patch_count)
    placed_keys = jnp.dot(placing, fresh_keys, preferred_element_type=jnp.float32)
    placed_values = jnp.dot(placing, fresh_values, preferred_element_type=jnp.float32)
    keys = jnp.where(inside, placed_keys.astype(jnp.bfloat16), keys_ref[0])
    values = jnp.where(inside, placed_values.astype(jnp.bfloat16), values_ref[0])
    keys_out[0] = keys
    values_out[0] = values
    scores = lax.dot_general(
        queries, keys, (((1,), (1,)), ((), ())), preferred_element_type=jnp.float32
    ) * head_dim ** (-0.5)
    expos = jnp.exp(scores)
    weights = (expos / jnp.sum(expos, axis=-1, keepdims=True)).astype(jnp.bfloat16)
    heads_ref[...] = jnp.dot(weights, values, preferred_element_type=jnp.float32).astype(
        jnp.bfloat16
    )


def attend_block(parts, shift_scale, qkv_weights, key_cache, value_cache, where, in_place):
    count = len(parts)
    span, width = parts[0].shape
    heads_here, seq_len, head_dim = key_cache.shape
    features = qkv_weights.shape[0]
    scale_blocks = jnp.transpose(shift_scale.reshape(2, count, width), (1, 0, 2))
    whole = lambda shape: pl.BlockSpec(shape, lambda h, where: (0,) * len(shape))
    cache_spec = pl.BlockSpec((1, seq_len, head_dim), lambda h, where: (h, 0, 0))
    grid_spec = pltpu.PrefetchScalarGridSpec(
        num_scalar_prefetch=1,
        grid=(heads_here,),
        in_specs=[whole((span, width)) for _ in parts]
        + [
            whole((count, 2, width)),
            pl.BlockSpec((features, 3 * head_dim), lambda h, where: (0, h)),
            cache_spec,
            cache_spec,
        ],
        out_specs=[
            pl.BlockSpec((span, head_dim), lambda h, where: (0, h)),
            cache_spec,
            cache_spec,
        ],
        scratch_shapes=[pltpu.VMEM((count, span, width), jnp.bfloat16)],
    )
    return pl.pallas_call(
        block_kernel,
        grid_spec=grid_spec,
        out_shape=[
            jax.ShapeDtypeStruct((span, heads_here * head_dim), jnp.bfloat16),
            jax.ShapeDtypeStruct(key_cache.shape, key_cache.dtype),
            jax.ShapeDtypeStruct(value_cache.shape, value_cache.dtype),
        ],
        input_output_aliases={count + 3: 1, count + 4: 2} if in_place else {},
        compiler_params=pltpu.CompilerParams(dimension_semantics=("arbitrary",)),
    )(where, *parts, scale_blocks, qkv_weights, key_cache, value_cache)


def exit_kernel(*refs):
    where_ref = refs[0]
    count = len(refs) - 5
    part_refs = refs[1 : 1 + count]
    weights_ref, own_ref, gate_ref = refs[1 + count : 4 + count]
    out_ref = refs[4 + count]
    patch_count = where_ref[1]
    projected = sum(
        jnp.dot(
            part_refs[part][...],
            weights_ref[where_ref[2 + part]],
            preferred_element_type=jnp.float32,
        )
        for part in range(count)
    )
    updated = own_ref[...].astype(jnp.float32) + gate_ref[...] * projected
    live = lax.broadcasted_iota(jnp.int32, updated.shape, 0) < patch_count
    out_ref[...] = jnp.where(live, updated, 0.0).astype(out_ref.dtype)


def leave_block(parts, out_weights, own_rows, gating_here, where):
    count = len(parts)
    span, head_width = parts[0].shape
    vmem = pl.BlockSpec(memory_space=pltpu.VMEM)
    smem = pl.BlockSpec(memory_space=pltpu.SMEM)
    return pl.pallas_call(
        exit_kernel,
        in_specs=[smem] + [vmem] * (count + 3),
        out_specs=vmem,
        out_shape=jax.ShapeDtypeStruct(own_rows.shape, own_rows.dtype),
    )(
        where,
        *parts,
        out_weights.reshape(count, head_width, out_weights.shape[1]),
        own_rows,
        gating_here.reshape(1, -1),
    )


def shards(
    incoming_states,
    transit_states,
    patch_sizes_list,
    outdated_lookups,
    outdated_contents,
    attention_projection,
    exit_projection,
    shift_and_scale,
    branch_gates,
):
    section_index = lax.axis_index("section")
    patches = patch_sizes_list.shape[0]
    biggest_patch_span = transit_states.shape[1]
    columns = incoming_states.shape[1]
    starts = jnp.cumsum(patch_sizes_list) - patch_sizes_list
    key_cache = outdated_lookups[0]
    value_cache = outdated_contents[0]
    qkv_weights = attention_projection[0]
    out_weights = exit_projection[0]
    shift_scale = shift_and_scale[0]
    gating_here = branch_gates[0]
    row_numbers = jnp.arange(biggest_patch_span)

    results = []
    entering_ext = jnp.concatenate(
        [incoming_states, jnp.zeros((biggest_patch_span, columns), jnp.bfloat16)], axis=0
    )
    section_zero = section_index == 0
    own_rows = jnp.where(section_zero, entering_ext[:biggest_patch_span], transit_states[0])
    own_rows = jnp.where(
        (row_numbers < pick_entry(patch_sizes_list, jnp.remainder(-section_index, patches)))[:, None],
        own_rows,
        0,
    )
    tables, own_rows = lax.optimization_barrier(
        (kernel_tables(patch_sizes_list, section_index), own_rows)
    )
    row_parts = [own_rows] + across_chips(own_rows)
    for turn_number in range(patches):
        where = tables[turn_number]
        head_rows, key_cache, value_cache = attend_block(
            with_partner(row_parts),
            shift_scale,
            qkv_weights,
            key_cache,
            value_cache,
            where,
            turn_number > 0,
        )
        updated = leave_block(
            with_partner([head_rows] + across_chips(head_rows)),
            out_weights,
            row_parts[0],
            gating_here,
            where,
        )
        results.append(updated)
        if turn_number + 1 < patches:
            entry_patch = lax.dynamic_slice_in_dim(
                entering_ext, starts[turn_number + 1], biggest_patch_span, 0
            )
            entry_patch = jnp.where(
                (row_numbers < patch_sizes_list[turn_number + 1])[:, None], entry_patch, 0
            )
            arrived = to_next_section(updated)
            entry_parts = [entry_patch] + across_chips_first_section(entry_patch)
            row_parts = [
                jnp.where(section_zero, entry, passed) for entry, passed in zip(entry_parts, arrived)
            ]
    return jnp.stack(results)[:, None]


def solution(mesh):
    return jax.shard_map(
        shards,
        mesh=mesh,
        in_specs=(
            P("groups", "seq"),
            P("section", "groups", "seq"),
            P("groups"),
            P("section", "seq", "groups", None),
            P("section", "seq", "groups", None),
            P("section", None, "seq"),
            P("section", None, "seq"),
            P("section", None, None),
            P("section", "seq"),
        ),
        out_specs=P(None, "section", "groups", "seq"),
        check_vma=False,
    )
```

```python
import jax
import jax.numpy as jnp
from jax import lax
from jax.experimental import pallas as pl
from jax.experimental.pallas import tpu as pltpu
from jax.sharding import PartitionSpec as P

epsilon = 1e-06


def rms_norm(values):
    return values * lax.rsqrt(jnp.mean(values * values, axis=-1, keepdims=True) + epsilon)


def pick_entry(vector, position):
    return jnp.sum(jnp.where(jnp.arange(vector.shape[0]) == position, vector, 0))


def across_chips(block):
    count = lax.axis_size("seq")
    return [
        lax.ppermute(block, "seq", [(source, (source + step) % count) for source in range(count)])
        for step in range(2, count, 2)
    ]


def with_partner(parts):
    count = lax.axis_size("seq")
    to_partner = [(source, source ^ 1) for source in range(count)]
    return parts + [lax.ppermute(part, "seq", to_partner) for part in parts]


def to_next_section(block, entry_block):
    sections = lax.axis_size("section")
    count = lax.axis_size("seq")
    last = lax.axis_index("section") == sections - 1
    payload = jnp.where(last, entry_block, block)
    arrived = []
    for step in range(0, count, 2):
        pairs = [
            (section * count + source, (section + 1) % sections * count + (source + step) % count)
            for section in range(sections - (1 if step == 0 else 0))
            for source in range(count)
        ]
        arrived.append(lax.ppermute(block if step == 0 else payload, ("section", "seq"), pairs))
    return arrived


def kernel_tables(patch_sizes_list, section_index):
    patches = patch_sizes_list.shape[0]
    count = lax.axis_size("seq")
    here = lax.axis_index("seq")
    chips = count // 2
    turn = lax.broadcasted_iota(jnp.int32, (patches, count + 2), 0)
    entry = lax.broadcasted_iota(jnp.int32, (patches, count + 2), 1) - 2
    patch_index = jnp.remainder(turn - section_index + patches, patches)
    patch_ids = jnp.arange(patches).reshape(1, 1, patches)
    sizes = patch_sizes_list.reshape(1, 1, patches)
    chosen = patch_ids == patch_index[:, :, None]
    patch_count = jnp.sum(jnp.where(chosen, sizes, 0), axis=-1)
    patch_start = jnp.sum(jnp.where(patch_ids < patch_index[:, :, None], sizes, 0), axis=-1)
    base = jnp.where(entry < chips, here, jnp.bitwise_xor(here, 1))
    sources = jnp.remainder(base - 2 * jnp.remainder(entry, chips) + count, count)
    return jnp.where(entry == -2, patch_start, jnp.where(entry == -1, patch_count, sources)).astype(
        jnp.int32
    )


def block_kernel(*refs):
    where_ref = refs[0]
    count = len(refs) - 9
    part_refs = refs[1 : 1 + count]
    scale_ref, weights_ref, keys_ref, values_ref = refs[1 + count : 5 + count]
    heads_ref, keys_out, values_out = refs[5 + count : 8 + count]
    shaped_ref = refs[8 + count]
    start = where_ref[0]
    patch_count = where_ref[1]
    head_dim = keys_ref.shape[2]
    seq_len = keys_ref.shape[1]
    span, width = part_refs[0].shape
    features = width * count

    @pl.when(pl.program_id(0) == 0)
    def _():
        parts = [part[...].astype(jnp.float32) for part in part_refs]
        row_mean = sum(jnp.sum(part, axis=-1, keepdims=True) for part in parts) / features
        centred = [part - row_mean for part in parts]
        spread = sum(jnp.sum(c * c, axis=-1, keepdims=True) for c in centred) / features
        inverse = lax.rsqrt(spread + epsilon)
        for part in range(count):
            slot = where_ref[2 + part]
            shift_scale = scale_ref[slot]
            shaped_ref[slot] = (
                (centred[part] * inverse) * (1.0 + shift_scale[1:2]) + shift_scale[0:1]
            ).astype(jnp.bfloat16)

    mixed = sum(
        jnp.dot(
            shaped_ref[slot],
            weights_ref[slot * width : (slot + 1) * width, :],
            preferred_element_type=jnp.float32,
        )
        for slot in range(count)
    )
    queries = rms_norm(mixed[:, :head_dim]).astype(jnp.bfloat16)
    fresh_keys = rms_norm(mixed[:, head_dim : 2 * head_dim]).astype(jnp.bfloat16)
    fresh_values = mixed[:, 2 * head_dim :].astype(jnp.bfloat16)
    rows = lax.broadcasted_iota(jnp.int32, (seq_len, span), 0)
    picks = lax.broadcasted_iota(jnp.int32, (seq_len, span), 1)
    placing = ((rows == picks + start) & (picks < patch_count)).astype(jnp.bfloat16)
    row_ids = lax.broadcasted_iota(jnp.int32, (seq_len, 1), 0)
    inside = (row_ids >= start) & (row_ids < start + patch_count)
    placed_keys = jnp.dot(placing, fresh_keys, preferred_element_type=jnp.float32)
    placed_values = jnp.dot(placing, fresh_values, preferred_element_type=jnp.float32)
    keys = jnp.where(inside, placed_keys.astype(jnp.bfloat16), keys_ref[0])
    values = jnp.where(inside, placed_values.astype(jnp.bfloat16), values_ref[0])
    keys_out[0] = keys
    values_out[0] = values
    scores = lax.dot_general(
        queries, keys, (((1,), (1,)), ((), ())), preferred_element_type=jnp.float32
    ) * head_dim ** (-0.5)
    expos = jnp.exp(scores)
    weights = (expos / jnp.sum(expos, axis=-1, keepdims=True)).astype(jnp.bfloat16)
    heads_ref[...] = jnp.dot(weights, values, preferred_element_type=jnp.float32).astype(
        jnp.bfloat16
    )


def attend_block(parts, shift_scale, qkv_weights, key_cache, value_cache, where, in_place):
    count = len(parts)
    span, width = parts[0].shape
    heads_here, seq_len, head_dim = key_cache.shape
    features = qkv_weights.shape[0]
    scale_blocks = jnp.transpose(shift_scale.reshape(2, count, width), (1, 0, 2))
    whole = lambda shape: pl.BlockSpec(shape, lambda h, where: (0,) * len(shape))
    cache_spec = pl.BlockSpec((1, seq_len, head_dim), lambda h, where: (h, 0, 0))
    grid_spec = pltpu.PrefetchScalarGridSpec(
        num_scalar_prefetch=1,
        grid=(heads_here,),
        in_specs=[whole((span, width)) for _ in parts]
        + [
            whole((count, 2, width)),
            pl.BlockSpec((features, 3 * head_dim), lambda h, where: (0, h)),
            cache_spec,
            cache_spec,
        ],
        out_specs=[
            pl.BlockSpec((span, head_dim), lambda h, where: (0, h)),
            cache_spec,
            cache_spec,
        ],
        scratch_shapes=[pltpu.VMEM((count, span, width), jnp.bfloat16)],
    )
    return pl.pallas_call(
        block_kernel,
        grid_spec=grid_spec,
        out_shape=[
            jax.ShapeDtypeStruct((span, heads_here * head_dim), jnp.bfloat16),
            jax.ShapeDtypeStruct(key_cache.shape, key_cache.dtype),
            jax.ShapeDtypeStruct(value_cache.shape, value_cache.dtype),
        ],
        input_output_aliases={count + 3: 1, count + 4: 2} if in_place else {},
        compiler_params=pltpu.CompilerParams(dimension_semantics=("arbitrary",)),
    )(where, *parts, scale_blocks, qkv_weights, key_cache, value_cache)


def exit_kernel(*refs):
    where_ref = refs[0]
    count = len(refs) - 5
    part_refs = refs[1 : 1 + count]
    weights_ref, own_ref, gate_ref = refs[1 + count : 4 + count]
    out_ref = refs[4 + count]
    patch_count = where_ref[1]
    projected = sum(
        jnp.dot(
            part_refs[part][...],
            weights_ref[where_ref[2 + part]],
            preferred_element_type=jnp.float32,
        )
        for part in range(count)
    )
    updated = own_ref[...].astype(jnp.float32) + gate_ref[...] * projected
    live = lax.broadcasted_iota(jnp.int32, updated.shape, 0) < patch_count
    out_ref[...] = jnp.where(live, updated, 0.0).astype(out_ref.dtype)


def leave_block(parts, out_weights, own_rows, gating_here, where):
    count = len(parts)
    span, head_width = parts[0].shape
    vmem = pl.BlockSpec(memory_space=pltpu.VMEM)
    smem = pl.BlockSpec(memory_space=pltpu.SMEM)
    return pl.pallas_call(
        exit_kernel,
        in_specs=[smem] + [vmem] * (count + 3),
        out_specs=vmem,
        out_shape=jax.ShapeDtypeStruct(own_rows.shape, own_rows.dtype),
    )(
        where,
        *parts,
        out_weights.reshape(count, head_width, out_weights.shape[1]),
        own_rows,
        gating_here.reshape(1, -1),
    )


def shards(
    incoming_states,
    transit_states,
    patch_sizes_list,
    outdated_lookups,
    outdated_contents,
    attention_projection,
    exit_projection,
    shift_and_scale,
    branch_gates,
):
    section_index = lax.axis_index("section")
    patches = patch_sizes_list.shape[0]
    biggest_patch_span = transit_states.shape[1]
    columns = incoming_states.shape[1]
    starts = jnp.cumsum(patch_sizes_list) - patch_sizes_list
    key_cache = outdated_lookups[0]
    value_cache = outdated_contents[0]
    qkv_weights = attention_projection[0]
    out_weights = exit_projection[0]
    shift_scale = shift_and_scale[0]
    gating_here = branch_gates[0]
    row_numbers = jnp.arange(biggest_patch_span)

    results = []
    entering_ext = jnp.concatenate(
        [incoming_states, jnp.zeros((biggest_patch_span, columns), jnp.bfloat16)], axis=0
    )
    section_zero = section_index == 0
    own_rows = jnp.where(section_zero, entering_ext[:biggest_patch_span], transit_states[0])
    own_rows = jnp.where(
        (row_numbers < pick_entry(patch_sizes_list, jnp.remainder(-section_index, patches)))[:, None],
        own_rows,
        0,
    )
    tables, own_rows = lax.optimization_barrier(
        (kernel_tables(patch_sizes_list, section_index), own_rows)
    )
    row_parts = [own_rows] + across_chips(own_rows)
    for turn_number in range(patches):
        where = tables[turn_number]
        head_rows, key_cache, value_cache = attend_block(
            with_partner(row_parts),
            shift_scale,
            qkv_weights,
            key_cache,
            value_cache,
            where,
            turn_number > 0,
        )
        updated = leave_block(
            with_partner([head_rows] + across_chips(head_rows)),
            out_weights,
            row_parts[0],
            gating_here,
            where,
        )
        results.append(updated)
        if turn_number + 1 < patches:
            entry_patch = lax.dynamic_slice_in_dim(
                entering_ext, starts[turn_number + 1], biggest_patch_span, 0
            )
            entry_patch = jnp.where(
                (row_numbers < patch_sizes_list[turn_number + 1])[:, None], entry_patch, 0
            )
            arrived = to_next_section(updated, entry_patch)
            row_parts = [jnp.where(section_zero, entry_patch, arrived[0])] + arrived[1:]
    return jnp.stack(results)[:, None]


def solution(mesh):
    return jax.shard_map(
        shards,
        mesh=mesh,
        in_specs=(
            P("groups", "seq"),
            P("section", "groups", "seq"),
            P("groups"),
            P("section", "seq", "groups", None),
            P("section", "seq", "groups", None),
            P("section", None, "seq"),
            P("section", None, "seq"),
            P("section", None, None),
            P("section", "seq"),
        ),
        out_specs=P(None, "section", "groups", "seq"),
        check_vma=False,
    )
```

```python
import jax
import jax.numpy as jnp
from jax import lax
from jax.experimental import pallas as pl
from jax.experimental.pallas import tpu as pltpu
from jax.sharding import PartitionSpec as P

epsilon = 1e-06


def passed_along(value, axis, steps):
    count = lax.axis_size(axis)
    leading, last = (max(0, -steps), min(count, count - steps))
    return lax.ppermute(value, axis, [(source, source + steps) for source in range(leading, last)])


def rms_norm(values):
    return values * lax.rsqrt(jnp.mean(values * values, axis=-1, keepdims=True) + epsilon)


def pick_entry(vector, position):
    return jnp.sum(jnp.where(jnp.arange(vector.shape[0]) == position, vector, 0))


def spread_over_seq(block):
    count = lax.axis_size("seq")
    to_partner = [(source, source ^ 1) for source in range(count)]
    across = [
        lax.ppermute(block, "seq", [(source, (source + step) % count) for source in range(count)])
        for step in range(2, count, 2)
    ]
    from_partner = lax.ppermute(block, "seq", to_partner)
    relayed = [lax.ppermute(part, "seq", to_partner) for part in across]
    return [block] + across + [from_partner] + relayed


def kernel_tables(patch_sizes_list, section_index):
    patches = patch_sizes_list.shape[0]
    count = lax.axis_size("seq")
    here = lax.axis_index("seq")
    chips = count // 2
    turn = lax.broadcasted_iota(jnp.int32, (patches, count + 2), 0)
    entry = lax.broadcasted_iota(jnp.int32, (patches, count + 2), 1) - 2
    patch_index = jnp.remainder(turn - section_index + patches, patches)
    patch_ids = jnp.arange(patches).reshape(1, 1, patches)
    sizes = patch_sizes_list.reshape(1, 1, patches)
    chosen = patch_ids == patch_index[:, :, None]
    patch_count = jnp.sum(jnp.where(chosen, sizes, 0), axis=-1)
    patch_start = jnp.sum(jnp.where(patch_ids < patch_index[:, :, None], sizes, 0), axis=-1)
    base = jnp.where(entry < chips, here, jnp.bitwise_xor(here, 1))
    sources = jnp.remainder(base - 2 * jnp.remainder(entry, chips) + count, count)
    return jnp.where(entry == -2, patch_start, jnp.where(entry == -1, patch_count, sources)).astype(
        jnp.int32
    )


def block_kernel(*refs):
    where_ref = refs[0]
    count = len(refs) - 9
    part_refs = refs[1 : 1 + count]
    scale_ref, weights_ref, keys_ref, values_ref = refs[1 + count : 5 + count]
    heads_ref, keys_out, values_out = refs[5 + count : 8 + count]
    shaped_ref = refs[8 + count]
    start = where_ref[0]
    patch_count = where_ref[1]
    head_dim = keys_ref.shape[2]
    seq_len = keys_ref.shape[1]
    span, width = part_refs[0].shape
    features = width * count

    @pl.when(pl.program_id(0) == 0)
    def _():
        parts = [part[...].astype(jnp.float32) for part in part_refs]
        row_mean = sum(jnp.sum(part, axis=-1, keepdims=True) for part in parts) / features
        centred = [part - row_mean for part in parts]
        spread = sum(jnp.sum(c * c, axis=-1, keepdims=True) for c in centred) / features
        inverse = lax.rsqrt(spread + epsilon)
        for part in range(count):
            slot = where_ref[2 + part]
            shift_scale = scale_ref[slot]
            shaped_ref[slot] = (
                (centred[part] * inverse) * (1.0 + shift_scale[1:2]) + shift_scale[0:1]
            ).astype(jnp.bfloat16)

    mixed = sum(
        jnp.dot(
            shaped_ref[slot],
            weights_ref[slot * width : (slot + 1) * width, :],
            preferred_element_type=jnp.float32,
        )
        for slot in range(count)
    )
    queries = rms_norm(mixed[:, :head_dim]).astype(jnp.bfloat16)
    fresh_keys = rms_norm(mixed[:, head_dim : 2 * head_dim]).astype(jnp.bfloat16)
    fresh_values = mixed[:, 2 * head_dim :].astype(jnp.bfloat16)
    rows = lax.broadcasted_iota(jnp.int32, (seq_len, span), 0)
    picks = lax.broadcasted_iota(jnp.int32, (seq_len, span), 1)
    placing = ((rows == picks + start) & (picks < patch_count)).astype(jnp.bfloat16)
    row_ids = lax.broadcasted_iota(jnp.int32, (seq_len, 1), 0)
    inside = (row_ids >= start) & (row_ids < start + patch_count)
    placed_keys = jnp.dot(placing, fresh_keys, preferred_element_type=jnp.float32)
    placed_values = jnp.dot(placing, fresh_values, preferred_element_type=jnp.float32)
    keys = jnp.where(inside, placed_keys.astype(jnp.bfloat16), keys_ref[0])
    values = jnp.where(inside, placed_values.astype(jnp.bfloat16), values_ref[0])
    keys_out[0] = keys
    values_out[0] = values
    scores = lax.dot_general(
        queries, keys, (((1,), (1,)), ((), ())), preferred_element_type=jnp.float32
    ) * head_dim ** (-0.5)
    expos = jnp.exp(scores)
    weights = (expos / jnp.sum(expos, axis=-1, keepdims=True)).astype(jnp.bfloat16)
    heads_ref[...] = jnp.dot(weights, values, preferred_element_type=jnp.float32).astype(
        jnp.bfloat16
    )


def attend_block(parts, shift_scale, qkv_weights, key_cache, value_cache, where, in_place):
    count = len(parts)
    span, width = parts[0].shape
    heads_here, seq_len, head_dim = key_cache.shape
    features = qkv_weights.shape[0]
    scale_blocks = jnp.transpose(shift_scale.reshape(2, count, width), (1, 0, 2))
    whole = lambda shape: pl.BlockSpec(shape, lambda h, where: (0,) * len(shape))
    cache_spec = pl.BlockSpec((1, seq_len, head_dim), lambda h, where: (h, 0, 0))
    grid_spec = pltpu.PrefetchScalarGridSpec(
        num_scalar_prefetch=1,
        grid=(heads_here,),
        in_specs=[whole((span, width)) for _ in parts]
        + [
            whole((count, 2, width)),
            pl.BlockSpec((features, 3 * head_dim), lambda h, where: (0, h)),
            cache_spec,
            cache_spec,
        ],
        out_specs=[
            pl.BlockSpec((span, head_dim), lambda h, where: (0, h)),
            cache_spec,
            cache_spec,
        ],
        scratch_shapes=[pltpu.VMEM((count, span, width), jnp.bfloat16)],
    )
    return pl.pallas_call(
        block_kernel,
        grid_spec=grid_spec,
        out_shape=[
            jax.ShapeDtypeStruct((span, heads_here * head_dim), jnp.bfloat16),
            jax.ShapeDtypeStruct(key_cache.shape, key_cache.dtype),
            jax.ShapeDtypeStruct(value_cache.shape, value_cache.dtype),
        ],
        input_output_aliases={count + 3: 1, count + 4: 2} if in_place else {},
        compiler_params=pltpu.CompilerParams(dimension_semantics=("arbitrary",)),
    )(where, *parts, scale_blocks, qkv_weights, key_cache, value_cache)


def exit_kernel(*refs):
    where_ref = refs[0]
    count = len(refs) - 5
    part_refs = refs[1 : 1 + count]
    weights_ref, own_ref, gate_ref = refs[1 + count : 4 + count]
    out_ref = refs[4 + count]
    patch_count = where_ref[1]
    projected = sum(
        jnp.dot(
            part_refs[part][...],
            weights_ref[where_ref[2 + part]],
            preferred_element_type=jnp.float32,
        )
        for part in range(count)
    )
    updated = own_ref[...].astype(jnp.float32) + gate_ref[...] * projected
    live = lax.broadcasted_iota(jnp.int32, updated.shape, 0) < patch_count
    out_ref[...] = jnp.where(live, updated, 0.0).astype(out_ref.dtype)


def leave_block(parts, out_weights, own_rows, gating_here, where):
    count = len(parts)
    span, head_width = parts[0].shape
    vmem = pl.BlockSpec(memory_space=pltpu.VMEM)
    smem = pl.BlockSpec(memory_space=pltpu.SMEM)
    return pl.pallas_call(
        exit_kernel,
        in_specs=[smem] + [vmem] * (count + 3),
        out_specs=vmem,
        out_shape=jax.ShapeDtypeStruct(own_rows.shape, own_rows.dtype),
    )(
        where,
        *parts,
        out_weights.reshape(count, head_width, out_weights.shape[1]),
        own_rows,
        gating_here.reshape(1, -1),
    )


def shards(
    incoming_states,
    transit_states,
    patch_sizes_list,
    outdated_lookups,
    outdated_contents,
    attention_projection,
    exit_projection,
    shift_and_scale,
    branch_gates,
):
    section_index = lax.axis_index("section")
    patches = patch_sizes_list.shape[0]
    biggest_patch_span = transit_states.shape[1]
    columns = incoming_states.shape[1]
    starts = jnp.cumsum(patch_sizes_list) - patch_sizes_list
    key_cache = outdated_lookups[0]
    value_cache = outdated_contents[0]
    qkv_weights = attention_projection[0]
    out_weights = exit_projection[0]
    shift_scale = shift_and_scale[0]
    gating_here = branch_gates[0]
    row_numbers = jnp.arange(biggest_patch_span)

    results = []
    entering_ext = jnp.concatenate(
        [incoming_states, jnp.zeros((biggest_patch_span, columns), jnp.bfloat16)], axis=0
    )
    earlier_result = transit_states[0]
    tables = kernel_tables(patch_sizes_list, section_index)
    for turn_number in range(patches):
        patch_index = jnp.remainder(turn_number - section_index, patches)
        patch_count = pick_entry(patch_sizes_list, patch_index)
        live_rows = row_numbers < patch_count
        entry_patch = lax.dynamic_slice_in_dim(
            entering_ext, starts[turn_number], biggest_patch_span, 0
        )
        own_rows = jnp.where(section_index == 0, entry_patch, earlier_result)
        own_rows = jnp.where(live_rows[:, None], own_rows, jnp.zeros_like(own_rows))
        if turn_number == 0:
            tables, own_rows = lax.optimization_barrier((tables, own_rows))
        where = tables[turn_number]
        head_rows, key_cache, value_cache = attend_block(
            spread_over_seq(own_rows),
            shift_scale,
            qkv_weights,
            key_cache,
            value_cache,
            where,
            turn_number > 0,
        )
        updated = leave_block(
            spread_over_seq(head_rows), out_weights, own_rows, gating_here, where
        )
        results.append(updated)
        if turn_number + 1 < patches:
            earlier_result = passed_along(updated, "section", 1)
    return jnp.stack(results)[:, None]


def solution(mesh):
    return jax.shard_map(
        shards,
        mesh=mesh,
        in_specs=(
            P("groups", "seq"),
            P("section", "groups", "seq"),
            P("groups"),
            P("section", "seq", "groups", None),
            P("section", "seq", "groups", None),
            P("section", None, "seq"),
            P("section", None, "seq"),
            P("section", None, None),
            P("section", "seq"),
        ),
        out_specs=P(None, "section", "groups", "seq"),
        check_vma=False,
    )
```

```python
import functools

import jax
import jax.numpy as jnp
from jax import lax
from jax.experimental import pallas as pl
from jax.experimental.pallas import tpu as pltpu
from jax.sharding import PartitionSpec as P

epsilon = 1e-06


def rms_norm(values):
    return values * lax.rsqrt(jnp.mean(values * values, axis=-1, keepdims=True) + epsilon)


def pick_entry(vector, position):
    return jnp.sum(jnp.where(jnp.arange(vector.shape[0]) == position, vector, 0))


def across_chips(block):
    count = lax.axis_size("seq")
    return [
        lax.ppermute(block, "seq", [(source, (source + step) % count) for source in range(count)])
        for step in range(2, count, 2)
    ]


def across_chips_first_section(block):
    count = lax.axis_size("seq")
    return [
        lax.ppermute(
            block, ("section", "seq"), [(source, (source + step) % count) for source in range(count)]
        )
        for step in range(2, count, 2)
    ]


def with_partner(parts):
    count = lax.axis_size("seq")
    to_partner = [(source, source ^ 1) for source in range(count)]
    return parts + [lax.ppermute(part, "seq", to_partner) for part in parts]


def to_next_section(block):
    sections = lax.axis_size("section")
    count = lax.axis_size("seq")
    return [
        lax.ppermute(
            block,
            ("section", "seq"),
            [
                (section * count + source, (section + 1) * count + (source + step) % count)
                for section in range(sections - 1)
                for source in range(count)
            ],
        )
        for step in range(0, count, 2)
    ]


def kernel_tables(patch_sizes_list, section_index):
    patches = patch_sizes_list.shape[0]
    count = lax.axis_size("seq")
    here = lax.axis_index("seq")
    chips = count // 2
    turn = lax.broadcasted_iota(jnp.int32, (patches, count + 2), 0)
    entry = lax.broadcasted_iota(jnp.int32, (patches, count + 2), 1) - 2
    patch_index = jnp.remainder(turn - section_index + patches, patches)
    patch_ids = jnp.arange(patches).reshape(1, 1, patches)
    sizes = patch_sizes_list.reshape(1, 1, patches)
    chosen = patch_ids == patch_index[:, :, None]
    patch_count = jnp.sum(jnp.where(chosen, sizes, 0), axis=-1)
    patch_start = jnp.sum(jnp.where(patch_ids < patch_index[:, :, None], sizes, 0), axis=-1)
    base = jnp.where(entry < chips, here, jnp.bitwise_xor(here, 1))
    sources = jnp.remainder(base - 2 * jnp.remainder(entry, chips) + count, count)
    return jnp.where(entry == -2, patch_start, jnp.where(entry == -1, patch_count, sources)).astype(
        jnp.int32
    )


def block_kernel(*refs):
    where_ref = refs[0]
    count = len(refs) - 9
    part_refs = refs[1 : 1 + count]
    scale_ref, weights_ref, keys_ref, values_ref = refs[1 + count : 5 + count]
    heads_ref, keys_out, values_out = refs[5 + count : 8 + count]
    shaped_ref = refs[8 + count]
    start = where_ref[0]
    patch_count = where_ref[1]
    head_dim = keys_ref.shape[2]
    seq_len = keys_ref.shape[1]
    span, width = part_refs[0].shape
    features = width * count

    @pl.when(pl.program_id(0) == 0)
    def _():
        parts = [part[...].astype(jnp.float32) for part in part_refs]
        row_mean = sum(jnp.sum(part, axis=-1, keepdims=True) for part in parts) / features
        centred = [part - row_mean for part in parts]
        spread = sum(jnp.sum(c * c, axis=-1, keepdims=True) for c in centred) / features
        inverse = lax.rsqrt(spread + epsilon)
        for part in range(count):
            slot = where_ref[2 + part]
            shift_scale = scale_ref[slot]
            shaped_ref[slot] = (
                (centred[part] * inverse) * (1.0 + shift_scale[1:2]) + shift_scale[0:1]
            ).astype(jnp.bfloat16)

    mixed = sum(
        jnp.dot(
            shaped_ref[slot],
            weights_ref[slot * width : (slot + 1) * width, :],
            preferred_element_type=jnp.float32,
        )
        for slot in range(count)
    )
    queries = rms_norm(mixed[:, :head_dim]).astype(jnp.bfloat16)
    fresh_keys = rms_norm(mixed[:, head_dim : 2 * head_dim]).astype(jnp.bfloat16)
    fresh_values = mixed[:, 2 * head_dim :].astype(jnp.bfloat16)
    rows = lax.broadcasted_iota(jnp.int32, (seq_len, span), 0)
    picks = lax.broadcasted_iota(jnp.int32, (seq_len, span), 1)
    placing = ((rows == picks + start) & (picks < patch_count)).astype(jnp.bfloat16)
    row_ids = lax.broadcasted_iota(jnp.int32, (seq_len, 1), 0)
    inside = (row_ids >= start) & (row_ids < start + patch_count)
    placed_keys = jnp.dot(placing, fresh_keys, preferred_element_type=jnp.float32)
    placed_values = jnp.dot(placing, fresh_values, preferred_element_type=jnp.float32)
    keys = jnp.where(inside, placed_keys.astype(jnp.bfloat16), keys_ref[0])
    values = jnp.where(inside, placed_values.astype(jnp.bfloat16), values_ref[0])
    keys_out[0] = keys
    values_out[0] = values
    scores = lax.dot_general(
        queries, keys, (((1,), (1,)), ((), ())), preferred_element_type=jnp.float32
    ) * head_dim ** (-0.5)
    expos = jnp.exp(scores)
    weights = (expos / jnp.sum(expos, axis=-1, keepdims=True)).astype(jnp.bfloat16)
    heads_ref[...] = jnp.dot(weights, values, preferred_element_type=jnp.float32).astype(
        jnp.bfloat16
    )


def attend_block(parts, shift_scale, qkv_weights, key_cache, value_cache, where, in_place):
    count = len(parts)
    span, width = parts[0].shape
    heads_here, seq_len, head_dim = key_cache.shape
    features = qkv_weights.shape[0]
    scale_blocks = jnp.transpose(shift_scale.reshape(2, count, width), (1, 0, 2))
    whole = lambda shape: pl.BlockSpec(shape, lambda h, where: (0,) * len(shape))
    cache_spec = pl.BlockSpec((1, seq_len, head_dim), lambda h, where: (h, 0, 0))
    grid_spec = pltpu.PrefetchScalarGridSpec(
        num_scalar_prefetch=1,
        grid=(heads_here,),
        in_specs=[whole((span, width)) for _ in parts]
        + [
            whole((count, 2, width)),
            pl.BlockSpec((features, 3 * head_dim), lambda h, where: (0, h)),
            cache_spec,
            cache_spec,
        ],
        out_specs=[
            pl.BlockSpec((span, head_dim), lambda h, where: (0, h)),
            cache_spec,
            cache_spec,
        ],
        scratch_shapes=[pltpu.VMEM((count, span, width), jnp.bfloat16)],
    )
    return pl.pallas_call(
        block_kernel,
        grid_spec=grid_spec,
        out_shape=[
            jax.ShapeDtypeStruct((span, heads_here * head_dim), jnp.bfloat16),
            jax.ShapeDtypeStruct(key_cache.shape, key_cache.dtype),
            jax.ShapeDtypeStruct(value_cache.shape, value_cache.dtype),
        ],
        input_output_aliases={count + 3: 1, count + 4: 2} if in_place else {},
        compiler_params=pltpu.CompilerParams(dimension_semantics=("arbitrary",)),
    )(where, *parts, scale_blocks, qkv_weights, key_cache, value_cache)


def exit_kernel(turn, *refs):
    where_ref = refs[0]
    count = len(refs) - 8
    part_refs = refs[1 : 1 + count]
    weights_ref, own_ref, gate_ref = refs[1 + count : 4 + count]
    out_ref, turns_ref, copied = refs[5 + count :]
    patch_count = where_ref[1]
    projected = sum(
        jnp.dot(
            part_refs[part][...],
            weights_ref[where_ref[2 + part]],
            preferred_element_type=jnp.float32,
        )
        for part in range(count)
    )
    updated = own_ref[...].astype(jnp.float32) + gate_ref[...] * projected
    live = lax.broadcasted_iota(jnp.int32, updated.shape, 0) < patch_count
    out_ref[...] = jnp.where(live, updated, 0.0).astype(out_ref.dtype)
    store = pltpu.make_async_copy(out_ref, turns_ref.at[turn], copied)
    store.start()
    store.wait()


def leave_block(parts, out_weights, own_rows, gating_here, where, every_turn, turn):
    count = len(parts)
    span, head_width = parts[0].shape
    vmem = pl.BlockSpec(memory_space=pltpu.VMEM)
    smem = pl.BlockSpec(memory_space=pltpu.SMEM)
    anywhere = pl.BlockSpec(memory_space=pl.ANY)
    return pl.pallas_call(
        functools.partial(exit_kernel, turn),
        in_specs=[smem] + [vmem] * (count + 3) + [anywhere],
        out_specs=[vmem, anywhere],
        out_shape=[
            jax.ShapeDtypeStruct(own_rows.shape, own_rows.dtype),
            jax.ShapeDtypeStruct(every_turn.shape, every_turn.dtype),
        ],
        scratch_shapes=[pltpu.SemaphoreType.DMA(())],
        input_output_aliases={count + 4: 1},
    )(
        where,
        *parts,
        out_weights.reshape(count, head_width, out_weights.shape[1]),
        own_rows,
        gating_here.reshape(1, -1),
        every_turn,
    )


def shards(
    incoming_states,
    transit_states,
    patch_sizes_list,
    outdated_lookups,
    outdated_contents,
    attention_projection,
    exit_projection,
    shift_and_scale,
    branch_gates,
):
    section_index = lax.axis_index("section")
    patches = patch_sizes_list.shape[0]
    biggest_patch_span = transit_states.shape[1]
    columns = incoming_states.shape[1]
    starts = jnp.cumsum(patch_sizes_list) - patch_sizes_list
    key_cache = outdated_lookups[0]
    value_cache = outdated_contents[0]
    qkv_weights = attention_projection[0]
    out_weights = exit_projection[0]
    shift_scale = shift_and_scale[0]
    gating_here = branch_gates[0]
    row_numbers = jnp.arange(biggest_patch_span)

    every_turn = jnp.zeros((patches, biggest_patch_span, incoming_states.shape[1]), jnp.bfloat16)
    entering_ext = jnp.concatenate(
        [incoming_states, jnp.zeros((biggest_patch_span, columns), jnp.bfloat16)], axis=0
    )
    section_zero = section_index == 0
    own_rows = jnp.where(section_zero, entering_ext[:biggest_patch_span], transit_states[0])
    own_rows = jnp.where(
        (row_numbers < pick_entry(patch_sizes_list, jnp.remainder(-section_index, patches)))[:, None],
        own_rows,
        0,
    )
    tables, own_rows = lax.optimization_barrier(
        (kernel_tables(patch_sizes_list, section_index), own_rows)
    )
    row_parts = [own_rows] + across_chips(own_rows)
    for turn_number in range(patches):
        where = tables[turn_number]
        head_rows, key_cache, value_cache = attend_block(
            with_partner(row_parts),
            shift_scale,
            qkv_weights,
            key_cache,
            value_cache,
            where,
            turn_number > 0,
        )
        updated, every_turn = leave_block(
            with_partner([head_rows] + across_chips(head_rows)),
            out_weights,
            row_parts[0],
            gating_here,
            where,
            every_turn,
            turn_number,
        )
        if turn_number + 1 < patches:
            entry_patch = lax.dynamic_slice_in_dim(
                entering_ext, starts[turn_number + 1], biggest_patch_span, 0
            )
            entry_patch = jnp.where(
                (row_numbers < patch_sizes_list[turn_number + 1])[:, None], entry_patch, 0
            )
            arrived = to_next_section(updated)
            entry_parts = [entry_patch] + across_chips_first_section(entry_patch)
            row_parts = [
                jnp.where(section_zero, entry, passed) for entry, passed in zip(entry_parts, arrived)
            ]
    return every_turn[:, None]


def solution(mesh):
    return jax.shard_map(
        shards,
        mesh=mesh,
        in_specs=(
            P("groups", "seq"),
            P("section", "groups", "seq"),
            P("groups"),
            P("section", "seq", "groups", None),
            P("section", "seq", "groups", None),
            P("section", None, "seq"),
            P("section", None, "seq"),
            P("section", None, None),
            P("section", "seq"),
        ),
        out_specs=P(None, "section", "groups", "seq"),
        check_vma=False,
    )
```

```python
import jax
import jax.numpy as jnp
from jax import lax
from jax.experimental import pallas as pl
from jax.experimental.pallas import tpu as pltpu
from jax.sharding import PartitionSpec as P

epsilon = 1e-06


def rms_norm(values):
    return values * lax.rsqrt(jnp.mean(values * values, axis=-1, keepdims=True) + epsilon)


def pick_entry(vector, position):
    return jnp.sum(jnp.where(jnp.arange(vector.shape[0]) == position, vector, 0))


def across_chips(block):
    count = lax.axis_size("seq")
    return [
        lax.ppermute(block, "seq", [(source, (source + step) % count) for source in range(count)])
        for step in range(2, count, 2)
    ]


def across_chips_first_section(block):
    count = lax.axis_size("seq")
    return [
        lax.ppermute(
            block, ("section", "seq"), [(source, (source + step) % count) for source in range(count)]
        )
        for step in range(2, count, 2)
    ]


def with_partner(parts):
    count = lax.axis_size("seq")
    to_partner = [(source, source ^ 1) for source in range(count)]
    return parts + [lax.ppermute(part, "seq", to_partner) for part in parts]


def to_next_section(block):
    sections = lax.axis_size("section")
    count = lax.axis_size("seq")
    return [
        lax.ppermute(
            block,
            ("section", "seq"),
            [
                (section * count + source, (section + 1) * count + (source + step) % count)
                for section in range(sections - 1)
                for source in range(count)
            ],
        )
        for step in range(0, count, 2)
    ]


def kernel_tables(patch_sizes_list, section_index):
    patches = patch_sizes_list.shape[0]
    count = lax.axis_size("seq")
    here = lax.axis_index("seq")
    chips = count // 2
    turn = lax.broadcasted_iota(jnp.int32, (patches, count + 2), 0)
    entry = lax.broadcasted_iota(jnp.int32, (patches, count + 2), 1) - 2
    patch_index = jnp.remainder(turn - section_index + patches, patches)
    patch_ids = jnp.arange(patches).reshape(1, 1, patches)
    sizes = patch_sizes_list.reshape(1, 1, patches)
    chosen = patch_ids == patch_index[:, :, None]
    patch_count = jnp.sum(jnp.where(chosen, sizes, 0), axis=-1)
    patch_start = jnp.sum(jnp.where(patch_ids < patch_index[:, :, None], sizes, 0), axis=-1)
    base = jnp.where(entry < chips, here, jnp.bitwise_xor(here, 1))
    sources = jnp.remainder(base - 2 * jnp.remainder(entry, chips) + count, count)
    return jnp.where(entry == -2, patch_start, jnp.where(entry == -1, patch_count, sources)).astype(
        jnp.int32
    )


def block_kernel(*refs):
    where_ref = refs[0]
    count = len(refs) - 11
    part_refs = refs[1 : 1 + count]
    scale_ref, weights_ref, keys_ref, values_ref = refs[1 + count : 5 + count]
    heads_ref, keys_out, values_out = refs[5 + count : 8 + count]
    shaped_ref, landed_ref, arrived = refs[8 + count :]
    start = where_ref[0]
    patch_count = where_ref[1]
    head_dim = keys_ref.shape[2]
    seq_len = keys_ref.shape[1]
    span, width = landed_ref.shape[1:]
    features = width * count

    @pl.when(pl.program_id(0) == 0)
    def _():
        copies = [
            pltpu.make_async_copy(part_refs[part], landed_ref.at[part], arrived.at[part])
            for part in range(count)
        ]
        for copy in copies:
            copy.start()
        for copy in copies:
            copy.wait()
        parts = [landed_ref[part].astype(jnp.float32) for part in range(count)]
        row_mean = sum(jnp.sum(part, axis=-1, keepdims=True) for part in parts) / features
        centred = [part - row_mean for part in parts]
        spread = sum(jnp.sum(c * c, axis=-1, keepdims=True) for c in centred) / features
        inverse = lax.rsqrt(spread + epsilon)
        for part in range(count):
            slot = where_ref[2 + part]
            shift_scale = scale_ref[slot]
            shaped_ref[slot] = (
                (centred[part] * inverse) * (1.0 + shift_scale[1:2]) + shift_scale[0:1]
            ).astype(jnp.bfloat16)

    mixed = sum(
        jnp.dot(
            shaped_ref[slot],
            weights_ref[slot * width : (slot + 1) * width, :],
            preferred_element_type=jnp.float32,
        )
        for slot in range(count)
    )
    queries = rms_norm(mixed[:, :head_dim]).astype(jnp.bfloat16)
    fresh_keys = rms_norm(mixed[:, head_dim : 2 * head_dim]).astype(jnp.bfloat16)
    fresh_values = mixed[:, 2 * head_dim :].astype(jnp.bfloat16)
    rows = lax.broadcasted_iota(jnp.int32, (seq_len, span), 0)
    picks = lax.broadcasted_iota(jnp.int32, (seq_len, span), 1)
    placing = ((rows == picks + start) & (picks < patch_count)).astype(jnp.bfloat16)
    row_ids = lax.broadcasted_iota(jnp.int32, (seq_len, 1), 0)
    inside = (row_ids >= start) & (row_ids < start + patch_count)
    placed_keys = jnp.dot(placing, fresh_keys, preferred_element_type=jnp.float32)
    placed_values = jnp.dot(placing, fresh_values, preferred_element_type=jnp.float32)
    keys = jnp.where(inside, placed_keys.astype(jnp.bfloat16), keys_ref[0])
    values = jnp.where(inside, placed_values.astype(jnp.bfloat16), values_ref[0])
    keys_out[0] = keys
    values_out[0] = values
    scores = lax.dot_general(
        queries, keys, (((1,), (1,)), ((), ())), preferred_element_type=jnp.float32
    ) * head_dim ** (-0.5)
    expos = jnp.exp(scores)
    weights = (expos / jnp.sum(expos, axis=-1, keepdims=True)).astype(jnp.bfloat16)
    heads_ref[...] = jnp.dot(weights, values, preferred_element_type=jnp.float32).astype(
        jnp.bfloat16
    )


def attend_block(parts, shift_scale, qkv_weights, key_cache, value_cache, where, in_place):
    count = len(parts)
    span, width = parts[0].shape
    heads_here, seq_len, head_dim = key_cache.shape
    features = qkv_weights.shape[0]
    scale_blocks = jnp.transpose(shift_scale.reshape(2, count, width), (1, 0, 2))
    whole = lambda shape: pl.BlockSpec(shape, lambda h, where: (0,) * len(shape))
    cache_spec = pl.BlockSpec((1, seq_len, head_dim), lambda h, where: (h, 0, 0))
    grid_spec = pltpu.PrefetchScalarGridSpec(
        num_scalar_prefetch=1,
        grid=(heads_here,),
        in_specs=[pl.BlockSpec(memory_space=pl.ANY) for _ in parts]
        + [
            whole((count, 2, width)),
            pl.BlockSpec((features, 3 * head_dim), lambda h, where: (0, h)),
            cache_spec,
            cache_spec,
        ],
        out_specs=[
            pl.BlockSpec((span, head_dim), lambda h, where: (0, h)),
            cache_spec,
            cache_spec,
        ],
        scratch_shapes=[
            pltpu.VMEM((count, span, width), jnp.bfloat16),
            pltpu.VMEM((count, span, width), jnp.bfloat16),
            pltpu.SemaphoreType.DMA((count,)),
        ],
    )
    return pl.pallas_call(
        block_kernel,
        grid_spec=grid_spec,
        out_shape=[
            jax.ShapeDtypeStruct((span, heads_here * head_dim), jnp.bfloat16),
            jax.ShapeDtypeStruct(key_cache.shape, key_cache.dtype),
            jax.ShapeDtypeStruct(value_cache.shape, value_cache.dtype),
        ],
        input_output_aliases={count + 3: 1, count + 4: 2} if in_place else {},
        compiler_params=pltpu.CompilerParams(dimension_semantics=("arbitrary",)),
    )(where, *parts, scale_blocks, qkv_weights, key_cache, value_cache)


def exit_kernel(*refs):
    where_ref = refs[0]
    count = len(refs) - 7
    part_refs = refs[1 : 1 + count]
    weights_ref, own_ref, gate_ref = refs[1 + count : 4 + count]
    out_ref, landed_ref, arrived = refs[4 + count :]
    patch_count = where_ref[1]
    copies = [
        pltpu.make_async_copy(part_refs[part], landed_ref.at[part], arrived.at[part])
        for part in range(count)
    ]
    for copy in copies:
        copy.start()
    for copy in copies:
        copy.wait()
    projected = sum(
        jnp.dot(
            landed_ref[part],
            weights_ref[where_ref[2 + part]],
            preferred_element_type=jnp.float32,
        )
        for part in range(count)
    )
    updated = own_ref[...].astype(jnp.float32) + gate_ref[...] * projected
    live = lax.broadcasted_iota(jnp.int32, updated.shape, 0) < patch_count
    out_ref[...] = jnp.where(live, updated, 0.0).astype(out_ref.dtype)


def leave_block(parts, out_weights, own_rows, gating_here, where):
    count = len(parts)
    span, head_width = parts[0].shape
    vmem = pl.BlockSpec(memory_space=pltpu.VMEM)
    smem = pl.BlockSpec(memory_space=pltpu.SMEM)
    return pl.pallas_call(
        exit_kernel,
        in_specs=[smem] + [pl.BlockSpec(memory_space=pl.ANY)] * count + [vmem] * 3,
        out_specs=vmem,
        out_shape=jax.ShapeDtypeStruct(own_rows.shape, own_rows.dtype),
        scratch_shapes=[
            pltpu.VMEM((count, span, head_width), parts[0].dtype),
            pltpu.SemaphoreType.DMA((count,)),
        ],
    )(
        where,
        *parts,
        out_weights.reshape(count, head_width, out_weights.shape[1]),
        own_rows,
        gating_here.reshape(1, -1),
    )


def shards(
    incoming_states,
    transit_states,
    patch_sizes_list,
    outdated_lookups,
    outdated_contents,
    attention_projection,
    exit_projection,
    shift_and_scale,
    branch_gates,
):
    section_index = lax.axis_index("section")
    patches = patch_sizes_list.shape[0]
    biggest_patch_span = transit_states.shape[1]
    columns = incoming_states.shape[1]
    starts = jnp.cumsum(patch_sizes_list) - patch_sizes_list
    key_cache = outdated_lookups[0]
    value_cache = outdated_contents[0]
    qkv_weights = attention_projection[0]
    out_weights = exit_projection[0]
    shift_scale = shift_and_scale[0]
    gating_here = branch_gates[0]
    row_numbers = jnp.arange(biggest_patch_span)

    results = []
    entering_ext = jnp.concatenate(
        [incoming_states, jnp.zeros((biggest_patch_span, columns), jnp.bfloat16)], axis=0
    )
    section_zero = section_index == 0
    own_rows = jnp.where(section_zero, entering_ext[:biggest_patch_span], transit_states[0])
    own_rows = jnp.where(
        (row_numbers < pick_entry(patch_sizes_list, jnp.remainder(-section_index, patches)))[:, None],
        own_rows,
        0,
    )
    tables, own_rows = lax.optimization_barrier(
        (kernel_tables(patch_sizes_list, section_index), own_rows)
    )
    row_parts = [own_rows] + across_chips(own_rows)
    for turn_number in range(patches):
        where = tables[turn_number]
        head_rows, key_cache, value_cache = attend_block(
            with_partner(row_parts),
            shift_scale,
            qkv_weights,
            key_cache,
            value_cache,
            where,
            turn_number > 0,
        )
        updated = leave_block(
            with_partner([head_rows] + across_chips(head_rows)),
            out_weights,
            row_parts[0],
            gating_here,
            where,
        )
        results.append(updated)
        if turn_number + 1 < patches:
            entry_patch = lax.dynamic_slice_in_dim(
                entering_ext, starts[turn_number + 1], biggest_patch_span, 0
            )
            entry_patch = jnp.where(
                (row_numbers < patch_sizes_list[turn_number + 1])[:, None], entry_patch, 0
            )
            arrived = to_next_section(updated)
            entry_parts = [entry_patch] + across_chips_first_section(entry_patch)
            row_parts = [
                jnp.where(section_zero, entry, passed) for entry, passed in zip(entry_parts, arrived)
            ]
    return jnp.stack(results)[:, None]


def solution(mesh):
    return jax.shard_map(
        shards,
        mesh=mesh,
        in_specs=(
            P("groups", "seq"),
            P("section", "groups", "seq"),
            P("groups"),
            P("section", "seq", "groups", None),
            P("section", "seq", "groups", None),
            P("section", None, "seq"),
            P("section", None, "seq"),
            P("section", None, None),
            P("section", "seq"),
        ),
        out_specs=P(None, "section", "groups", "seq"),
        check_vma=False,
    )
```

```python
import jax
import jax.numpy as jnp
from jax import lax
from jax.experimental import pallas as pl
from jax.experimental.pallas import tpu as pltpu
from jax.sharding import PartitionSpec as P

epsilon = 1e-06


def rms_norm(values):
    return values * lax.rsqrt(jnp.mean(values * values, axis=-1, keepdims=True) + epsilon)


def pick_entry(vector, position):
    return jnp.sum(jnp.where(jnp.arange(vector.shape[0]) == position, vector, 0))


def across_chips(block):
    count = lax.axis_size("seq")
    return [
        lax.ppermute(block, "seq", [(source, (source + step) % count) for source in range(count)])
        for step in range(2, count, 2)
    ]


def across_chips_first_section(block):
    count = lax.axis_size("seq")
    return [
        lax.ppermute(
            block, ("section", "seq"), [(source, (source + step) % count) for source in range(count)]
        )
        for step in range(2, count, 2)
    ]


def with_partner(parts):
    count = lax.axis_size("seq")
    to_partner = [(source, source ^ 1) for source in range(count)]
    return parts + [lax.ppermute(part, "seq", to_partner) for part in parts]


def to_next_section(block):
    sections = lax.axis_size("section")
    count = lax.axis_size("seq")
    return [
        lax.ppermute(
            block,
            ("section", "seq"),
            [
                (section * count + source, (section + 1) * count + (source + step) % count)
                for section in range(sections - 1)
                for source in range(count)
            ],
        )
        for step in range(0, count, 2)
    ]


def kernel_tables(patch_sizes_list, section_index):
    patches = patch_sizes_list.shape[0]
    count = lax.axis_size("seq")
    here = lax.axis_index("seq")
    chips = count // 2
    turn = lax.broadcasted_iota(jnp.int32, (patches, count + 2), 0)
    entry = lax.broadcasted_iota(jnp.int32, (patches, count + 2), 1) - 2
    patch_index = jnp.remainder(turn - section_index + patches, patches)
    patch_ids = jnp.arange(patches).reshape(1, 1, patches)
    sizes = patch_sizes_list.reshape(1, 1, patches)
    chosen = patch_ids == patch_index[:, :, None]
    patch_count = jnp.sum(jnp.where(chosen, sizes, 0), axis=-1)
    patch_start = jnp.sum(jnp.where(patch_ids < patch_index[:, :, None], sizes, 0), axis=-1)
    base = jnp.where(entry < chips, here, jnp.bitwise_xor(here, 1))
    sources = jnp.remainder(base - 2 * jnp.remainder(entry, chips) + count, count)
    return jnp.where(entry == -2, patch_start, jnp.where(entry == -1, patch_count, sources)).astype(
        jnp.int32
    )


def block_kernel(*refs):
    where_ref = refs[0]
    count = len(refs) - 9
    part_refs = refs[1 : 1 + count]
    scale_ref, weights_ref, keys_ref, values_ref = refs[1 + count : 5 + count]
    heads_ref, keys_out, values_out = refs[5 + count : 8 + count]
    shaped_ref = refs[8 + count]
    start = where_ref[0]
    patch_count = where_ref[1]
    head_dim = keys_ref.shape[2]
    seq_len = keys_ref.shape[1]
    span, width = part_refs[0].shape
    features = width * count

    @pl.when(pl.program_id(0) == 0)
    def _():
        parts = [part[...].astype(jnp.float32) for part in part_refs]
        row_mean = sum(jnp.sum(part, axis=-1, keepdims=True) for part in parts) / features
        centred = [part - row_mean for part in parts]
        spread = sum(jnp.sum(c * c, axis=-1, keepdims=True) for c in centred) / features
        inverse = lax.rsqrt(spread + epsilon)
        for part in range(count):
            slot = where_ref[2 + part]
            shift_scale = scale_ref[slot]
            shaped_ref[slot] = (
                (centred[part] * inverse) * (1.0 + shift_scale[1:2]) + shift_scale[0:1]
            ).astype(jnp.bfloat16)

    mixed = sum(
        jnp.dot(
            shaped_ref[slot],
            weights_ref[slot * width : (slot + 1) * width, :],
            preferred_element_type=jnp.float32,
        )
        for slot in range(count)
    )
    queries = rms_norm(mixed[:, :head_dim]).astype(jnp.bfloat16)
    fresh_keys = rms_norm(mixed[:, head_dim : 2 * head_dim]).astype(jnp.bfloat16)
    fresh_values = mixed[:, 2 * head_dim :].astype(jnp.bfloat16)
    rows = lax.broadcasted_iota(jnp.int32, (seq_len, span), 0)
    picks = lax.broadcasted_iota(jnp.int32, (seq_len, span), 1)
    placing = ((rows == picks + start) & (picks < patch_count)).astype(jnp.bfloat16)
    row_ids = lax.broadcasted_iota(jnp.int32, (seq_len, 1), 0)
    inside = (row_ids >= start) & (row_ids < start + patch_count)
    placed_keys = jnp.dot(placing, fresh_keys, preferred_element_type=jnp.float32)
    placed_values = jnp.dot(placing, fresh_values, preferred_element_type=jnp.float32)
    keys = jnp.where(inside, placed_keys.astype(jnp.bfloat16), keys_ref[0])
    values = jnp.where(inside, placed_values.astype(jnp.bfloat16), values_ref[0])
    keys_out[0] = keys
    values_out[0] = values
    scores = lax.dot_general(
        queries, keys, (((1,), (1,)), ((), ())), preferred_element_type=jnp.float32
    ) * head_dim ** (-0.5)
    expos = jnp.exp(scores)
    weights = (expos / jnp.sum(expos, axis=-1, keepdims=True)).astype(jnp.bfloat16)
    heads_ref[...] = jnp.dot(weights, values, preferred_element_type=jnp.float32).astype(
        jnp.bfloat16
    )


def attend_block(parts, shift_scale, qkv_weights, key_cache, value_cache, where, in_place):
    count = len(parts)
    span, width = parts[0].shape
    heads_here, seq_len, head_dim = key_cache.shape
    features = qkv_weights.shape[0]
    scale_blocks = jnp.transpose(shift_scale.reshape(2, count, width), (1, 0, 2))
    whole = lambda shape: pl.BlockSpec(shape, lambda h, where: (0,) * len(shape))
    cache_spec = pl.BlockSpec((1, seq_len, head_dim), lambda h, where: (h, 0, 0))
    grid_spec = pltpu.PrefetchScalarGridSpec(
        num_scalar_prefetch=1,
        grid=(heads_here,),
        in_specs=[whole((span, width)) for _ in parts]
        + [
            whole((count, 2, width)),
            pl.BlockSpec((features, 3 * head_dim), lambda h, where: (0, h)),
            cache_spec,
            cache_spec,
        ],
        out_specs=[
            pl.BlockSpec((span, head_dim), lambda h, where: (0, h)),
            cache_spec,
            cache_spec,
        ],
        scratch_shapes=[pltpu.VMEM((count, span, width), jnp.bfloat16)],
    )
    return pl.pallas_call(
        block_kernel,
        grid_spec=grid_spec,
        out_shape=[
            jax.ShapeDtypeStruct((span, heads_here * head_dim), jnp.bfloat16),
            jax.ShapeDtypeStruct(key_cache.shape, key_cache.dtype),
            jax.ShapeDtypeStruct(value_cache.shape, value_cache.dtype),
        ],
        input_output_aliases={count + 3: 1, count + 4: 2} if in_place else {},
        compiler_params=pltpu.CompilerParams(dimension_semantics=("arbitrary",)),
    )(where, *parts, scale_blocks, qkv_weights, key_cache, value_cache)


def exit_kernel(*refs):
    where_ref = refs[0]
    count = len(refs) - 5
    part_refs = refs[1 : 1 + count]
    weights_ref, own_ref, gate_ref = refs[1 + count : 4 + count]
    out_ref = refs[4 + count]
    patch_count = where_ref[1]
    projected = sum(
        jnp.dot(
            part_refs[part][...],
            weights_ref[where_ref[2 + part]],
            preferred_element_type=jnp.float32,
        )
        for part in range(count)
    )
    updated = own_ref[...].astype(jnp.float32) + gate_ref[...] * projected
    live = lax.broadcasted_iota(jnp.int32, updated.shape, 0) < patch_count
    out_ref[...] = jnp.where(live, updated, 0.0).astype(out_ref.dtype)


def leave_block(parts, out_weights, own_rows, gating_here, where):
    count = len(parts)
    span, head_width = parts[0].shape
    vmem = pl.BlockSpec(memory_space=pltpu.VMEM)
    smem = pl.BlockSpec(memory_space=pltpu.SMEM)
    return pl.pallas_call(
        exit_kernel,
        in_specs=[smem] + [vmem] * (count + 3),
        out_specs=vmem,
        out_shape=jax.ShapeDtypeStruct(own_rows.shape, own_rows.dtype),
    )(
        where,
        *parts,
        out_weights.reshape(count, head_width, out_weights.shape[1]),
        own_rows,
        gating_here.reshape(1, -1),
    )


def shards(
    incoming_states,
    transit_states,
    patch_sizes_list,
    outdated_lookups,
    outdated_contents,
    attention_projection,
    exit_projection,
    shift_and_scale,
    branch_gates,
):
    section_index = lax.axis_index("section")
    patches = patch_sizes_list.shape[0]
    biggest_patch_span = transit_states.shape[1]
    columns = incoming_states.shape[1]
    starts = jnp.cumsum(patch_sizes_list) - patch_sizes_list
    key_cache = outdated_lookups[0]
    value_cache = outdated_contents[0]
    qkv_weights = attention_projection[0]
    out_weights = exit_projection[0]
    shift_scale = shift_and_scale[0]
    gating_here = branch_gates[0]
    row_numbers = jnp.arange(biggest_patch_span)

    results = []
    entering_ext = jnp.concatenate(
        [incoming_states, jnp.zeros((biggest_patch_span, columns), jnp.bfloat16)], axis=0
    )
    section_zero = section_index == 0
    own_rows = jnp.where(section_zero, entering_ext[:biggest_patch_span], transit_states[0])
    own_rows = jnp.where(
        (row_numbers < pick_entry(patch_sizes_list, jnp.remainder(-section_index, patches)))[:, None],
        own_rows,
        0,
    )
    tables, own_rows = lax.optimization_barrier(
        (kernel_tables(patch_sizes_list, section_index), own_rows)
    )
    row_parts = [own_rows] + across_chips(own_rows)
    entering_across = [
        jnp.concatenate([rows, jnp.zeros((biggest_patch_span, columns), jnp.bfloat16)], axis=0)
        for rows in across_chips_first_section(incoming_states)
    ]
    for turn_number in range(patches):
        where = tables[turn_number]
        head_rows, key_cache, value_cache = attend_block(
            with_partner(row_parts),
            shift_scale,
            qkv_weights,
            key_cache,
            value_cache,
            where,
            turn_number > 0,
        )
        updated = leave_block(
            with_partner([head_rows] + across_chips(head_rows)),
            out_weights,
            row_parts[0],
            gating_here,
            where,
        )
        results.append(updated)
        if turn_number + 1 < patches:
            entry_live = (row_numbers < patch_sizes_list[turn_number + 1])[:, None]
            entry_parts = [
                jnp.where(
                    entry_live,
                    lax.dynamic_slice_in_dim(
                        rows, starts[turn_number + 1], biggest_patch_span, 0
                    ),
                    0,
                )
                for rows in [entering_ext] + entering_across
            ]
            arrived = to_next_section(updated)
            row_parts = [
                jnp.where(section_zero, entry, passed) for entry, passed in zip(entry_parts, arrived)
            ]
    return jnp.stack(results)[:, None]


def solution(mesh):
    return jax.shard_map(
        shards,
        mesh=mesh,
        in_specs=(
            P("groups", "seq"),
            P("section", "groups", "seq"),
            P("groups"),
            P("section", "seq", "groups", None),
            P("section", "seq", "groups", None),
            P("section", None, "seq"),
            P("section", None, "seq"),
            P("section", None, None),
            P("section", "seq"),
        ),
        out_specs=P(None, "section", "groups", "seq"),
        check_vma=False,
    )
```

```python
import jax
import jax.numpy as jnp
from jax import lax
from jax.experimental import pallas as pl
from jax.experimental.pallas import tpu as pltpu
from jax.sharding import PartitionSpec as P

epsilon = 1e-06


def rms_norm(values):
    return values * lax.rsqrt(jnp.mean(values * values, axis=-1, keepdims=True) + epsilon)


def pick_entry(vector, position):
    return jnp.sum(jnp.where(jnp.arange(vector.shape[0]) == position, vector, 0))


def across_chips(block):
    count = lax.axis_size("seq")
    return [
        lax.ppermute(block, "seq", [(source, (source + step) % count) for source in range(count)])
        for step in range(2, count, 2)
    ]


def across_chips_first_section(block):
    count = lax.axis_size("seq")
    return [
        lax.ppermute(
            block, ("section", "seq"), [(source, (source + step) % count) for source in range(count)]
        )
        for step in range(2, count, 2)
    ]


def with_partner(parts):
    count = lax.axis_size("seq")
    to_partner = [(source, source ^ 1) for source in range(count)]
    return parts + [lax.ppermute(part, "seq", to_partner) for part in parts]


def to_next_section(block):
    sections = lax.axis_size("section")
    count = lax.axis_size("seq")
    return [
        lax.ppermute(
            block,
            ("section", "seq"),
            [
                (section * count + source, (section + 1) * count + (source + step) % count)
                for section in range(sections - 1)
                for source in range(count)
            ],
        )
        for step in range(0, count, 2)
    ]


def kernel_tables(patch_sizes_list, section_index):
    patches = patch_sizes_list.shape[0]
    count = lax.axis_size("seq")
    here = lax.axis_index("seq")
    chips = count // 2
    turn = lax.broadcasted_iota(jnp.int32, (patches, count + 2), 0)
    entry = lax.broadcasted_iota(jnp.int32, (patches, count + 2), 1) - 2
    patch_index = jnp.remainder(turn - section_index + patches, patches)
    patch_ids = jnp.arange(patches).reshape(1, 1, patches)
    sizes = patch_sizes_list.reshape(1, 1, patches)
    chosen = patch_ids == patch_index[:, :, None]
    patch_count = jnp.sum(jnp.where(chosen, sizes, 0), axis=-1)
    patch_start = jnp.sum(jnp.where(patch_ids < patch_index[:, :, None], sizes, 0), axis=-1)
    base = jnp.where(entry < chips, here, jnp.bitwise_xor(here, 1))
    sources = jnp.remainder(base - 2 * jnp.remainder(entry, chips) + count, count)
    return jnp.where(entry == -2, patch_start, jnp.where(entry == -1, patch_count, sources)).astype(
        jnp.int32
    )


def block_kernel(*refs):
    where_ref = refs[0]
    count = len(refs) - 9
    part_refs = refs[1 : 1 + count]
    scale_ref, weights_ref, keys_ref, values_ref = refs[1 + count : 5 + count]
    heads_ref, keys_out, values_out = refs[5 + count : 8 + count]
    shaped_ref = refs[8 + count]
    start = where_ref[0]
    patch_count = where_ref[1]
    head_dim = keys_ref.shape[2]
    seq_len = keys_ref.shape[1]
    span, width = part_refs[0].shape
    features = width * count

    @pl.when(pl.program_id(0) == 0)
    def _():
        parts = [part[...].astype(jnp.float32) for part in part_refs]
        row_mean = sum(jnp.sum(part, axis=-1, keepdims=True) for part in parts) / features
        centred = [part - row_mean for part in parts]
        spread = sum(jnp.sum(c * c, axis=-1, keepdims=True) for c in centred) / features
        inverse = lax.rsqrt(spread + epsilon)
        for part in range(count):
            slot = where_ref[2 + part]
            shift_scale = scale_ref[slot]
            shaped_ref[slot] = (
                (centred[part] * inverse) * (1.0 + shift_scale[1:2]) + shift_scale[0:1]
            ).astype(jnp.bfloat16)

    mixed = sum(
        jnp.dot(
            shaped_ref[slot],
            weights_ref[slot * width : (slot + 1) * width, :],
            preferred_element_type=jnp.float32,
        )
        for slot in range(count)
    )
    queries = rms_norm(mixed[:, :head_dim]).astype(jnp.bfloat16)
    fresh_keys = rms_norm(mixed[:, head_dim : 2 * head_dim]).astype(jnp.bfloat16)
    fresh_values = mixed[:, 2 * head_dim :].astype(jnp.bfloat16)
    rows = lax.broadcasted_iota(jnp.int32, (seq_len, span), 0)
    picks = lax.broadcasted_iota(jnp.int32, (seq_len, span), 1)
    placing = ((rows == picks + start) & (picks < patch_count)).astype(jnp.bfloat16)
    row_ids = lax.broadcasted_iota(jnp.int32, (seq_len, 1), 0)
    inside = (row_ids >= start) & (row_ids < start + patch_count)
    placed_keys = jnp.dot(placing, fresh_keys, preferred_element_type=jnp.float32)
    placed_values = jnp.dot(placing, fresh_values, preferred_element_type=jnp.float32)
    keys = jnp.where(inside, placed_keys.astype(jnp.bfloat16), keys_ref[0])
    values = jnp.where(inside, placed_values.astype(jnp.bfloat16), values_ref[0])
    keys_out[0] = keys
    values_out[0] = values
    scores = lax.dot_general(
        queries, keys, (((1,), (1,)), ((), ())), preferred_element_type=jnp.float32
    ) * head_dim ** (-0.5)
    expos = jnp.exp(scores)
    weights = (expos / jnp.sum(expos, axis=-1, keepdims=True)).astype(jnp.bfloat16)
    heads_ref[...] = jnp.dot(weights, values, preferred_element_type=jnp.float32).astype(
        jnp.bfloat16
    )


def attend_block(parts, shift_scale, qkv_weights, key_cache, value_cache, where, in_place):
    count = len(parts)
    span, width = parts[0].shape
    heads_here, seq_len, head_dim = key_cache.shape
    features = qkv_weights.shape[0]
    scale_blocks = jnp.transpose(shift_scale.reshape(2, count, width), (1, 0, 2))
    whole = lambda shape: pl.BlockSpec(shape, lambda h, where: (0,) * len(shape))
    cache_spec = pl.BlockSpec((1, seq_len, head_dim), lambda h, where: (h, 0, 0))
    grid_spec = pltpu.PrefetchScalarGridSpec(
        num_scalar_prefetch=1,
        grid=(heads_here,),
        in_specs=[whole((span, width)) for _ in parts]
        + [
            whole((count, 2, width)),
            pl.BlockSpec((features, 3 * head_dim), lambda h, where: (0, h)),
            cache_spec,
            cache_spec,
        ],
        out_specs=[
            pl.BlockSpec((span, head_dim), lambda h, where: (0, h)),
            cache_spec,
            cache_spec,
        ],
        scratch_shapes=[pltpu.VMEM((count, span, width), jnp.bfloat16)],
    )
    return pl.pallas_call(
        block_kernel,
        grid_spec=grid_spec,
        out_shape=[
            jax.ShapeDtypeStruct((span, heads_here * head_dim), jnp.bfloat16),
            jax.ShapeDtypeStruct(key_cache.shape, key_cache.dtype),
            jax.ShapeDtypeStruct(value_cache.shape, value_cache.dtype),
        ],
        input_output_aliases={count + 3: 1, count + 4: 2} if in_place else {},
        compiler_params=pltpu.CompilerParams(dimension_semantics=("arbitrary",)),
    )(where, *parts, scale_blocks, qkv_weights, key_cache, value_cache)


def exit_kernel(*refs):
    where_ref = refs[0]
    count = len(refs) - 5
    part_refs = refs[1 : 1 + count]
    weights_ref, own_ref, gate_ref = refs[1 + count : 4 + count]
    out_ref = refs[4 + count]
    patch_count = where_ref[1]
    projected = sum(
        jnp.dot(
            part_refs[part][...],
            weights_ref[where_ref[2 + part]],
            preferred_element_type=jnp.float32,
        )
        for part in range(count)
    )
    updated = own_ref[...].astype(jnp.float32) + gate_ref[...] * projected
    live = lax.broadcasted_iota(jnp.int32, updated.shape, 0) < patch_count
    out_ref[...] = jnp.where(live, updated, 0.0).astype(out_ref.dtype)


def leave_block(parts, out_weights, own_rows, gating_here, where):
    count = len(parts)
    span, head_width = parts[0].shape
    vmem = pl.BlockSpec(memory_space=pltpu.VMEM)
    smem = pl.BlockSpec(memory_space=pltpu.SMEM)
    return pl.pallas_call(
        exit_kernel,
        in_specs=[smem] + [vmem] * (count + 3),
        out_specs=vmem,
        out_shape=jax.ShapeDtypeStruct(own_rows.shape, own_rows.dtype),
    )(
        where,
        *parts,
        out_weights.reshape(count, head_width, out_weights.shape[1]),
        own_rows,
        gating_here.reshape(1, -1),
    )


def shards(
    incoming_states,
    transit_states,
    patch_sizes_list,
    outdated_lookups,
    outdated_contents,
    attention_projection,
    exit_projection,
    shift_and_scale,
    branch_gates,
):
    section_index = lax.axis_index("section")
    patches = patch_sizes_list.shape[0]
    biggest_patch_span = transit_states.shape[1]
    columns = incoming_states.shape[1]
    starts = jnp.cumsum(patch_sizes_list) - patch_sizes_list
    key_cache = outdated_lookups[0]
    value_cache = outdated_contents[0]
    qkv_weights = attention_projection[0]
    out_weights = exit_projection[0]
    shift_scale = shift_and_scale[0]
    gating_here = branch_gates[0]
    row_numbers = jnp.arange(biggest_patch_span)

    results = []
    entering_ext = jnp.concatenate(
        [incoming_states, jnp.zeros((biggest_patch_span, columns), jnp.bfloat16)], axis=0
    )
    section_zero = section_index == 0
    own_rows = jnp.where(section_zero, entering_ext[:biggest_patch_span], transit_states[0])
    own_rows = jnp.where(
        (row_numbers < pick_entry(patch_sizes_list, jnp.remainder(-section_index, patches)))[:, None],
        own_rows,
        0,
    )
    tables, own_rows = lax.optimization_barrier(
        (kernel_tables(patch_sizes_list, section_index), own_rows)
    )
    row_parts = [own_rows] + across_chips(own_rows)
    for turn_number in range(patches):
        where = tables[turn_number]
        rows_here = with_partner(row_parts)
        if turn_number + 1 < patches:
            entry_patch = lax.dynamic_slice_in_dim(
                entering_ext, starts[turn_number + 1], biggest_patch_span, 0
            )
            entry_patch = jnp.where(
                (row_numbers < patch_sizes_list[turn_number + 1])[:, None], entry_patch, 0
            )
            entry_patch, rows_here = lax.optimization_barrier((entry_patch, rows_here))
            entry_parts = [entry_patch] + across_chips_first_section(entry_patch)
        head_rows, key_cache, value_cache = attend_block(
            rows_here,
            shift_scale,
            qkv_weights,
            key_cache,
            value_cache,
            where,
            turn_number > 0,
        )
        updated = leave_block(
            with_partner([head_rows] + across_chips(head_rows)),
            out_weights,
            row_parts[0],
            gating_here,
            where,
        )
        results.append(updated)
        if turn_number + 1 < patches:
            arrived = to_next_section(updated)
            row_parts = [
                jnp.where(section_zero, entry, passed) for entry, passed in zip(entry_parts, arrived)
            ]
    return jnp.stack(results)[:, None]


def solution(mesh):
    return jax.shard_map(
        shards,
        mesh=mesh,
        in_specs=(
            P("groups", "seq"),
            P("section", "groups", "seq"),
            P("groups"),
            P("section", "seq", "groups", None),
            P("section", "seq", "groups", None),
            P("section", None, "seq"),
            P("section", None, "seq"),
            P("section", None, None),
            P("section", "seq"),
        ),
        out_specs=P(None, "section", "groups", "seq"),
        check_vma=False,
    )
```

```python
import jax
import jax.numpy as jnp
from jax import lax
from jax.experimental import pallas as pl
from jax.experimental.pallas import tpu as pltpu
from jax.sharding import PartitionSpec as P

epsilon = 1e-06


def rms_norm(values):
    return values * lax.rsqrt(jnp.mean(values * values, axis=-1, keepdims=True) + epsilon)


def pick_entry(vector, position):
    return jnp.sum(jnp.where(jnp.arange(vector.shape[0]) == position, vector, 0))


def across_chips(block):
    count = lax.axis_size("seq")
    return [
        lax.ppermute(block, "seq", [(source, (source + step) % count) for source in range(count)])
        for step in range(2, count, 2)
    ]


def across_chips_first_section(block):
    count = lax.axis_size("seq")
    return [
        lax.ppermute(
            block, ("section", "seq"), [(source, (source + step) % count) for source in range(count)]
        )
        for step in range(2, count, 2)
    ]


def with_partner(parts):
    count = lax.axis_size("seq")
    to_partner = [(source, source ^ 1) for source in range(count)]
    return parts + [lax.ppermute(part, "seq", to_partner) for part in parts]


def to_next_section(block):
    sections = lax.axis_size("section")
    count = lax.axis_size("seq")
    return [
        lax.ppermute(
            block,
            ("section", "seq"),
            [
                (section * count + source, (section + 1) * count + (source + step) % count)
                for section in range(sections - 1)
                for source in range(count)
            ],
        )
        for step in range(0, count, 2)
    ]


def kernel_tables(patch_sizes_list, section_index):
    patches = patch_sizes_list.shape[0]
    count = lax.axis_size("seq")
    here = lax.axis_index("seq")
    chips = count // 2
    turn = lax.broadcasted_iota(jnp.int32, (patches, count + 2), 0)
    entry = lax.broadcasted_iota(jnp.int32, (patches, count + 2), 1) - 2
    patch_index = jnp.remainder(turn - section_index + patches, patches)
    patch_ids = jnp.arange(patches).reshape(1, 1, patches)
    sizes = patch_sizes_list.reshape(1, 1, patches)
    chosen = patch_ids == patch_index[:, :, None]
    patch_count = jnp.sum(jnp.where(chosen, sizes, 0), axis=-1)
    patch_start = jnp.sum(jnp.where(patch_ids < patch_index[:, :, None], sizes, 0), axis=-1)
    base = jnp.where(entry < chips, here, jnp.bitwise_xor(here, 1))
    sources = jnp.remainder(base - 2 * jnp.remainder(entry, chips) + count, count)
    return jnp.where(entry == -2, patch_start, jnp.where(entry == -1, patch_count, sources)).astype(
        jnp.int32
    )


def block_kernel(*refs):
    where_ref = refs[0]
    count = len(refs) - 9
    part_refs = refs[1 : 1 + count]
    scale_ref, weights_ref, keys_ref, values_ref = refs[1 + count : 5 + count]
    heads_ref, keys_out, values_out = refs[5 + count : 8 + count]
    shaped_ref = refs[8 + count]
    start = where_ref[0]
    patch_count = where_ref[1]
    head_dim = keys_ref.shape[2]
    seq_len = keys_ref.shape[1]
    span, width = part_refs[0].shape
    features = width * count

    @pl.when(pl.program_id(0) == 0)
    def _():
        parts = [part[...].astype(jnp.float32) for part in part_refs]
        row_mean = sum(jnp.sum(part, axis=-1, keepdims=True) for part in parts) / features
        centred = [part - row_mean for part in parts]
        spread = sum(jnp.sum(c * c, axis=-1, keepdims=True) for c in centred) / features
        inverse = lax.rsqrt(spread + epsilon)
        for part in range(count):
            slot = where_ref[2 + part]
            shift_scale = scale_ref[slot]
            shaped_ref[slot] = (
                (centred[part] * inverse) * (1.0 + shift_scale[1:2]) + shift_scale[0:1]
            ).astype(jnp.bfloat16)

    mixed = sum(
        jnp.dot(
            shaped_ref[slot],
            weights_ref[slot * width : (slot + 1) * width, :],
            preferred_element_type=jnp.float32,
        )
        for slot in range(count)
    )
    queries = rms_norm(mixed[:, :head_dim]).astype(jnp.bfloat16)
    fresh_keys = rms_norm(mixed[:, head_dim : 2 * head_dim]).astype(jnp.bfloat16)
    fresh_values = mixed[:, 2 * head_dim :].astype(jnp.bfloat16)
    rows = lax.broadcasted_iota(jnp.int32, (seq_len, span), 0)
    picks = lax.broadcasted_iota(jnp.int32, (seq_len, span), 1)
    placing = ((rows == picks + start) & (picks < patch_count)).astype(jnp.bfloat16)
    row_ids = lax.broadcasted_iota(jnp.int32, (seq_len, 1), 0)
    inside = (row_ids >= start) & (row_ids < start + patch_count)
    placed_keys = jnp.dot(placing, fresh_keys, preferred_element_type=jnp.float32)
    placed_values = jnp.dot(placing, fresh_values, preferred_element_type=jnp.float32)
    keys = jnp.where(inside, placed_keys.astype(jnp.bfloat16), keys_ref[0])
    values = jnp.where(inside, placed_values.astype(jnp.bfloat16), values_ref[0])
    keys_out[0] = keys
    values_out[0] = values
    scores = lax.dot_general(
        queries, keys, (((1,), (1,)), ((), ())), preferred_element_type=jnp.float32
    ) * head_dim ** (-0.5)
    expos = jnp.exp(scores)
    weights = (expos / jnp.sum(expos, axis=-1, keepdims=True)).astype(jnp.bfloat16)
    heads_ref[...] = jnp.dot(weights, values, preferred_element_type=jnp.float32).astype(
        jnp.bfloat16
    )


def attend_block(parts, shift_scale, qkv_weights, key_cache, value_cache, where, in_place):
    count = len(parts)
    span, width = parts[0].shape
    heads_here, seq_len, head_dim = key_cache.shape
    features = qkv_weights.shape[0]
    scale_blocks = jnp.transpose(shift_scale.reshape(2, count, width), (1, 0, 2))
    whole = lambda shape: pl.BlockSpec(shape, lambda h, where: (0,) * len(shape))
    cache_spec = pl.BlockSpec((1, seq_len, head_dim), lambda h, where: (h, 0, 0))
    grid_spec = pltpu.PrefetchScalarGridSpec(
        num_scalar_prefetch=1,
        grid=(heads_here,),
        in_specs=[whole((span, width)) for _ in parts]
        + [
            whole((count, 2, width)),
            pl.BlockSpec((features, 3 * head_dim), lambda h, where: (0, h)),
            cache_spec,
            cache_spec,
        ],
        out_specs=[
            pl.BlockSpec((span, head_dim), lambda h, where: (0, h)),
            cache_spec,
            cache_spec,
        ],
        scratch_shapes=[pltpu.VMEM((count, span, width), jnp.bfloat16)],
    )
    return pl.pallas_call(
        block_kernel,
        grid_spec=grid_spec,
        out_shape=[
            jax.ShapeDtypeStruct((span, heads_here * head_dim), jnp.bfloat16),
            jax.ShapeDtypeStruct(key_cache.shape, key_cache.dtype),
            jax.ShapeDtypeStruct(value_cache.shape, value_cache.dtype),
        ],
        input_output_aliases={count + 3: 1, count + 4: 2} if in_place else {},
        compiler_params=pltpu.CompilerParams(dimension_semantics=("arbitrary",)),
    )(where, *parts, scale_blocks, qkv_weights, key_cache, value_cache)


def exit_kernel(*refs):
    where_ref = refs[0]
    count = len(refs) - 5
    part_refs = refs[1 : 1 + count]
    weights_ref, own_ref, gate_ref = refs[1 + count : 4 + count]
    out_ref = refs[4 + count]
    patch_count = where_ref[1]
    projected = sum(
        jnp.dot(
            part_refs[part][...],
            weights_ref[where_ref[2 + part]],
            preferred_element_type=jnp.float32,
        )
        for part in range(count)
    )
    updated = own_ref[...].astype(jnp.float32) + gate_ref[...] * projected
    live = lax.broadcasted_iota(jnp.int32, updated.shape, 0) < patch_count
    out_ref[...] = jnp.where(live, updated, 0.0).astype(out_ref.dtype)


def leave_block(parts, out_weights, own_rows, gating_here, where):
    count = len(parts)
    span, head_width = parts[0].shape
    vmem = pl.BlockSpec(memory_space=pltpu.VMEM)
    smem = pl.BlockSpec(memory_space=pltpu.SMEM)
    return pl.pallas_call(
        exit_kernel,
        in_specs=[smem] + [vmem] * (count + 3),
        out_specs=vmem,
        out_shape=jax.ShapeDtypeStruct(own_rows.shape, own_rows.dtype),
    )(
        where,
        *parts,
        out_weights.reshape(count, head_width, out_weights.shape[1]),
        own_rows,
        gating_here.reshape(1, -1),
    )


def shards(
    incoming_states,
    transit_states,
    patch_sizes_list,
    outdated_lookups,
    outdated_contents,
    attention_projection,
    exit_projection,
    shift_and_scale,
    branch_gates,
):
    section_index = lax.axis_index("section")
    patches = patch_sizes_list.shape[0]
    biggest_patch_span = transit_states.shape[1]
    columns = incoming_states.shape[1]
    starts = jnp.cumsum(patch_sizes_list) - patch_sizes_list
    key_cache = outdated_lookups[0]
    value_cache = outdated_contents[0]
    qkv_weights = attention_projection[0]
    out_weights = exit_projection[0]
    shift_scale = shift_and_scale[0]
    gating_here = branch_gates[0]
    row_numbers = jnp.arange(biggest_patch_span)

    results = []
    entering_ext = jnp.concatenate(
        [incoming_states, jnp.zeros((biggest_patch_span, columns), jnp.bfloat16)], axis=0
    )
    section_zero = section_index == 0
    own_rows = jnp.where(section_zero, entering_ext[:biggest_patch_span], transit_states[0])
    own_rows = jnp.where(
        (row_numbers < pick_entry(patch_sizes_list, jnp.remainder(-section_index, patches)))[:, None],
        own_rows,
        0,
    )
    row_parts = [own_rows] + across_chips(own_rows)
    tables, row_parts = lax.optimization_barrier(
        (kernel_tables(patch_sizes_list, section_index), row_parts)
    )
    for turn_number in range(patches):
        where = tables[turn_number]
        head_rows, key_cache, value_cache = attend_block(
            with_partner(row_parts),
            shift_scale,
            qkv_weights,
            key_cache,
            value_cache,
            where,
            turn_number > 0,
        )
        updated = leave_block(
            with_partner([head_rows] + across_chips(head_rows)),
            out_weights,
            row_parts[0],
            gating_here,
            where,
        )
        results.append(updated)
        if turn_number + 1 < patches:
            entry_patch = lax.dynamic_slice_in_dim(
                entering_ext, starts[turn_number + 1], biggest_patch_span, 0
            )
            entry_patch = jnp.where(
                (row_numbers < patch_sizes_list[turn_number + 1])[:, None], entry_patch, 0
            )
            arrived = to_next_section(updated)
            entry_parts = [entry_patch] + across_chips_first_section(entry_patch)
            row_parts = [
                jnp.where(section_zero, entry, passed) for entry, passed in zip(entry_parts, arrived)
            ]
    return jnp.stack(results)[:, None]


def solution(mesh):
    return jax.shard_map(
        shards,
        mesh=mesh,
        in_specs=(
            P("groups", "seq"),
            P("section", "groups", "seq"),
            P("groups"),
            P("section", "seq", "groups", None),
            P("section", "seq", "groups", None),
            P("section", None, "seq"),
            P("section", None, "seq"),
            P("section", None, None),
            P("section", "seq"),
        ),
        out_specs=P(None, "section", "groups", "seq"),
        check_vma=False,
    )
```

```python
import jax
import jax.numpy as jnp
from jax import lax
from jax.experimental import pallas as pl
from jax.experimental.pallas import tpu as pltpu
from jax.sharding import PartitionSpec as P

epsilon = 1e-06


def rms_norm(values):
    return values * lax.rsqrt(jnp.mean(values * values, axis=-1, keepdims=True) + epsilon)


def pick_entry(vector, position):
    return jnp.sum(jnp.where(jnp.arange(vector.shape[0]) == position, vector, 0))


def across_chips(block):
    count = lax.axis_size("seq")
    return [
        lax.ppermute(block, "seq", [(source, (source + step) % count) for source in range(count)])
        for step in range(2, count, 2)
    ]


def across_chips_first_section(block):
    count = lax.axis_size("seq")
    return [
        lax.ppermute(
            block, ("section", "seq"), [(source, (source + step) % count) for source in range(count)]
        )
        for step in range(2, count, 2)
    ]


def with_partner(parts):
    count = lax.axis_size("seq")
    to_partner = [(source, source ^ 1) for source in range(count)]
    return parts + [lax.ppermute(part, "seq", to_partner) for part in parts]


def to_next_section(block):
    sections = lax.axis_size("section")
    count = lax.axis_size("seq")
    return [
        lax.ppermute(
            block,
            ("section", "seq"),
            [
                (section * count + source, (section + 1) * count + (source + step) % count)
                for section in range(sections - 1)
                for source in range(count)
            ],
        )
        for step in range(0, count, 2)
    ]


def kernel_tables(patch_sizes_list, section_index):
    patches = patch_sizes_list.shape[0]
    count = lax.axis_size("seq")
    here = lax.axis_index("seq")
    chips = count // 2
    turn = lax.broadcasted_iota(jnp.int32, (patches, count + 2), 0)
    entry = lax.broadcasted_iota(jnp.int32, (patches, count + 2), 1) - 2
    patch_index = jnp.remainder(turn - section_index + patches, patches)
    patch_ids = jnp.arange(patches).reshape(1, 1, patches)
    sizes = patch_sizes_list.reshape(1, 1, patches)
    chosen = patch_ids == patch_index[:, :, None]
    patch_count = jnp.sum(jnp.where(chosen, sizes, 0), axis=-1)
    patch_start = jnp.sum(jnp.where(patch_ids < patch_index[:, :, None], sizes, 0), axis=-1)
    base = jnp.where(entry < chips, here, jnp.bitwise_xor(here, 1))
    sources = jnp.remainder(base - 2 * jnp.remainder(entry, chips) + count, count)
    return jnp.where(entry == -2, patch_start, jnp.where(entry == -1, patch_count, sources)).astype(
        jnp.int32
    )


def block_kernel(*refs):
    where_ref = refs[0]
    count = len(refs) - 9
    part_refs = refs[1 : 1 + count]
    scale_ref, weights_ref, keys_ref, values_ref = refs[1 + count : 5 + count]
    heads_ref, keys_out, values_out = refs[5 + count : 8 + count]
    shaped_ref = refs[8 + count]
    start = where_ref[0]
    patch_count = where_ref[1]
    head_dim = keys_ref.shape[2]
    seq_len = keys_ref.shape[1]
    span, width = part_refs[0].shape
    features = width * count

    @pl.when(pl.program_id(0) == 0)
    def _():
        parts = [part[...].astype(jnp.float32) for part in part_refs]
        row_mean = sum(jnp.sum(part, axis=-1, keepdims=True) for part in parts) / features
        centred = [part - row_mean for part in parts]
        spread = sum(jnp.sum(c * c, axis=-1, keepdims=True) for c in centred) / features
        inverse = lax.rsqrt(spread + epsilon)
        for part in range(count):
            slot = where_ref[2 + part]
            shift_scale = scale_ref[slot]
            shaped_ref[slot] = (
                (centred[part] * inverse) * (1.0 + shift_scale[1:2]) + shift_scale[0:1]
            ).astype(jnp.bfloat16)

    mixed = sum(
        jnp.dot(
            shaped_ref[slot],
            weights_ref[slot * width : (slot + 1) * width, :],
            preferred_element_type=jnp.float32,
        )
        for slot in range(count)
    )
    queries = rms_norm(mixed[:, :head_dim]).astype(jnp.bfloat16)
    fresh_keys = rms_norm(mixed[:, head_dim : 2 * head_dim]).astype(jnp.bfloat16)
    fresh_values = mixed[:, 2 * head_dim :].astype(jnp.bfloat16)
    rows = lax.broadcasted_iota(jnp.int32, (seq_len, span), 0)
    picks = lax.broadcasted_iota(jnp.int32, (seq_len, span), 1)
    placing = ((rows == picks + start) & (picks < patch_count)).astype(jnp.bfloat16)
    row_ids = lax.broadcasted_iota(jnp.int32, (seq_len, 1), 0)
    inside = (row_ids >= start) & (row_ids < start + patch_count)
    placed_keys = jnp.dot(placing, fresh_keys, preferred_element_type=jnp.float32)
    placed_values = jnp.dot(placing, fresh_values, preferred_element_type=jnp.float32)
    keys = jnp.where(inside, placed_keys.astype(jnp.bfloat16), keys_ref[0])
    values = jnp.where(inside, placed_values.astype(jnp.bfloat16), values_ref[0])
    keys_out[0] = keys
    values_out[0] = values
    scores = lax.dot_general(
        queries, keys, (((1,), (1,)), ((), ())), preferred_element_type=jnp.float32
    ) * head_dim ** (-0.5)
    expos = jnp.exp(scores)
    weights = (expos / jnp.sum(expos, axis=-1, keepdims=True)).astype(jnp.bfloat16)
    heads_ref[...] = jnp.dot(weights, values, preferred_element_type=jnp.float32).astype(
        jnp.bfloat16
    )


def attend_block(parts, shift_scale, qkv_weights, key_cache, value_cache, where, in_place):
    count = len(parts)
    span, width = parts[0].shape
    heads_here, seq_len, head_dim = key_cache.shape
    features = qkv_weights.shape[0]
    scale_blocks = jnp.transpose(shift_scale.reshape(2, count, width), (1, 0, 2))
    whole = lambda shape: pl.BlockSpec(shape, lambda h, where: (0,) * len(shape))
    cache_spec = pl.BlockSpec((1, seq_len, head_dim), lambda h, where: (h, 0, 0))
    grid_spec = pltpu.PrefetchScalarGridSpec(
        num_scalar_prefetch=1,
        grid=(heads_here,),
        in_specs=[whole((span, width)) for _ in parts]
        + [
            whole((count, 2, width)),
            pl.BlockSpec((features, 3 * head_dim), lambda h, where: (0, h)),
            cache_spec,
            cache_spec,
        ],
        out_specs=[
            pl.BlockSpec((span, head_dim), lambda h, where: (0, h)),
            cache_spec,
            cache_spec,
        ],
        scratch_shapes=[pltpu.VMEM((count, span, width), jnp.bfloat16)],
    )
    return pl.pallas_call(
        block_kernel,
        grid_spec=grid_spec,
        out_shape=[
            jax.ShapeDtypeStruct((span, heads_here * head_dim), jnp.bfloat16),
            jax.ShapeDtypeStruct(key_cache.shape, key_cache.dtype),
            jax.ShapeDtypeStruct(value_cache.shape, value_cache.dtype),
        ],
        input_output_aliases={count + 3: 1, count + 4: 2} if in_place else {},
        compiler_params=pltpu.CompilerParams(dimension_semantics=("arbitrary",)),
    )(where, *parts, scale_blocks, qkv_weights, key_cache, value_cache)


def exit_kernel(*refs):
    where_ref = refs[0]
    count = len(refs) - 5
    part_refs = refs[1 : 1 + count]
    weights_ref, own_ref, gate_ref = refs[1 + count : 4 + count]
    out_ref = refs[4 + count]
    patch_count = where_ref[1]
    projected = sum(
        jnp.dot(
            part_refs[part][...],
            weights_ref[where_ref[2 + part]],
            preferred_element_type=jnp.float32,
        )
        for part in range(count)
    )
    updated = own_ref[...].astype(jnp.float32) + gate_ref[...] * projected
    live = lax.broadcasted_iota(jnp.int32, updated.shape, 0) < patch_count
    out_ref[...] = jnp.where(live, updated, 0.0).astype(out_ref.dtype)


def leave_block(parts, out_weights, own_rows, gating_here, where):
    count = len(parts)
    span, head_width = parts[0].shape
    vmem = pl.BlockSpec(memory_space=pltpu.VMEM)
    smem = pl.BlockSpec(memory_space=pltpu.SMEM)
    return pl.pallas_call(
        exit_kernel,
        in_specs=[smem] + [vmem] * (count + 3),
        out_specs=vmem,
        out_shape=jax.ShapeDtypeStruct(own_rows.shape, own_rows.dtype),
    )(
        where,
        *parts,
        out_weights.reshape(count, head_width, out_weights.shape[1]),
        own_rows,
        gating_here.reshape(1, -1),
    )


def shards(
    incoming_states,
    transit_states,
    patch_sizes_list,
    outdated_lookups,
    outdated_contents,
    attention_projection,
    exit_projection,
    shift_and_scale,
    branch_gates,
):
    section_index = lax.axis_index("section")
    patches = patch_sizes_list.shape[0]
    biggest_patch_span = transit_states.shape[1]
    columns = incoming_states.shape[1]
    starts = jnp.cumsum(patch_sizes_list) - patch_sizes_list
    key_cache = outdated_lookups[0]
    value_cache = outdated_contents[0]
    qkv_weights = attention_projection[0]
    out_weights = exit_projection[0]
    shift_scale = shift_and_scale[0]
    gating_here = branch_gates[0]
    row_numbers = jnp.arange(biggest_patch_span)

    results = []
    entering_ext = jnp.concatenate(
        [incoming_states, jnp.zeros((biggest_patch_span, columns), jnp.bfloat16)], axis=0
    )
    section_zero = section_index == 0
    own_rows = jnp.where(section_zero, entering_ext[:biggest_patch_span], transit_states[0])
    own_rows = jnp.where(
        (row_numbers < pick_entry(patch_sizes_list, jnp.remainder(-section_index, patches)))[:, None],
        own_rows,
        0,
    )
    tables, own_rows = lax.optimization_barrier(
        (kernel_tables(patch_sizes_list, section_index), own_rows)
    )
    row_parts = [own_rows] + across_chips(own_rows)
    for turn_number in range(patches):
        where = tables[turn_number]
        rows_here = with_partner(row_parts)
        if turn_number == 0:
            later_entries, rows_here = lax.optimization_barrier((incoming_states, rows_here))
            entering_across = [
                jnp.concatenate(
                    [rows, jnp.zeros((biggest_patch_span, columns), jnp.bfloat16)], axis=0
                )
                for rows in across_chips_first_section(later_entries)
            ]
        head_rows, key_cache, value_cache = attend_block(
            rows_here,
            shift_scale,
            qkv_weights,
            key_cache,
            value_cache,
            where,
            turn_number > 0,
        )
        updated = leave_block(
            with_partner([head_rows] + across_chips(head_rows)),
            out_weights,
            row_parts[0],
            gating_here,
            where,
        )
        results.append(updated)
        if turn_number + 1 < patches:
            entry_live = (row_numbers < patch_sizes_list[turn_number + 1])[:, None]
            entry_parts = [
                jnp.where(
                    entry_live,
                    lax.dynamic_slice_in_dim(
                        rows, starts[turn_number + 1], biggest_patch_span, 0
                    ),
                    0,
                )
                for rows in [entering_ext] + entering_across
            ]
            arrived = to_next_section(updated)
            row_parts = [
                jnp.where(section_zero, entry, passed) for entry, passed in zip(entry_parts, arrived)
            ]
    return jnp.stack(results)[:, None]


def solution(mesh):
    return jax.shard_map(
        shards,
        mesh=mesh,
        in_specs=(
            P("groups", "seq"),
            P("section", "groups", "seq"),
            P("groups"),
            P("section", "seq", "groups", None),
            P("section", "seq", "groups", None),
            P("section", None, "seq"),
            P("section", None, "seq"),
            P("section", None, None),
            P("section", "seq"),
        ),
        out_specs=P(None, "section", "groups", "seq"),
        check_vma=False,
    )
```

```python
import jax
import jax.numpy as jnp
from jax import lax
from jax.experimental import pallas as pl
from jax.experimental.pallas import tpu as pltpu
from jax.sharding import PartitionSpec as P

epsilon = 1e-06


def rms_norm(values):
    return values * lax.rsqrt(jnp.mean(values * values, axis=-1, keepdims=True) + epsilon)


def pick_entry(vector, position):
    return jnp.sum(jnp.where(jnp.arange(vector.shape[0]) == position, vector, 0))


def across_chips(block):
    count = lax.axis_size("seq")
    return [
        lax.ppermute(block, "seq", [(source, (source + step) % count) for source in range(count)])
        for step in range(2, count, 2)
    ]


def across_chips_first_section(block):
    count = lax.axis_size("seq")
    return [
        lax.ppermute(
            block, ("section", "seq"), [(source, (source + step) % count) for source in range(count)]
        )
        for step in range(2, count, 2)
    ]


def with_partner(parts):
    count = lax.axis_size("seq")
    to_partner = [(source, source ^ 1) for source in range(count)]
    return parts + [lax.ppermute(part, "seq", to_partner) for part in parts]


def to_next_section(block):
    sections = lax.axis_size("section")
    count = lax.axis_size("seq")
    return [
        lax.ppermute(
            block,
            ("section", "seq"),
            [
                (section * count + source, (section + 1) * count + (source + step) % count)
                for section in range(sections - 1)
                for source in range(count)
            ],
        )
        for step in range(0, count, 2)
    ]


def kernel_tables(patch_sizes_list, section_index):
    patches = patch_sizes_list.shape[0]
    count = lax.axis_size("seq")
    here = lax.axis_index("seq")
    chips = count // 2
    turn = lax.broadcasted_iota(jnp.int32, (patches, count + 2), 0)
    entry = lax.broadcasted_iota(jnp.int32, (patches, count + 2), 1) - 2
    patch_index = jnp.remainder(turn - section_index + patches, patches)
    patch_ids = jnp.arange(patches).reshape(1, 1, patches)
    sizes = patch_sizes_list.reshape(1, 1, patches)
    chosen = patch_ids == patch_index[:, :, None]
    patch_count = jnp.sum(jnp.where(chosen, sizes, 0), axis=-1)
    patch_start = jnp.sum(jnp.where(patch_ids < patch_index[:, :, None], sizes, 0), axis=-1)
    base = jnp.where(entry < chips, here, jnp.bitwise_xor(here, 1))
    sources = jnp.remainder(base - 2 * jnp.remainder(entry, chips) + count, count)
    return jnp.where(entry == -2, patch_start, jnp.where(entry == -1, patch_count, sources)).astype(
        jnp.int32
    )


def block_kernel(*refs):
    where_ref = refs[0]
    count = len(refs) - 10
    part_refs = refs[1 : 1 + count]
    scale_ref, weights_ref, keys_ref, values_ref = refs[1 + count : 5 + count]
    heads_ref, keys_out, values_out = refs[5 + count : 8 + count]
    shaped_ref, staging_ref = refs[8 + count :]
    start = where_ref[0]
    patch_count = where_ref[1]
    head_dim = keys_ref.shape[2]
    seq_len = keys_ref.shape[1]
    span, width = part_refs[0].shape
    features = width * count

    @pl.when(pl.program_id(0) == 0)
    def _():
        parts = [part[...].astype(jnp.float32) for part in part_refs]
        row_mean = sum(jnp.sum(part, axis=-1, keepdims=True) for part in parts) / features
        centred = [part - row_mean for part in parts]
        spread = sum(jnp.sum(c * c, axis=-1, keepdims=True) for c in centred) / features
        inverse = lax.rsqrt(spread + epsilon)
        for part in range(count):
            slot = where_ref[2 + part]
            shift_scale = scale_ref[slot]
            shaped_ref[slot] = (
                (centred[part] * inverse) * (1.0 + shift_scale[1:2]) + shift_scale[0:1]
            ).astype(jnp.bfloat16)

    mixed = sum(
        jnp.dot(
            shaped_ref[slot],
            weights_ref[slot * width : (slot + 1) * width, :],
            preferred_element_type=jnp.float32,
        )
        for slot in range(count)
    )
    queries = rms_norm(mixed[:, :head_dim]).astype(jnp.bfloat16)
    fresh_keys = rms_norm(mixed[:, head_dim : 2 * head_dim]).astype(jnp.bfloat16)
    fresh_values = mixed[:, 2 * head_dim :].astype(jnp.bfloat16)
    live = lax.broadcasted_iota(jnp.int32, (span, 1), 0) < patch_count
    staging_ref[:seq_len] = keys_ref[0].astype(jnp.float32)
    window = staging_ref[pl.ds(start, span)]
    staging_ref[pl.ds(start, span)] = jnp.where(live, fresh_keys.astype(jnp.float32), window)
    keys = staging_ref[:seq_len].astype(jnp.bfloat16)
    staging_ref[:seq_len] = values_ref[0].astype(jnp.float32)
    window = staging_ref[pl.ds(start, span)]
    staging_ref[pl.ds(start, span)] = jnp.where(live, fresh_values.astype(jnp.float32), window)
    values = staging_ref[:seq_len].astype(jnp.bfloat16)
    keys_out[0] = keys
    values_out[0] = values
    scores = lax.dot_general(
        queries, keys, (((1,), (1,)), ((), ())), preferred_element_type=jnp.float32
    ) * head_dim ** (-0.5)
    expos = jnp.exp(scores)
    weights = (expos / jnp.sum(expos, axis=-1, keepdims=True)).astype(jnp.bfloat16)
    heads_ref[...] = jnp.dot(weights, values, preferred_element_type=jnp.float32).astype(
        jnp.bfloat16
    )


def attend_block(parts, shift_scale, qkv_weights, key_cache, value_cache, where, in_place):
    count = len(parts)
    span, width = parts[0].shape
    heads_here, seq_len, head_dim = key_cache.shape
    features = qkv_weights.shape[0]
    scale_blocks = jnp.transpose(shift_scale.reshape(2, count, width), (1, 0, 2))
    whole = lambda shape: pl.BlockSpec(shape, lambda h, where: (0,) * len(shape))
    cache_spec = pl.BlockSpec((1, seq_len, head_dim), lambda h, where: (h, 0, 0))
    grid_spec = pltpu.PrefetchScalarGridSpec(
        num_scalar_prefetch=1,
        grid=(heads_here,),
        in_specs=[whole((span, width)) for _ in parts]
        + [
            whole((count, 2, width)),
            pl.BlockSpec((features, 3 * head_dim), lambda h, where: (0, h)),
            cache_spec,
            cache_spec,
        ],
        out_specs=[
            pl.BlockSpec((span, head_dim), lambda h, where: (0, h)),
            cache_spec,
            cache_spec,
        ],
        scratch_shapes=[
            pltpu.VMEM((count, span, width), jnp.bfloat16),
            pltpu.VMEM((seq_len + span, head_dim), jnp.float32),
        ],
    )
    return pl.pallas_call(
        block_kernel,
        grid_spec=grid_spec,
        out_shape=[
            jax.ShapeDtypeStruct((span, heads_here * head_dim), jnp.bfloat16),
            jax.ShapeDtypeStruct(key_cache.shape, key_cache.dtype),
            jax.ShapeDtypeStruct(value_cache.shape, value_cache.dtype),
        ],
        input_output_aliases={count + 3: 1, count + 4: 2} if in_place else {},
        compiler_params=pltpu.CompilerParams(dimension_semantics=("arbitrary",)),
    )(where, *parts, scale_blocks, qkv_weights, key_cache, value_cache)


def exit_kernel(*refs):
    where_ref = refs[0]
    count = len(refs) - 5
    part_refs = refs[1 : 1 + count]
    weights_ref, own_ref, gate_ref = refs[1 + count : 4 + count]
    out_ref = refs[4 + count]
    patch_count = where_ref[1]
    projected = sum(
        jnp.dot(
            part_refs[part][...],
            weights_ref[where_ref[2 + part]],
            preferred_element_type=jnp.float32,
        )
        for part in range(count)
    )
    updated = own_ref[...].astype(jnp.float32) + gate_ref[...] * projected
    live = lax.broadcasted_iota(jnp.int32, updated.shape, 0) < patch_count
    out_ref[...] = jnp.where(live, updated, 0.0).astype(out_ref.dtype)


def leave_block(parts, out_weights, own_rows, gating_here, where):
    count = len(parts)
    span, head_width = parts[0].shape
    vmem = pl.BlockSpec(memory_space=pltpu.VMEM)
    smem = pl.BlockSpec(memory_space=pltpu.SMEM)
    return pl.pallas_call(
        exit_kernel,
        in_specs=[smem] + [vmem] * (count + 3),
        out_specs=vmem,
        out_shape=jax.ShapeDtypeStruct(own_rows.shape, own_rows.dtype),
    )(
        where,
        *parts,
        out_weights.reshape(count, head_width, out_weights.shape[1]),
        own_rows,
        gating_here.reshape(1, -1),
    )


def shards(
    incoming_states,
    transit_states,
    patch_sizes_list,
    outdated_lookups,
    outdated_contents,
    attention_projection,
    exit_projection,
    shift_and_scale,
    branch_gates,
):
    section_index = lax.axis_index("section")
    patches = patch_sizes_list.shape[0]
    biggest_patch_span = transit_states.shape[1]
    columns = incoming_states.shape[1]
    starts = jnp.cumsum(patch_sizes_list) - patch_sizes_list
    key_cache = outdated_lookups[0]
    value_cache = outdated_contents[0]
    qkv_weights = attention_projection[0]
    out_weights = exit_projection[0]
    shift_scale = shift_and_scale[0]
    gating_here = branch_gates[0]
    row_numbers = jnp.arange(biggest_patch_span)

    results = []
    entering_ext = jnp.concatenate(
        [incoming_states, jnp.zeros((biggest_patch_span, columns), jnp.bfloat16)], axis=0
    )
    section_zero = section_index == 0
    own_rows = jnp.where(section_zero, entering_ext[:biggest_patch_span], transit_states[0])
    own_rows = jnp.where(
        (row_numbers < pick_entry(patch_sizes_list, jnp.remainder(-section_index, patches)))[:, None],
        own_rows,
        0,
    )
    row_parts = [own_rows] + across_chips(own_rows)
    tables, row_parts = lax.optimization_barrier(
        (kernel_tables(patch_sizes_list, section_index), row_parts)
    )
    for turn_number in range(patches):
        where = tables[turn_number]
        head_rows, key_cache, value_cache = attend_block(
            with_partner(row_parts),
            shift_scale,
            qkv_weights,
            key_cache,
            value_cache,
            where,
            turn_number > 0,
        )
        updated = leave_block(
            with_partner([head_rows] + across_chips(head_rows)),
            out_weights,
            row_parts[0],
            gating_here,
            where,
        )
        results.append(updated)
        if turn_number + 1 < patches:
            entry_patch = lax.dynamic_slice_in_dim(
                entering_ext, starts[turn_number + 1], biggest_patch_span, 0
            )
            entry_patch = jnp.where(
                (row_numbers < patch_sizes_list[turn_number + 1])[:, None], entry_patch, 0
            )
            arrived = to_next_section(updated)
            entry_parts = [entry_patch] + across_chips_first_section(entry_patch)
            row_parts = [
                jnp.where(section_zero, entry, passed) for entry, passed in zip(entry_parts, arrived)
            ]
    return jnp.stack(results)[:, None]


def solution(mesh):
    return jax.shard_map(
        shards,
        mesh=mesh,
        in_specs=(
            P("groups", "seq"),
            P("section", "groups", "seq"),
            P("groups"),
            P("section", "seq", "groups", None),
            P("section", "seq", "groups", None),
            P("section", None, "seq"),
            P("section", None, "seq"),
            P("section", None, None),
            P("section", "seq"),
        ),
        out_specs=P(None, "section", "groups", "seq"),
        check_vma=False,
    )
```

```python
import jax
import jax.numpy as jnp
from jax import lax
from jax.experimental import pallas as pl
from jax.experimental.pallas import tpu as pltpu
from jax.sharding import PartitionSpec as P

epsilon = 1e-06


def rms_norm(values):
    return values * lax.rsqrt(jnp.mean(values * values, axis=-1, keepdims=True) + epsilon)


def pick_entry(vector, position):
    return jnp.sum(jnp.where(jnp.arange(vector.shape[0]) == position, vector, 0))


def across_chips(block):
    count = lax.axis_size("seq")
    return [
        lax.ppermute(block, "seq", [(source, (source + step) % count) for source in range(count)])
        for step in range(2, count, 2)
    ]


def across_chips_first_section(block):
    count = lax.axis_size("seq")
    return [
        lax.ppermute(
            block, ("section", "seq"), [(source, (source + step) % count) for source in range(count)]
        )
        for step in range(2, count, 2)
    ]


def with_partner(parts):
    count = lax.axis_size("seq")
    to_partner = [(source, source ^ 1) for source in range(count)]
    return parts + [lax.ppermute(part, "seq", to_partner) for part in parts]


def to_next_section(block):
    sections = lax.axis_size("section")
    count = lax.axis_size("seq")
    return [
        lax.ppermute(
            block,
            ("section", "seq"),
            [
                (section * count + source, (section + 1) * count + (source + step) % count)
                for section in range(sections - 1)
                for source in range(count)
            ],
        )
        for step in range(0, count, 2)
    ]


def kernel_tables(patch_sizes_list, section_index):
    patches = patch_sizes_list.shape[0]
    count = lax.axis_size("seq")
    here = lax.axis_index("seq")
    chips = count // 2
    turn = lax.broadcasted_iota(jnp.int32, (patches, count + 2), 0)
    entry = lax.broadcasted_iota(jnp.int32, (patches, count + 2), 1) - 2
    patch_index = jnp.remainder(turn - section_index + patches, patches)
    patch_ids = jnp.arange(patches).reshape(1, 1, patches)
    sizes = patch_sizes_list.reshape(1, 1, patches)
    chosen = patch_ids == patch_index[:, :, None]
    patch_count = jnp.sum(jnp.where(chosen, sizes, 0), axis=-1)
    patch_start = jnp.sum(jnp.where(patch_ids < patch_index[:, :, None], sizes, 0), axis=-1)
    base = jnp.where(entry < chips, here, jnp.bitwise_xor(here, 1))
    sources = jnp.remainder(base - 2 * jnp.remainder(entry, chips) + count, count)
    return jnp.where(entry == -2, patch_start, jnp.where(entry == -1, patch_count, sources)).astype(
        jnp.int32
    )


def block_kernel(*refs):
    where_ref = refs[0]
    count = len(refs) - 11
    part_refs = refs[1 : 1 + count]
    scale_ref, weights_ref, keys_ref, values_ref = refs[1 + count : 5 + count]
    heads_ref, keys_out, values_out = refs[5 + count : 8 + count]
    shaped_ref, staging_ref, value_staging_ref = refs[8 + count :]
    start = where_ref[0]
    patch_count = where_ref[1]
    head_dim = keys_ref.shape[2]
    seq_len = keys_ref.shape[1]
    span, width = part_refs[0].shape
    features = width * count

    @pl.when(pl.program_id(0) == 0)
    def _():
        parts = [part[...].astype(jnp.float32) for part in part_refs]
        row_mean = sum(jnp.sum(part, axis=-1, keepdims=True) for part in parts) / features
        centred = [part - row_mean for part in parts]
        spread = sum(jnp.sum(c * c, axis=-1, keepdims=True) for c in centred) / features
        inverse = lax.rsqrt(spread + epsilon)
        for part in range(count):
            slot = where_ref[2 + part]
            shift_scale = scale_ref[slot]
            shaped_ref[slot] = (
                (centred[part] * inverse) * (1.0 + shift_scale[1:2]) + shift_scale[0:1]
            ).astype(jnp.bfloat16)

    mixed = sum(
        jnp.dot(
            shaped_ref[slot],
            weights_ref[slot * width : (slot + 1) * width, :],
            preferred_element_type=jnp.float32,
        )
        for slot in range(count)
    )
    queries = rms_norm(mixed[:, :head_dim]).astype(jnp.bfloat16)
    fresh_keys = rms_norm(mixed[:, head_dim : 2 * head_dim]).astype(jnp.bfloat16)
    fresh_values = mixed[:, 2 * head_dim :].astype(jnp.bfloat16)
    live = lax.broadcasted_iota(jnp.int32, (span, 1), 0) < patch_count
    staging_ref[:seq_len] = keys_ref[0].astype(jnp.float32)
    window = staging_ref[pl.ds(start, span)]
    staging_ref[pl.ds(start, span)] = jnp.where(live, fresh_keys.astype(jnp.float32), window)
    keys = staging_ref[:seq_len].astype(jnp.bfloat16)
    value_staging_ref[:seq_len] = values_ref[0].astype(jnp.float32)
    window = value_staging_ref[pl.ds(start, span)]
    value_staging_ref[pl.ds(start, span)] = jnp.where(
        live, fresh_values.astype(jnp.float32), window
    )
    values = value_staging_ref[:seq_len].astype(jnp.bfloat16)
    keys_out[0] = keys
    values_out[0] = values
    scores = lax.dot_general(
        queries, keys, (((1,), (1,)), ((), ())), preferred_element_type=jnp.float32
    ) * head_dim ** (-0.5)
    expos = jnp.exp(scores)
    weights = (expos / jnp.sum(expos, axis=-1, keepdims=True)).astype(jnp.bfloat16)
    heads_ref[...] = jnp.dot(weights, values, preferred_element_type=jnp.float32).astype(
        jnp.bfloat16
    )


def attend_block(parts, shift_scale, qkv_weights, key_cache, value_cache, where, in_place):
    count = len(parts)
    span, width = parts[0].shape
    heads_here, seq_len, head_dim = key_cache.shape
    features = qkv_weights.shape[0]
    scale_blocks = jnp.transpose(shift_scale.reshape(2, count, width), (1, 0, 2))
    whole = lambda shape: pl.BlockSpec(shape, lambda h, where: (0,) * len(shape))
    cache_spec = pl.BlockSpec((1, seq_len, head_dim), lambda h, where: (h, 0, 0))
    grid_spec = pltpu.PrefetchScalarGridSpec(
        num_scalar_prefetch=1,
        grid=(heads_here,),
        in_specs=[whole((span, width)) for _ in parts]
        + [
            whole((count, 2, width)),
            pl.BlockSpec((features, 3 * head_dim), lambda h, where: (0, h)),
            cache_spec,
            cache_spec,
        ],
        out_specs=[
            pl.BlockSpec((span, head_dim), lambda h, where: (0, h)),
            cache_spec,
            cache_spec,
        ],
        scratch_shapes=[
            pltpu.VMEM((count, span, width), jnp.bfloat16),
            pltpu.VMEM((seq_len + span, head_dim), jnp.float32),
            pltpu.VMEM((seq_len + span, head_dim), jnp.float32),
        ],
    )
    return pl.pallas_call(
        block_kernel,
        grid_spec=grid_spec,
        out_shape=[
            jax.ShapeDtypeStruct((span, heads_here * head_dim), jnp.bfloat16),
            jax.ShapeDtypeStruct(key_cache.shape, key_cache.dtype),
            jax.ShapeDtypeStruct(value_cache.shape, value_cache.dtype),
        ],
        input_output_aliases={count + 3: 1, count + 4: 2} if in_place else {},
        compiler_params=pltpu.CompilerParams(dimension_semantics=("arbitrary",)),
    )(where, *parts, scale_blocks, qkv_weights, key_cache, value_cache)


def exit_kernel(*refs):
    where_ref = refs[0]
    count = len(refs) - 5
    part_refs = refs[1 : 1 + count]
    weights_ref, own_ref, gate_ref = refs[1 + count : 4 + count]
    out_ref = refs[4 + count]
    patch_count = where_ref[1]
    projected = sum(
        jnp.dot(
            part_refs[part][...],
            weights_ref[where_ref[2 + part]],
            preferred_element_type=jnp.float32,
        )
        for part in range(count)
    )
    updated = own_ref[...].astype(jnp.float32) + gate_ref[...] * projected
    live = lax.broadcasted_iota(jnp.int32, updated.shape, 0) < patch_count
    out_ref[...] = jnp.where(live, updated, 0.0).astype(out_ref.dtype)


def leave_block(parts, out_weights, own_rows, gating_here, where):
    count = len(parts)
    span, head_width = parts[0].shape
    vmem = pl.BlockSpec(memory_space=pltpu.VMEM)
    smem = pl.BlockSpec(memory_space=pltpu.SMEM)
    return pl.pallas_call(
        exit_kernel,
        in_specs=[smem] + [vmem] * (count + 3),
        out_specs=vmem,
        out_shape=jax.ShapeDtypeStruct(own_rows.shape, own_rows.dtype),
    )(
        where,
        *parts,
        out_weights.reshape(count, head_width, out_weights.shape[1]),
        own_rows,
        gating_here.reshape(1, -1),
    )


def shards(
    incoming_states,
    transit_states,
    patch_sizes_list,
    outdated_lookups,
    outdated_contents,
    attention_projection,
    exit_projection,
    shift_and_scale,
    branch_gates,
):
    section_index = lax.axis_index("section")
    patches = patch_sizes_list.shape[0]
    biggest_patch_span = transit_states.shape[1]
    columns = incoming_states.shape[1]
    starts = jnp.cumsum(patch_sizes_list) - patch_sizes_list
    key_cache = outdated_lookups[0]
    value_cache = outdated_contents[0]
    qkv_weights = attention_projection[0]
    out_weights = exit_projection[0]
    shift_scale = shift_and_scale[0]
    gating_here = branch_gates[0]
    row_numbers = jnp.arange(biggest_patch_span)

    results = []
    entering_ext = jnp.concatenate(
        [incoming_states, jnp.zeros((biggest_patch_span, columns), jnp.bfloat16)], axis=0
    )
    section_zero = section_index == 0
    own_rows = jnp.where(section_zero, entering_ext[:biggest_patch_span], transit_states[0])
    own_rows = jnp.where(
        (row_numbers < pick_entry(patch_sizes_list, jnp.remainder(-section_index, patches)))[:, None],
        own_rows,
        0,
    )
    row_parts = [own_rows] + across_chips(own_rows)
    tables, row_parts = lax.optimization_barrier(
        (kernel_tables(patch_sizes_list, section_index), row_parts)
    )
    for turn_number in range(patches):
        where = tables[turn_number]
        head_rows, key_cache, value_cache = attend_block(
            with_partner(row_parts),
            shift_scale,
            qkv_weights,
            key_cache,
            value_cache,
            where,
            turn_number > 0,
        )
        updated = leave_block(
            with_partner([head_rows] + across_chips(head_rows)),
            out_weights,
            row_parts[0],
            gating_here,
            where,
        )
        results.append(updated)
        if turn_number + 1 < patches:
            entry_patch = lax.dynamic_slice_in_dim(
                entering_ext, starts[turn_number + 1], biggest_patch_span, 0
            )
            entry_patch = jnp.where(
                (row_numbers < patch_sizes_list[turn_number + 1])[:, None], entry_patch, 0
            )
            arrived = to_next_section(updated)
            entry_parts = [entry_patch] + across_chips_first_section(entry_patch)
            row_parts = [
                jnp.where(section_zero, entry, passed) for entry, passed in zip(entry_parts, arrived)
            ]
    return jnp.stack(results)[:, None]


def solution(mesh):
    return jax.shard_map(
        shards,
        mesh=mesh,
        in_specs=(
            P("groups", "seq"),
            P("section", "groups", "seq"),
            P("groups"),
            P("section", "seq", "groups", None),
            P("section", "seq", "groups", None),
            P("section", None, "seq"),
            P("section", None, "seq"),
            P("section", None, None),
            P("section", "seq"),
        ),
        out_specs=P(None, "section", "groups", "seq"),
        check_vma=False,
    )
```

```python
import jax
import jax.numpy as jnp
from jax import lax
from jax.experimental import pallas as pl
from jax.experimental.pallas import tpu as pltpu
from jax.sharding import PartitionSpec as P

epsilon = 1e-06


def rms_norm(values):
    return values * lax.rsqrt(jnp.mean(values * values, axis=-1, keepdims=True) + epsilon)


def pick_entry(vector, position):
    return jnp.sum(jnp.where(jnp.arange(vector.shape[0]) == position, vector, 0))


def across_chips(block):
    count = lax.axis_size("seq")
    return [
        lax.ppermute(block, "seq", [(source, (source + step) % count) for source in range(count)])
        for step in range(2, count, 2)
    ]


def across_chips_first_section(block):
    count = lax.axis_size("seq")
    return [
        lax.ppermute(
            block, ("section", "seq"), [(source, (source + step) % count) for source in range(count)]
        )
        for step in range(2, count, 2)
    ]


def with_partner(parts):
    count = lax.axis_size("seq")
    to_partner = [(source, source ^ 1) for source in range(count)]
    return parts + [lax.ppermute(part, "seq", to_partner) for part in parts]


def to_next_section(block):
    sections = lax.axis_size("section")
    count = lax.axis_size("seq")
    return [
        lax.ppermute(
            block,
            ("section", "seq"),
            [
                (section * count + source, (section + 1) * count + (source + step) % count)
                for section in range(sections - 1)
                for source in range(count)
            ],
        )
        for step in range(0, count, 2)
    ]


def kernel_tables(patch_sizes_list, section_index):
    patches = patch_sizes_list.shape[0]
    count = lax.axis_size("seq")
    here = lax.axis_index("seq")
    chips = count // 2
    turn = lax.broadcasted_iota(jnp.int32, (patches, count + 2), 0)
    entry = lax.broadcasted_iota(jnp.int32, (patches, count + 2), 1) - 2
    patch_index = jnp.remainder(turn - section_index + patches, patches)
    patch_ids = jnp.arange(patches).reshape(1, 1, patches)
    sizes = patch_sizes_list.reshape(1, 1, patches)
    chosen = patch_ids == patch_index[:, :, None]
    patch_count = jnp.sum(jnp.where(chosen, sizes, 0), axis=-1)
    patch_start = jnp.sum(jnp.where(patch_ids < patch_index[:, :, None], sizes, 0), axis=-1)
    base = jnp.where(entry < chips, here, jnp.bitwise_xor(here, 1))
    sources = jnp.remainder(base - 2 * jnp.remainder(entry, chips) + count, count)
    return jnp.where(entry == -2, patch_start, jnp.where(entry == -1, patch_count, sources)).astype(
        jnp.int32
    )


def block_kernel(*refs):
    where_ref = refs[0]
    count = len(refs) - 10
    part_refs = refs[1 : 1 + count]
    scale_ref, weights_ref, keys_ref, values_ref = refs[1 + count : 5 + count]
    heads_ref, keys_out, values_out = refs[5 + count : 8 + count]
    shaped_ref, staging_ref = refs[8 + count :]
    start = where_ref[0]
    patch_count = where_ref[1]
    head_dim = keys_ref.shape[2]
    seq_len = keys_ref.shape[1]
    span, width = part_refs[0].shape
    features = width * count

    @pl.when(pl.program_id(0) == 0)
    def _():
        parts = [part[...].astype(jnp.float32) for part in part_refs]
        row_mean = sum(jnp.sum(part, axis=-1, keepdims=True) for part in parts) / features
        centred = [part - row_mean for part in parts]
        spread = sum(jnp.sum(c * c, axis=-1, keepdims=True) for c in centred) / features
        inverse = lax.rsqrt(spread + epsilon)
        for part in range(count):
            slot = where_ref[2 + part]
            shift_scale = scale_ref[slot]
            shaped_ref[slot] = (
                (centred[part] * inverse) * (1.0 + shift_scale[1:2]) + shift_scale[0:1]
            ).astype(jnp.bfloat16)

    mixed = sum(
        jnp.dot(
            shaped_ref[slot],
            weights_ref[slot * width : (slot + 1) * width, :],
            preferred_element_type=jnp.float32,
        )
        for slot in range(count)
    )
    queries = rms_norm(mixed[:, :head_dim]).astype(jnp.bfloat16)
    fresh_keys = rms_norm(mixed[:, head_dim : 2 * head_dim]).astype(jnp.bfloat16)
    fresh_values = mixed[:, 2 * head_dim :].astype(jnp.bfloat16)
    live = lax.broadcasted_iota(jnp.int32, (span, 1), 0) < patch_count
    staging_ref[:seq_len] = keys_ref[0].astype(jnp.float32)
    window = staging_ref[pl.ds(start, span)]
    staging_ref[pl.ds(start, span)] = jnp.where(live, fresh_keys.astype(jnp.float32), window)
    keys = staging_ref[:seq_len].astype(jnp.bfloat16)
    staging_ref[:seq_len] = values_ref[0].astype(jnp.float32)
    window = staging_ref[pl.ds(start, span)]
    staging_ref[pl.ds(start, span)] = jnp.where(live, fresh_values.astype(jnp.float32), window)
    values = staging_ref[:seq_len].astype(jnp.bfloat16)
    keys_out[0] = keys
    values_out[0] = values
    scores = lax.dot_general(
        queries, keys, (((1,), (1,)), ((), ())), preferred_element_type=jnp.float32
    ) * head_dim ** (-0.5)
    expos = jnp.exp(scores)
    weights = (expos / jnp.sum(expos, axis=-1, keepdims=True)).astype(jnp.bfloat16)
    heads_ref[...] = jnp.dot(weights, values, preferred_element_type=jnp.float32).astype(
        jnp.bfloat16
    )


def attend_block(parts, shift_scale, qkv_weights, key_cache, value_cache, where, in_place):
    count = len(parts)
    span, width = parts[0].shape
    heads_here, seq_len, head_dim = key_cache.shape
    features = qkv_weights.shape[0]
    scale_blocks = jnp.transpose(shift_scale.reshape(2, count, width), (1, 0, 2))
    whole = lambda shape: pl.BlockSpec(shape, lambda h, where: (0,) * len(shape))
    cache_spec = pl.BlockSpec((1, seq_len, head_dim), lambda h, where: (h, 0, 0))
    grid_spec = pltpu.PrefetchScalarGridSpec(
        num_scalar_prefetch=1,
        grid=(heads_here,),
        in_specs=[whole((span, width)) for _ in parts]
        + [
            whole((count, 2, width)),
            pl.BlockSpec((features, 3 * head_dim), lambda h, where: (0, h)),
            cache_spec,
            cache_spec,
        ],
        out_specs=[
            pl.BlockSpec((span, head_dim), lambda h, where: (0, h)),
            cache_spec,
            cache_spec,
        ],
        scratch_shapes=[
            pltpu.VMEM((count, span, width), jnp.bfloat16),
            pltpu.VMEM((seq_len + span, head_dim), jnp.float32),
        ],
    )
    return pl.pallas_call(
        block_kernel,
        grid_spec=grid_spec,
        out_shape=[
            jax.ShapeDtypeStruct((span, heads_here * head_dim), jnp.bfloat16),
            jax.ShapeDtypeStruct(key_cache.shape, key_cache.dtype),
            jax.ShapeDtypeStruct(value_cache.shape, value_cache.dtype),
        ],
        input_output_aliases={count + 3: 1, count + 4: 2} if in_place else {},
        compiler_params=pltpu.CompilerParams(dimension_semantics=("arbitrary",)),
    )(where, *parts, scale_blocks, qkv_weights, key_cache, value_cache)


def exit_kernel(*refs):
    where_ref = refs[0]
    count = len(refs) - 5
    part_refs = refs[1 : 1 + count]
    weights_ref, own_ref, gate_ref = refs[1 + count : 4 + count]
    out_ref = refs[4 + count]
    patch_count = where_ref[1]
    projected = sum(
        jnp.dot(
            part_refs[part][...],
            weights_ref[where_ref[2 + part]],
            preferred_element_type=jnp.float32,
        )
        for part in range(count)
    )
    updated = own_ref[...].astype(jnp.float32) + gate_ref[...] * projected
    live = lax.broadcasted_iota(jnp.int32, updated.shape, 0) < patch_count
    out_ref[...] = jnp.where(live, updated, 0.0).astype(out_ref.dtype)


def leave_block(parts, out_weights, own_rows, gating_here, where):
    count = len(parts)
    span, head_width = parts[0].shape
    width = out_weights.shape[1]
    half = width // 2 if width % 256 == 0 else width
    whole = lambda shape: pl.BlockSpec(shape, lambda j, where: (0,) * len(shape))
    grid_spec = pltpu.PrefetchScalarGridSpec(
        num_scalar_prefetch=1,
        grid=(width // half,),
        in_specs=[whole((span, head_width)) for _ in parts]
        + [
            pl.BlockSpec((count, head_width, half), lambda j, where: (0, 0, j)),
            pl.BlockSpec((span, half), lambda j, where: (0, j)),
            pl.BlockSpec((1, half), lambda j, where: (0, j)),
        ],
        out_specs=pl.BlockSpec((span, half), lambda j, where: (0, j)),
    )
    return pl.pallas_call(
        exit_kernel,
        grid_spec=grid_spec,
        out_shape=jax.ShapeDtypeStruct(own_rows.shape, own_rows.dtype),
        compiler_params=pltpu.CompilerParams(dimension_semantics=("arbitrary",)),
    )(
        where,
        *parts,
        out_weights.reshape(count, head_width, width),
        own_rows,
        gating_here.reshape(1, -1),
    )


def shards(
    incoming_states,
    transit_states,
    patch_sizes_list,
    outdated_lookups,
    outdated_contents,
    attention_projection,
    exit_projection,
    shift_and_scale,
    branch_gates,
):
    section_index = lax.axis_index("section")
    patches = patch_sizes_list.shape[0]
    biggest_patch_span = transit_states.shape[1]
    columns = incoming_states.shape[1]
    starts = jnp.cumsum(patch_sizes_list) - patch_sizes_list
    key_cache = outdated_lookups[0]
    value_cache = outdated_contents[0]
    qkv_weights = attention_projection[0]
    out_weights = exit_projection[0]
    shift_scale = shift_and_scale[0]
    gating_here = branch_gates[0]
    row_numbers = jnp.arange(biggest_patch_span)

    results = []
    entering_ext = jnp.concatenate(
        [incoming_states, jnp.zeros((biggest_patch_span, columns), jnp.bfloat16)], axis=0
    )
    section_zero = section_index == 0
    own_rows = jnp.where(section_zero, entering_ext[:biggest_patch_span], transit_states[0])
    own_rows = jnp.where(
        (row_numbers < pick_entry(patch_sizes_list, jnp.remainder(-section_index, patches)))[:, None],
        own_rows,
        0,
    )
    row_parts = [own_rows] + across_chips(own_rows)
    tables, row_parts = lax.optimization_barrier(
        (kernel_tables(patch_sizes_list, section_index), row_parts)
    )
    for turn_number in range(patches):
        where = tables[turn_number]
        head_rows, key_cache, value_cache = attend_block(
            with_partner(row_parts),
            shift_scale,
            qkv_weights,
            key_cache,
            value_cache,
            where,
            turn_number > 0,
        )
        updated = leave_block(
            with_partner([head_rows] + across_chips(head_rows)),
            out_weights,
            row_parts[0],
            gating_here,
            where,
        )
        results.append(updated)
        if turn_number + 1 < patches:
            entry_patch = lax.dynamic_slice_in_dim(
                entering_ext, starts[turn_number + 1], biggest_patch_span, 0
            )
            entry_patch = jnp.where(
                (row_numbers < patch_sizes_list[turn_number + 1])[:, None], entry_patch, 0
            )
            arrived = to_next_section(updated)
            entry_parts = [entry_patch] + across_chips_first_section(entry_patch)
            row_parts = [
                jnp.where(section_zero, entry, passed) for entry, passed in zip(entry_parts, arrived)
            ]
    return jnp.stack(results)[:, None]


def solution(mesh):
    return jax.shard_map(
        shards,
        mesh=mesh,
        in_specs=(
            P("groups", "seq"),
            P("section", "groups", "seq"),
            P("groups"),
            P("section", "seq", "groups", None),
            P("section", "seq", "groups", None),
            P("section", None, "seq"),
            P("section", None, "seq"),
            P("section", None, None),
            P("section", "seq"),
        ),
        out_specs=P(None, "section", "groups", "seq"),
        check_vma=False,
    )
```
